512 devices in a mesh: dp: 32 (over x_lo, z), ctx: 16 (over y, x_hi, core).
Axes of the slice: x: 4 (x_hi: 2, x_lo: 2; x = x_hi * 2 + x_lo), y: 4, z: 16, core: 2. Of those that a mesh axis runs over, the one named last changes fastest.
Arguments:
- queries: bfloat16 [32, 2048, 2048], P('dp', 'ctx'), may hold values from -6 to 6
- key_state_matrix: bfloat16 [32, 2048, 2048], P('dp', 'ctx'), may hold values from -6 to 6
- value_state_matrix: bfloat16 [32, 2048, 2048], P('dp', 'ctx'), may hold values from -6 to 6
- cotangent: bfloat16 [32, 2048, 2048], P('dp', 'ctx'), may hold values from -6 to 6
- sublayer_norm_gain: float32 [2048], replicated, may hold values from 0.5 to 1.5
- sublayer_norm_bias: float32 [2048], replicated, may hold values from -3 to 3
- segment_blocks: int32 [4], replicated, may hold values from 1 to 16, as said below
- dilation_rates: int32 [4], replicated, may hold values from 1 to 16, as said below
Outputs:
- normed: bfloat16 [32, 2048, 2048], P('dp', 'ctx')
- grad_queries: bfloat16 [32, 2048, 2048], P('dp', 'ctx')
- grad_keys: bfloat16 [32, 2048, 2048], P('dp', 'ctx')
- grad_values: bfloat16 [32, 2048, 2048], P('dp', 'ctx')
- grad_gain: float32 [2048], P('ctx')
- grad_bias: float32 [2048], P('ctx')
The draws below stay inside these ranges and needn't reach their ends.
Inputs may be any that keep to these rules, and one draw needn't show every extreme that they name: segment_blocks[0] is 1; the other entries are powers of two from 2 to 16, and at least one of them equals 16. dilation_rates[0] is 1; entries 1 to 3 are 2, 16 and one of 4 or 8, in some order.
All inputs are finite; a program needn't handle non-finite values.
Results may differ from the reference program's by a relative error of at most 0.011.
Values may be sent and summed in bfloat16 or wider, within the bound.
No kernel may reach another device: no remote copies, remote signals or barrier semaphores. Data moves between devices by JAX's collectives and lax.ppermute only.
A program may use at most 64 MiB of HBM per device.

```python
import math
import jax
import jax.numpy as jnp
from jax import lax

D = 2048
H = 16
DH = 128
BLK = 128
G = 4
SLIDES = 32
SEQ = 2048


def drawn_pair(key):
    base = jax.random.fold_in(key, 11)
    shape = (SLIDES, SEQ, D)
    first_branch = jax.random.normal(jax.random.fold_in(base, 1), shape)
    second = jax.random.normal(jax.random.fold_in(base, 2), shape)
    return (jnp.clip(first_branch, -6.0, 6.0), jnp.clip(second, -6.0, 6.0))


def draw_queries(key, part):
    return drawn_pair(key)[0].astype(jnp.bfloat16)


def draw_key_state_matrix(key, part):
    return drawn_pair(key)[1].astype(jnp.bfloat16)


def draw_value_state_matrix(key, part):
    base = jax.random.fold_in(key, 23)
    shape = (SLIDES, SEQ, D)
    column = (jnp.arange(D, dtype=jnp.int32) // DH).astype(jnp.float32)
    rise = 0.5 + column / (H - 1)
    values = jax.random.normal(jax.random.fold_in(base, 1), shape) * rise
    return jnp.clip(values, -6.0, 6.0).astype(jnp.bfloat16)


def draw_cotangent(key, part):
    base = jax.random.fold_in(key, 29)
    shape = (SLIDES, SEQ, D)
    place = jnp.arange(SEQ, dtype=jnp.int32)[None, :, None]
    slide_ids = jnp.arange(SLIDES, dtype=jnp.int32)[:, None, None]
    order = (slide_ids * SEQ + place).astype(jnp.float32)
    rise = 0.5 + order / (SLIDES * SEQ - 1)
    values = jax.random.normal(jax.random.fold_in(base, 1), shape) * rise
    return jnp.clip(values, -6.0, 6.0).astype(jnp.bfloat16)


def branch_places(key):
    return jax.random.permutation(jax.random.fold_in(key, 41), jnp.arange(1, 4, dtype=jnp.int32))


def draw_segment_blocks(key, part):
    last_len = SEQ // BLK
    top_power = last_len.bit_length() - 1
    full_place = jax.random.randint(jax.random.fold_in(key, 53), (), 1, 4)
    powers = jax.random.randint(jax.random.fold_in(key, 31), (4,), 1, top_power)
    lengths = jnp.power(2, powers).astype(jnp.int32)
    slots = jnp.arange(4, dtype=jnp.int32)
    result = jnp.where(slots == full_place, last_len, lengths)
    return jnp.where(slots == 0, 1, result).astype(jnp.int32)


def draw_dilation_rates(key, part):
    places = branch_places(key)
    power = jax.random.randint(jax.random.fold_in(key, 37), (), 2, 4)
    middle = jnp.power(2, power).astype(jnp.int32)
    rates = jnp.stack([jnp.full((), 2, jnp.int32), middle, jnp.full((), 16, jnp.int32)])
    result = jnp.ones((4,), jnp.int32)
    return result.at[places].set(rates)


def centred(stream_key, shape, scale, limit, kind=jnp.bfloat16):
    return jnp.clip(scale * jax.random.normal(stream_key, shape, jnp.float32), -limit, limit).astype(kind)


def setup_inputs(seed: int = 0) -> dict:
    arg_keys = jax.random.split(jax.random.key(seed), 9)
    queries = draw_queries(jax.random.fold_in(arg_keys[8], 71), 0)
    key_state_matrix = draw_key_state_matrix(jax.random.fold_in(arg_keys[8], 71), 0)
    value_state_matrix = draw_value_state_matrix(jax.random.fold_in(arg_keys[8], 71), 0)
    cotangent = draw_cotangent(jax.random.fold_in(arg_keys[8], 71), 0)
    sublayer_norm_gain = jnp.clip(1.0 + 0.1 * jax.random.normal(arg_keys[4], (D,), jnp.float32), 0.5, 1.5)
    sublayer_norm_bias = centred(arg_keys[5], (D,), 0.5, 3.0, jnp.float32)
    segment_blocks = draw_segment_blocks(jax.random.fold_in(arg_keys[8], 71), 0)
    dilation_rates = draw_dilation_rates(jax.random.fold_in(arg_keys[8], 71), 0)
    return {"queries": queries, "key_state_matrix": key_state_matrix, "value_state_matrix": value_state_matrix, "cotangent": cotangent, "sublayer_norm_gain": sublayer_norm_gain, "sublayer_norm_bias": sublayer_norm_bias, "segment_blocks": segment_blocks, "dilation_rates": dilation_rates}


def branch_mask_list(token_positions, head_number, segment_blocks, dilation_rates):
    first_branch = jnp.zeros((token_positions.shape[0], token_positions.shape[0]), jnp.float32)
    remaining_branches = jnp.zeros((token_positions.shape[0], token_positions.shape[0]), jnp.float32)
    for dilation_branch in range(G):
        seg_width = segment_blocks[dilation_branch] * BLK
        dilation_rate = dilation_rates[dilation_branch]
        same_seg = token_positions[:, None] // seg_width == token_positions[None, :] // seg_width
        selected_rows = token_positions % dilation_rate == head_number % dilation_rate
        term = (same_seg & selected_rows[:, None] & selected_rows[None, :]).astype(jnp.float32)
        if dilation_branch == 0:
            first_branch = first_branch + term
        else:
            remaining_branches = remaining_branches + term
    return (first_branch, remaining_branches)

def two_parts(first_branch, second):
    first_branch = lax.optimization_barrier(first_branch)
    second = lax.optimization_barrier(second)
    return (first_branch.astype(jnp.float32) + second.astype(jnp.float32)).astype(jnp.bfloat16)

def reference(queries, key_state_matrix, value_state_matrix, cotangent, sublayer_norm_gain, sublayer_norm_bias, segment_blocks, dilation_rates):
    token_positions = jnp.arange(SEQ, dtype=jnp.int32)
    head_list = jnp.arange(H, dtype=jnp.int32)
    scaling = 1.0 / math.sqrt(DH)

    def split_heads(array):
        return array.reshape(SEQ, H, DH).transpose(1, 0, 2)

    def merge_heads(array):
        return array.transpose(1, 0, 2).reshape(SEQ, D)

    def head_probs(head_number, query_h, key_h):
        first_branch, remaining_branches = branch_mask_list(token_positions, head_number, segment_blocks, dilation_rates)
        counted = first_branch + remaining_branches
        scores = jnp.dot(query_h, key_h.T, preferred_element_type=jnp.float32) * scaling
        masked = jnp.where(counted > 0, scores, -1e+30)
        return (first_branch, remaining_branches, counted, masked)

    def slide_pass(inputs):
        slide_q, slide_k, slide_v, slide_cot = inputs
        heads_q = split_heads(slide_q)
        heads_k = split_heads(slide_k)
        heads_v = split_heads(slide_v)

        def forward_head(items):
            head_number, query_h, key_h, value_h = items
            first_branch, remaining_branches, counted, masked = head_probs(head_number, query_h, key_h)
            row_max = lax.optimization_barrier(jnp.max(masked, axis=1))
            log_norm = row_max + jnp.log(lax.optimization_barrier(jnp.sum(counted * jnp.exp(masked - row_max[:, None]), axis=1)))
            expo = jnp.exp(masked - log_norm[:, None])
            prob_first = (first_branch * expo).astype(jnp.bfloat16)
            prob_rest = (remaining_branches * expo).astype(jnp.bfloat16)
            out_first = jnp.dot(prob_first, value_h, preferred_element_type=jnp.float32).astype(jnp.bfloat16)
            out_rest = jnp.dot(prob_rest, value_h, preferred_element_type=jnp.float32).astype(jnp.bfloat16)
            return (two_parts(out_first, out_rest), log_norm)
        heads_out, heads_lse = lax.map(forward_head, (head_list, heads_q, heads_k, heads_v))
        values = merge_heads(heads_out).astype(jnp.float32)
        mean_row = lax.optimization_barrier(jnp.mean(values, axis=1, keepdims=True))
        var_row = lax.optimization_barrier(jnp.mean(values * values, axis=1, keepdims=True)) - mean_row * mean_row
        inv_std = lax.rsqrt(var_row + 1e-05)
        centered = (values - mean_row) * inv_std
        normed = (centered * sublayer_norm_gain + sublayer_norm_bias).astype(jnp.bfloat16)
        grad_y = slide_cot.astype(jnp.float32)
        scaled = grad_y * sublayer_norm_gain
        grad_attn = (inv_std * (scaled - lax.optimization_barrier(jnp.mean(scaled, axis=1, keepdims=True)) - centered * lax.optimization_barrier(jnp.mean(scaled * centered, axis=1, keepdims=True)))).astype(jnp.bfloat16)
        gain_part = lax.optimization_barrier(jnp.sum(grad_y * centered, axis=0))
        bias_part = lax.optimization_barrier(jnp.sum(grad_y, axis=0))
        heads_grad = split_heads(grad_attn)

        def backward_head(items):
            head_number, query_h, key_h, value_h, out_h, grad_h, lse_h = items
            first_branch, remaining_branches, counted, masked = head_probs(head_number, query_h, key_h)
            expo = jnp.exp(masked - lse_h[:, None])
            grad_prob = jnp.dot(grad_h, value_h.T, preferred_element_type=jnp.float32)
            delta_row = lax.optimization_barrier(jnp.sum(grad_h.astype(jnp.float32) * out_h.astype(jnp.float32), axis=1))
            common = expo * (grad_prob - delta_row[:, None])
            results = []
            for mult in (first_branch, remaining_branches):
                grad_score = (mult * common).astype(jnp.bfloat16)
                prob_bf = (mult * expo).astype(jnp.bfloat16)
                grad_q = (jnp.dot(grad_score, key_h, preferred_element_type=jnp.float32) * scaling).astype(jnp.bfloat16)
                grad_k = (jnp.dot(grad_score.T, query_h, preferred_element_type=jnp.float32) * scaling).astype(jnp.bfloat16)
                grad_v = jnp.dot(prob_bf.T, grad_h, preferred_element_type=jnp.float32).astype(jnp.bfloat16)
                results.append((grad_q, grad_k, grad_v))
            return (two_parts(results[0][0], results[1][0]), two_parts(results[0][1], results[1][1]), two_parts(results[0][2], results[1][2]))
        grads = lax.map(backward_head, (head_list, heads_q, heads_k, heads_v, heads_out, heads_grad, heads_lse))
        return (normed, merge_heads(grads[0]), merge_heads(grads[1]), merge_heads(grads[2]), gain_part, bias_part)
    normed, grad_queries, grad_keys, grad_values, gain_parts, bias_parts = lax.map(slide_pass, (queries, key_state_matrix, value_state_matrix, cotangent))
    loss_scale = 1.0 / math.sqrt(SLIDES * SEQ)
    grad_gain = lax.optimization_barrier(jnp.sum(gain_parts, axis=0)) * loss_scale
    grad_bias = lax.optimization_barrier(jnp.sum(bias_parts, axis=0)) * loss_scale
    return (normed, grad_queries, grad_keys, grad_values, grad_gain, grad_bias)
```

```python
import math

import jax
import jax.numpy as jnp
from jax import lax
from jax.sharding import PartitionSpec as P

H = 16
BLK = 128
G = 4


epsilon = 1e-05


def pick_rows(array, parity):
    pairs = array.reshape((array.shape[0] // 2, 2) + array.shape[1:])
    cond = (parity == 0).reshape((-1,) + (1,) * (array.ndim - 2))
    return jnp.where(cond, pairs[:, 0], pairs[:, 1])


def spread_rows(packed, parity, base):
    pairs = base.reshape((base.shape[0] // 2, 2) + base.shape[1:])
    cond = (parity == 0).reshape((-1,) + (1,) * (base.ndim - 2))
    first_branch = jnp.where(cond, packed, pairs[:, 0])
    second = jnp.where(cond, pairs[:, 1], packed)
    return jnp.stack([first_branch, second], axis=1).reshape(base.shape)


def add_parts(full_part, packed_part, parity):
    spread = spread_rows(packed_part, parity, jnp.zeros_like(full_part))
    full_part = lax.optimization_barrier(full_part)
    spread = lax.optimization_barrier(spread)
    return (full_part.astype(jnp.float32) + spread.astype(jnp.float32)).astype(jnp.bfloat16)


def block_view(array):
    return array.reshape((array.shape[0] // BLK, BLK) + array.shape[1:])


def lse_view(log_norm):
    return jnp.transpose(block_view(log_norm), (0, 2, 1))


def local_scores(query_row_set, key_row_set):
    scaling = 1.0 / math.sqrt(query_row_set.shape[-1])
    return (
        jnp.einsum(
            "bqhd,bkhd->bhqk",
            block_view(query_row_set),
            block_view(key_row_set),
            preferred_element_type=jnp.float32,
        )
        * scaling
    )


def local_lse(query_row_set, key_row_set):
    scores = local_scores(query_row_set, key_row_set)
    row_max = jnp.max(scores, axis=3)
    total = row_max + jnp.log(jnp.sum(jnp.exp(scores - row_max[..., None]), axis=3))
    return jnp.transpose(total, (0, 2, 1)).reshape(query_row_set.shape[0], query_row_set.shape[1])


def local_output(query_row_set, key_row_set, value_row_set, log_norm):
    scores = local_scores(query_row_set, key_row_set)
    prob_bf = jnp.exp(scores - lse_view(log_norm)[..., None]).astype(jnp.bfloat16)
    output = jnp.einsum(
        "bhqk,bkhd->bqhd", prob_bf, block_view(value_row_set), preferred_element_type=jnp.float32
    )
    return output.astype(jnp.bfloat16).reshape(query_row_set.shape)


def local_backward(query_row_set, key_row_set, value_row_set, grad_rows, log_norm, delta_row):
    scaling = 1.0 / math.sqrt(query_row_set.shape[-1])
    scores = local_scores(query_row_set, key_row_set)
    prob_full = jnp.exp(scores - lse_view(log_norm)[..., None])
    prob_bf = prob_full.astype(jnp.bfloat16)
    grad_prob = jnp.einsum(
        "bqhd,bkhd->bhqk",
        block_view(grad_rows),
        block_view(value_row_set),
        preferred_element_type=jnp.float32,
    )
    grad_score = (prob_full * (grad_prob - lse_view(delta_row)[..., None])).astype(jnp.bfloat16)
    grad_q = jnp.einsum(
        "bhqk,bkhd->bqhd", grad_score, block_view(key_row_set), preferred_element_type=jnp.float32
    )
    grad_k = jnp.einsum(
        "bhqk,bqhd->bkhd", grad_score, block_view(query_row_set), preferred_element_type=jnp.float32
    )
    grad_v = jnp.einsum(
        "bhqk,bqhd->bkhd", prob_bf, block_view(grad_rows), preferred_element_type=jnp.float32
    )
    shape = query_row_set.shape
    return (
        (grad_q * scaling).astype(jnp.bfloat16).reshape(shape),
        (grad_k * scaling).astype(jnp.bfloat16).reshape(shape),
        grad_v.astype(jnp.bfloat16).reshape(shape),
    )


def packed_positions(start, count, head_indices):
    rows = start + jnp.arange(count, dtype=jnp.int32)
    return 2 * rows[None, :] + (head_indices % 2)[:, None]


def dilation_multiplier(
    query_positions, key_positions, head_indices, segment_blocks, dilation_rates
):
    counted = jnp.zeros(
        (head_indices.shape[0], query_positions.shape[1], key_positions.shape[1]), jnp.float32
    )
    for dilation_branch in range(1, G):
        seg_width = segment_blocks[dilation_branch] * BLK
        dilation_rate = dilation_rates[dilation_branch]
        same_seg = (
            query_positions[:, :, None] // seg_width == key_positions[:, None, :] // seg_width
        )
        selected_queries = query_positions % dilation_rate == head_indices[:, None] % dilation_rate
        selected_keys = key_positions % dilation_rate == head_indices[:, None] % dilation_rate
        counted = counted + (
            same_seg & selected_queries[:, :, None] & selected_keys[:, None, :]
        ).astype(jnp.float32)
    return counted


def sparse_attention_forward(
    query_row_set,
    key_row_set,
    value_row_set,
    baseline_logsumexp,
    head_indices,
    segment_blocks,
    dilation_rates,
):
    length_all, heads_here, head_size = query_row_set.shape
    rows_per_block = min(512, length_all)
    blocks = length_all // rows_per_block
    scaling = 1.0 / math.sqrt(head_size)
    key_positions = packed_positions(0, length_all, head_indices)

    def one_block(block_id):
        starting_row = block_id * rows_per_block
        q_block = lax.dynamic_slice_in_dim(query_row_set, starting_row, rows_per_block, 0)
        own_lse = lax.dynamic_slice_in_dim(baseline_logsumexp, starting_row, rows_per_block, 0).T
        counted = dilation_multiplier(
            packed_positions(starting_row, rows_per_block, head_indices),
            key_positions,
            head_indices,
            segment_blocks,
            dilation_rates,
        )
        scores = (
            jnp.einsum("qhd,khd->hqk", q_block, key_row_set, preferred_element_type=jnp.float32)
            * scaling
        )
        masked = jnp.where(counted > 0, scores, -1e30)
        row_max = jnp.max(masked, axis=2)
        part_lse = row_max + jnp.log(
            jnp.sum(counted * jnp.exp(masked - row_max[:, :, None]), axis=2)
        )
        top = jnp.maximum(part_lse, own_lse)
        log_norm = top + jnp.log(jnp.exp(part_lse - top) + jnp.exp(own_lse - top))
        prob_bf = (counted * jnp.exp(masked - log_norm[:, :, None])).astype(jnp.bfloat16)
        output = jnp.einsum(
            "hqk,khd->qhd", prob_bf, value_row_set, preferred_element_type=jnp.float32
        ).astype(jnp.bfloat16)
        return (output, log_norm)

    outputs, lse_blocks = lax.map(one_block, jnp.arange(blocks, dtype=jnp.int32))
    return (
        outputs.reshape(length_all, heads_here, head_size),
        jnp.transpose(lse_blocks, (0, 2, 1)).reshape(length_all, heads_here),
    )


def dilated_backward(
    query_row_set,
    key_row_set,
    value_row_set,
    grad_rows,
    log_norm,
    delta_row,
    head_indices,
    segment_blocks,
    dilation_rates,
):
    length_all, heads_here, head_size = query_row_set.shape
    rows_per_block = min(512, length_all)
    blocks = length_all // rows_per_block
    scaling = 1.0 / math.sqrt(head_size)
    key_positions = packed_positions(0, length_all, head_indices)

    def step(carry, block_id):
        acc_k, acc_v = carry
        starting_row = block_id * rows_per_block
        q_block = lax.dynamic_slice_in_dim(query_row_set, starting_row, rows_per_block, 0)
        g_block = lax.dynamic_slice_in_dim(grad_rows, starting_row, rows_per_block, 0)
        lse_block = lax.dynamic_slice_in_dim(log_norm, starting_row, rows_per_block, 0).T
        delta_block = lax.dynamic_slice_in_dim(delta_row, starting_row, rows_per_block, 0).T
        counted = dilation_multiplier(
            packed_positions(starting_row, rows_per_block, head_indices),
            key_positions,
            head_indices,
            segment_blocks,
            dilation_rates,
        )
        scores = (
            jnp.einsum("qhd,khd->hqk", q_block, key_row_set, preferred_element_type=jnp.float32)
            * scaling
        )
        masked = jnp.where(counted > 0, scores, -1e30)
        prob_full = counted * jnp.exp(masked - lse_block[:, :, None])
        prob_bf = prob_full.astype(jnp.bfloat16)
        grad_prob = jnp.einsum(
            "qhd,khd->hqk", g_block, value_row_set, preferred_element_type=jnp.float32
        )
        grad_score = (prob_full * (grad_prob - delta_block[:, :, None])).astype(jnp.bfloat16)
        grad_q = (
            jnp.einsum("hqk,khd->qhd", grad_score, key_row_set, preferred_element_type=jnp.float32)
            * scaling
        ).astype(jnp.bfloat16)
        acc_k = acc_k + jnp.einsum(
            "hqk,qhd->khd", grad_score, q_block, preferred_element_type=jnp.float32
        )
        acc_v = acc_v + jnp.einsum(
            "hqk,qhd->khd", prob_bf, g_block, preferred_element_type=jnp.float32
        )
        return ((acc_k, acc_v), grad_q)

    zeros_all = jnp.zeros((length_all, heads_here, head_size), jnp.float32)
    (acc_k, acc_v), grad_q = lax.scan(
        step, (zeros_all, zeros_all), jnp.arange(blocks, dtype=jnp.int32)
    )
    return (
        grad_q.reshape(length_all, heads_here, head_size),
        (acc_k * scaling).astype(jnp.bfloat16),
        acc_v.astype(jnp.bfloat16),
    )


def dense_attention_forward(
    query_row_set, key_row_set, value_row_set, head_indices, segment_blocks, dilation_rates
):
    parity = head_indices % 2
    own_lse = local_lse(query_row_set, key_row_set)
    packed_out, packed_lse = sparse_attention_forward(
        pick_rows(query_row_set, parity),
        pick_rows(key_row_set, parity),
        pick_rows(value_row_set, parity),
        pick_rows(own_lse, parity),
        head_indices,
        segment_blocks,
        dilation_rates,
    )
    log_norm = spread_rows(packed_lse, parity, own_lse)
    attended = add_parts(
        local_output(query_row_set, key_row_set, value_row_set, log_norm), packed_out, parity
    )
    return (attended, log_norm)


def full_backward(
    query_row_set,
    key_row_set,
    value_row_set,
    attended,
    grad_attended,
    log_norm,
    head_indices,
    segment_blocks,
    dilation_rates,
):
    parity = head_indices % 2
    delta_row = jnp.sum(grad_attended.astype(jnp.float32) * attended.astype(jnp.float32), axis=2)
    local_parts = local_backward(
        query_row_set, key_row_set, value_row_set, grad_attended, log_norm, delta_row
    )
    packed_parts = dilated_backward(
        pick_rows(query_row_set, parity),
        pick_rows(key_row_set, parity),
        pick_rows(value_row_set, parity),
        pick_rows(grad_attended, parity),
        pick_rows(log_norm, parity),
        pick_rows(delta_row, parity),
        head_indices,
        segment_blocks,
        dilation_rates,
    )
    return tuple(
        (
            add_parts(first_branch, second, parity)
            for first_branch, second in zip(local_parts, packed_parts)
        )
    )


def butterfly_sum(value, axis_name):
    count = lax.axis_size(axis_name)
    step = 1
    while step < count:
        pairs = [(i, i ^ step) for i in range(count)]
        value = value + lax.ppermute(value, axis_name, pairs)
        step *= 2
    return value


def token_norm(values, cot_rows, sublayer_norm_gain, sublayer_norm_bias):
    mean_row = jnp.mean(values, axis=1, keepdims=True)
    var_row = jnp.mean(values * values, axis=1, keepdims=True) - mean_row * mean_row
    inv_std = lax.rsqrt(var_row + epsilon)
    centered = (values - mean_row) * inv_std
    normed = (centered * sublayer_norm_gain + sublayer_norm_bias).astype(jnp.bfloat16)
    grad_y = cot_rows.astype(jnp.float32)
    scaled = grad_y * sublayer_norm_gain
    grad_tokens = (
        inv_std
        * (
            scaled
            - jnp.mean(scaled, axis=1, keepdims=True)
            - centered * jnp.mean(scaled * centered, axis=1, keepdims=True)
        )
    ).astype(jnp.bfloat16)
    return (normed, grad_tokens, jnp.sum(grad_y * centered, axis=0), jnp.sum(grad_y, axis=0))


def shards(
    queries,
    key_state_matrix,
    value_state_matrix,
    cotangent,
    sublayer_norm_gain,
    sublayer_norm_bias,
    segment_blocks,
    dilation_rates,
):
    tokens_here = queries.shape[1]
    width_all = queries.shape[2]
    head_size = width_all // H
    ctx_count = lax.axis_size("ctx")
    heads_here = H // ctx_count
    head_first = lax.axis_index("ctx") * heads_here
    head_indices = head_first + jnp.arange(heads_here, dtype=jnp.int32)
    loss_scale = 1.0 / math.sqrt(lax.axis_size("dp") * tokens_here * ctx_count)
    shape_out = (1, tokens_here, width_all)

    def to_heads(array):
        return array.reshape(tokens_here, H, head_size)

    query_head_tensor, key_head_tensor, value_head_tensor = (
        lax.all_to_all(to_heads(queries[0]), "ctx", split_axis=1, concat_axis=0, tiled=True),
        lax.all_to_all(
            to_heads(key_state_matrix[0]), "ctx", split_axis=1, concat_axis=0, tiled=True
        ),
        lax.all_to_all(
            to_heads(value_state_matrix[0]), "ctx", split_axis=1, concat_axis=0, tiled=True
        ),
    )
    attended, log_norm = dense_attention_forward(
        query_head_tensor,
        key_head_tensor,
        value_head_tensor,
        head_indices,
        segment_blocks,
        dilation_rates,
    )
    tokens_view = lax.all_to_all(attended, "ctx", split_axis=0, concat_axis=1, tiled=True).reshape(
        tokens_here, width_all
    )
    normed, grad_tokens, gain_part, bias_part = token_norm(
        tokens_view.astype(jnp.float32), cotangent[0], sublayer_norm_gain, sublayer_norm_bias
    )
    normed = normed.reshape(shape_out)
    grad_attended = lax.all_to_all(
        to_heads(grad_tokens), "ctx", split_axis=1, concat_axis=0, tiled=True
    )
    both = lax.psum_scatter(
        jnp.stack([gain_part, bias_part], axis=1), "ctx", scatter_dimension=0, tiled=True
    )
    both = butterfly_sum(both, "dp")
    grad_gain, grad_bias = both[:, 0], both[:, 1]
    grad_q, grad_k, grad_v = full_backward(
        query_head_tensor,
        key_head_tensor,
        value_head_tensor,
        attended,
        grad_attended,
        log_norm,
        head_indices,
        segment_blocks,
        dilation_rates,
    )
    back_q, back_k, back_v = (
        lax.all_to_all(grad_q, "ctx", split_axis=0, concat_axis=1, tiled=True),
        lax.all_to_all(grad_k, "ctx", split_axis=0, concat_axis=1, tiled=True),
        lax.all_to_all(grad_v, "ctx", split_axis=0, concat_axis=1, tiled=True),
    )
    return (
        normed,
        back_q.reshape(shape_out),
        back_k.reshape(shape_out),
        back_v.reshape(shape_out),
        grad_gain * loss_scale,
        grad_bias * loss_scale,
    )


def solution(mesh):
    return jax.shard_map(
        shards,
        mesh=mesh,
        in_specs=(
            P("dp", "ctx", None),
            P("dp", "ctx", None),
            P("dp", "ctx", None),
            P("dp", "ctx", None),
            P(),
            P(),
            P(),
            P(),
        ),
        out_specs=(
            P("dp", "ctx", None),
            P("dp", "ctx", None),
            P("dp", "ctx", None),
            P("dp", "ctx", None),
            P("ctx"),
            P("ctx"),
        ),
        check_vma=False,
    )
```

```python
import math

import jax
import jax.numpy as jnp
from jax import lax
from jax.sharding import PartitionSpec as P

H = 16
BLK = 128
G = 4


epsilon = 1e-05


def pick_rows(array, parity):
    pairs = array.reshape((array.shape[0] // 2, 2) + array.shape[1:])
    cond = (parity == 0).reshape((-1,) + (1,) * (array.ndim - 2))
    return jnp.where(cond, pairs[:, 0], pairs[:, 1])


def spread_rows(packed, parity, base):
    pairs = base.reshape((base.shape[0] // 2, 2) + base.shape[1:])
    cond = (parity == 0).reshape((-1,) + (1,) * (base.ndim - 2))
    first_branch = jnp.where(cond, packed, pairs[:, 0])
    second = jnp.where(cond, pairs[:, 1], packed)
    return jnp.stack([first_branch, second], axis=1).reshape(base.shape)


def add_parts(full_part, packed_part, parity):
    spread = spread_rows(packed_part, parity, jnp.zeros_like(full_part))
    full_part = lax.optimization_barrier(full_part)
    spread = lax.optimization_barrier(spread)
    return (full_part.astype(jnp.float32) + spread.astype(jnp.float32)).astype(jnp.bfloat16)


def block_view(array):
    return array.reshape((array.shape[0] // BLK, BLK) + array.shape[1:])


def lse_view(log_norm):
    return jnp.transpose(block_view(log_norm), (0, 2, 1))


def local_scores(query_row_set, key_row_set):
    scaling = 1.0 / math.sqrt(query_row_set.shape[-1])
    return (
        jnp.einsum(
            "bqhd,bkhd->bhqk",
            block_view(query_row_set),
            block_view(key_row_set),
            preferred_element_type=jnp.float32,
        )
        * scaling
    )


def local_lse(query_row_set, key_row_set):
    scores = local_scores(query_row_set, key_row_set)
    row_max = jnp.max(scores, axis=3)
    total = row_max + jnp.log(jnp.sum(jnp.exp(scores - row_max[..., None]), axis=3))
    return jnp.transpose(total, (0, 2, 1)).reshape(query_row_set.shape[0], query_row_set.shape[1])


def local_output(query_row_set, key_row_set, value_row_set, log_norm):
    scores = local_scores(query_row_set, key_row_set)
    prob_bf = jnp.exp(scores - lse_view(log_norm)[..., None]).astype(jnp.bfloat16)
    output = jnp.einsum(
        "bhqk,bkhd->bqhd", prob_bf, block_view(value_row_set), preferred_element_type=jnp.float32
    )
    return output.astype(jnp.bfloat16).reshape(query_row_set.shape)


def local_backward(query_row_set, key_row_set, value_row_set, grad_rows, log_norm, delta_row):
    scaling = 1.0 / math.sqrt(query_row_set.shape[-1])
    scores = local_scores(query_row_set, key_row_set)
    prob_full = jnp.exp(scores - lse_view(log_norm)[..., None])
    prob_bf = prob_full.astype(jnp.bfloat16)
    grad_prob = jnp.einsum(
        "bqhd,bkhd->bhqk",
        block_view(grad_rows),
        block_view(value_row_set),
        preferred_element_type=jnp.float32,
    )
    grad_score = (prob_full * (grad_prob - lse_view(delta_row)[..., None])).astype(jnp.bfloat16)
    grad_q = jnp.einsum(
        "bhqk,bkhd->bqhd", grad_score, block_view(key_row_set), preferred_element_type=jnp.float32
    )
    grad_k = jnp.einsum(
        "bhqk,bqhd->bkhd", grad_score, block_view(query_row_set), preferred_element_type=jnp.float32
    )
    grad_v = jnp.einsum(
        "bhqk,bqhd->bkhd", prob_bf, block_view(grad_rows), preferred_element_type=jnp.float32
    )
    shape = query_row_set.shape
    return (
        (grad_q * scaling).astype(jnp.bfloat16).reshape(shape),
        (grad_k * scaling).astype(jnp.bfloat16).reshape(shape),
        grad_v.astype(jnp.bfloat16).reshape(shape),
    )


def packed_positions(start, count, head_indices):
    rows = start + jnp.arange(count, dtype=jnp.int32)
    return 2 * rows[None, :] + (head_indices % 2)[:, None]


def dilation_multiplier(
    query_positions, key_positions, head_indices, segment_blocks, dilation_rates
):
    counted = jnp.zeros(
        (head_indices.shape[0], query_positions.shape[1], key_positions.shape[1]), jnp.float32
    )
    for dilation_branch in range(1, G):
        seg_width = segment_blocks[dilation_branch] * BLK
        dilation_rate = dilation_rates[dilation_branch]
        same_seg = (
            query_positions[:, :, None] // seg_width == key_positions[:, None, :] // seg_width
        )
        selected_queries = query_positions % dilation_rate == head_indices[:, None] % dilation_rate
        selected_keys = key_positions % dilation_rate == head_indices[:, None] % dilation_rate
        counted = counted + (
            same_seg & selected_queries[:, :, None] & selected_keys[:, None, :]
        ).astype(jnp.float32)
    return counted


def sparse_attention_forward(
    query_row_set,
    key_row_set,
    value_row_set,
    baseline_logsumexp,
    head_indices,
    segment_blocks,
    dilation_rates,
):
    length_all, heads_here, head_size = query_row_set.shape
    rows_per_block = min(512, length_all)
    blocks = length_all // rows_per_block
    scaling = 1.0 / math.sqrt(head_size)
    key_positions = packed_positions(0, length_all, head_indices)

    def one_block(block_id):
        starting_row = block_id * rows_per_block
        q_block = lax.dynamic_slice_in_dim(query_row_set, starting_row, rows_per_block, 0)
        own_lse = lax.dynamic_slice_in_dim(baseline_logsumexp, starting_row, rows_per_block, 0).T
        counted = dilation_multiplier(
            packed_positions(starting_row, rows_per_block, head_indices),
            key_positions,
            head_indices,
            segment_blocks,
            dilation_rates,
        )
        scores = (
            jnp.einsum("qhd,khd->hqk", q_block, key_row_set, preferred_element_type=jnp.float32)
            * scaling
        )
        masked = jnp.where(counted > 0, scores, -1e30)
        row_max = jnp.max(masked, axis=2)
        part_lse = row_max + jnp.log(
            jnp.sum(counted * jnp.exp(masked - row_max[:, :, None]), axis=2)
        )
        top = jnp.maximum(part_lse, own_lse)
        log_norm = top + jnp.log(jnp.exp(part_lse - top) + jnp.exp(own_lse - top))
        prob_bf = (counted * jnp.exp(masked - log_norm[:, :, None])).astype(jnp.bfloat16)
        output = jnp.einsum(
            "hqk,khd->qhd", prob_bf, value_row_set, preferred_element_type=jnp.float32
        ).astype(jnp.bfloat16)
        return (output, log_norm)

    outputs, lse_blocks = lax.map(one_block, jnp.arange(blocks, dtype=jnp.int32))
    return (
        outputs.reshape(length_all, heads_here, head_size),
        jnp.transpose(lse_blocks, (0, 2, 1)).reshape(length_all, heads_here),
    )


def dilated_backward(
    query_row_set,
    key_row_set,
    value_row_set,
    grad_rows,
    log_norm,
    delta_row,
    head_indices,
    segment_blocks,
    dilation_rates,
):
    length_all, heads_here, head_size = query_row_set.shape
    rows_per_block = min(512, length_all)
    blocks = length_all // rows_per_block
    scaling = 1.0 / math.sqrt(head_size)
    key_positions = packed_positions(0, length_all, head_indices)

    def step(carry, block_id):
        acc_k, acc_v = carry
        starting_row = block_id * rows_per_block
        q_block = lax.dynamic_slice_in_dim(query_row_set, starting_row, rows_per_block, 0)
        g_block = lax.dynamic_slice_in_dim(grad_rows, starting_row, rows_per_block, 0)
        lse_block = lax.dynamic_slice_in_dim(log_norm, starting_row, rows_per_block, 0).T
        delta_block = lax.dynamic_slice_in_dim(delta_row, starting_row, rows_per_block, 0).T
        counted = dilation_multiplier(
            packed_positions(starting_row, rows_per_block, head_indices),
            key_positions,
            head_indices,
            segment_blocks,
            dilation_rates,
        )
        scores = (
            jnp.einsum("qhd,khd->hqk", q_block, key_row_set, preferred_element_type=jnp.float32)
            * scaling
        )
        masked = jnp.where(counted > 0, scores, -1e30)
        prob_full = counted * jnp.exp(masked - lse_block[:, :, None])
        prob_bf = prob_full.astype(jnp.bfloat16)
        grad_prob = jnp.einsum(
            "qhd,khd->hqk", g_block, value_row_set, preferred_element_type=jnp.float32
        )
        grad_score = (prob_full * (grad_prob - delta_block[:, :, None])).astype(jnp.bfloat16)
        grad_q = (
            jnp.einsum("hqk,khd->qhd", grad_score, key_row_set, preferred_element_type=jnp.float32)
            * scaling
        ).astype(jnp.bfloat16)
        acc_k = acc_k + jnp.einsum(
            "hqk,qhd->khd", grad_score, q_block, preferred_element_type=jnp.float32
        )
        acc_v = acc_v + jnp.einsum(
            "hqk,qhd->khd", prob_bf, g_block, preferred_element_type=jnp.float32
        )
        return ((acc_k, acc_v), grad_q)

    zeros_all = jnp.zeros((length_all, heads_here, head_size), jnp.float32)
    (acc_k, acc_v), grad_q = lax.scan(
        step, (zeros_all, zeros_all), jnp.arange(blocks, dtype=jnp.int32)
    )
    return (
        grad_q.reshape(length_all, heads_here, head_size),
        (acc_k * scaling).astype(jnp.bfloat16),
        acc_v.astype(jnp.bfloat16),
    )


def dense_attention_forward(
    query_row_set, key_row_set, value_row_set, head_indices, segment_blocks, dilation_rates
):
    parity = head_indices % 2
    own_lse = local_lse(query_row_set, key_row_set)
    packed_out, packed_lse = sparse_attention_forward(
        pick_rows(query_row_set, parity),
        pick_rows(key_row_set, parity),
        pick_rows(value_row_set, parity),
        pick_rows(own_lse, parity),
        head_indices,
        segment_blocks,
        dilation_rates,
    )
    log_norm = spread_rows(packed_lse, parity, own_lse)
    attended = add_parts(
        local_output(query_row_set, key_row_set, value_row_set, log_norm), packed_out, parity
    )
    return (attended, log_norm)


def full_backward(
    query_row_set,
    key_row_set,
    value_row_set,
    attended,
    grad_attended,
    log_norm,
    head_indices,
    segment_blocks,
    dilation_rates,
):
    parity = head_indices % 2
    delta_row = jnp.sum(grad_attended.astype(jnp.float32) * attended.astype(jnp.float32), axis=2)
    local_parts = local_backward(
        query_row_set, key_row_set, value_row_set, grad_attended, log_norm, delta_row
    )
    packed_parts = dilated_backward(
        pick_rows(query_row_set, parity),
        pick_rows(key_row_set, parity),
        pick_rows(value_row_set, parity),
        pick_rows(grad_attended, parity),
        pick_rows(log_norm, parity),
        pick_rows(delta_row, parity),
        head_indices,
        segment_blocks,
        dilation_rates,
    )
    return tuple(
        (
            add_parts(first_branch, second, parity)
            for first_branch, second in zip(local_parts, packed_parts)
        )
    )


def token_norm(values, cot_rows, sublayer_norm_gain, sublayer_norm_bias):
    mean_row = jnp.mean(values, axis=1, keepdims=True)
    var_row = jnp.mean(values * values, axis=1, keepdims=True) - mean_row * mean_row
    inv_std = lax.rsqrt(var_row + epsilon)
    centered = (values - mean_row) * inv_std
    normed = (centered * sublayer_norm_gain + sublayer_norm_bias).astype(jnp.bfloat16)
    grad_y = cot_rows.astype(jnp.float32)
    scaled = grad_y * sublayer_norm_gain
    grad_tokens = (
        inv_std
        * (
            scaled
            - jnp.mean(scaled, axis=1, keepdims=True)
            - centered * jnp.mean(scaled * centered, axis=1, keepdims=True)
        )
    ).astype(jnp.bfloat16)
    return (normed, grad_tokens, jnp.sum(grad_y * centered, axis=0), jnp.sum(grad_y, axis=0))


def shards(
    queries,
    key_state_matrix,
    value_state_matrix,
    cotangent,
    sublayer_norm_gain,
    sublayer_norm_bias,
    segment_blocks,
    dilation_rates,
):
    tokens_here = queries.shape[1]
    width_all = queries.shape[2]
    head_size = width_all // H
    ctx_count = lax.axis_size("ctx")
    heads_here = H // ctx_count
    head_first = lax.axis_index("ctx") * heads_here
    head_indices = head_first + jnp.arange(heads_here, dtype=jnp.int32)
    loss_scale = 1.0 / math.sqrt(lax.axis_size("dp") * tokens_here * ctx_count)
    shape_out = (1, tokens_here, width_all)

    def to_heads(array):
        return array.reshape(tokens_here, H, head_size)

    stacked_in = jnp.stack(
        [to_heads(queries[0]), to_heads(key_state_matrix[0]), to_heads(value_state_matrix[0])]
    )
    stacked_in = lax.all_to_all(stacked_in, "ctx", split_axis=2, concat_axis=1, tiled=True)
    query_head_tensor, key_head_tensor, value_head_tensor = (
        stacked_in[0],
        stacked_in[1],
        stacked_in[2],
    )
    attended, log_norm = dense_attention_forward(
        query_head_tensor,
        key_head_tensor,
        value_head_tensor,
        head_indices,
        segment_blocks,
        dilation_rates,
    )
    tokens_view = lax.all_to_all(attended, "ctx", split_axis=0, concat_axis=1, tiled=True).reshape(
        tokens_here, width_all
    )
    normed, grad_tokens, gain_part, bias_part = token_norm(
        tokens_view.astype(jnp.float32), cotangent[0], sublayer_norm_gain, sublayer_norm_bias
    )
    normed = normed.reshape(shape_out)
    grad_attended = lax.all_to_all(
        to_heads(grad_tokens), "ctx", split_axis=1, concat_axis=0, tiled=True
    )
    width_here = width_all // ctx_count
    both = jnp.stack([gain_part, bias_part]).reshape(2, ctx_count, width_here)
    both = lax.all_to_all(jnp.swapaxes(both, 0, 1), "ctx", 0, 0, tiled=True)
    both = jnp.sum(both, axis=0)
    dp_count = lax.axis_size("dp")
    both = jnp.broadcast_to(both[None], (dp_count,) + both.shape)
    both = jnp.sum(lax.all_to_all(both, "dp", 0, 0, tiled=True), axis=0)
    grad_gain, grad_bias = both[0], both[1]
    grad_q, grad_k, grad_v = full_backward(
        query_head_tensor,
        key_head_tensor,
        value_head_tensor,
        attended,
        grad_attended,
        log_norm,
        head_indices,
        segment_blocks,
        dilation_rates,
    )
    stacked_out = lax.all_to_all(
        jnp.stack([grad_q, grad_k, grad_v]), "ctx", split_axis=1, concat_axis=2, tiled=True
    )
    back_q, back_k, back_v = stacked_out[0], stacked_out[1], stacked_out[2]
    return (
        normed,
        back_q.reshape(shape_out),
        back_k.reshape(shape_out),
        back_v.reshape(shape_out),
        grad_gain * loss_scale,
        grad_bias * loss_scale,
    )


def solution(mesh):
    return jax.shard_map(
        shards,
        mesh=mesh,
        in_specs=(
            P("dp", "ctx", None),
            P("dp", "ctx", None),
            P("dp", "ctx", None),
            P("dp", "ctx", None),
            P(),
            P(),
            P(),
            P(),
        ),
        out_specs=(
            P("dp", "ctx", None),
            P("dp", "ctx", None),
            P("dp", "ctx", None),
            P("dp", "ctx", None),
            P("ctx"),
            P("ctx"),
        ),
        check_vma=False,
    )
```

```python
import math

import jax
import jax.numpy as jnp
from jax import lax
from jax.sharding import PartitionSpec as P

H = 16
BLK = 128
G = 4


epsilon = 1e-05


def pick_rows(array, parity):
    pairs = array.reshape((array.shape[0] // 2, 2) + array.shape[1:])
    cond = (parity == 0).reshape((-1,) + (1,) * (array.ndim - 2))
    return jnp.where(cond, pairs[:, 0], pairs[:, 1])


def spread_rows(packed, parity, base):
    pairs = base.reshape((base.shape[0] // 2, 2) + base.shape[1:])
    cond = (parity == 0).reshape((-1,) + (1,) * (base.ndim - 2))
    first_branch = jnp.where(cond, packed, pairs[:, 0])
    second = jnp.where(cond, pairs[:, 1], packed)
    return jnp.stack([first_branch, second], axis=1).reshape(base.shape)


def add_parts(full_part, packed_part, parity):
    spread = spread_rows(packed_part, parity, jnp.zeros_like(full_part))
    full_part = lax.optimization_barrier(full_part)
    spread = lax.optimization_barrier(spread)
    return (full_part.astype(jnp.float32) + spread.astype(jnp.float32)).astype(jnp.bfloat16)


def block_view(array):
    return array.reshape((array.shape[0] // BLK, BLK) + array.shape[1:])


def lse_view(log_norm):
    return jnp.transpose(block_view(log_norm), (0, 2, 1))


def local_scores(query_row_set, key_row_set):
    scaling = 1.0 / math.sqrt(query_row_set.shape[-1])
    return (
        jnp.einsum(
            "bqhd,bkhd->bhqk",
            block_view(query_row_set),
            block_view(key_row_set),
            preferred_element_type=jnp.float32,
        )
        * scaling
    )


def local_lse(query_row_set, key_row_set):
    scores = local_scores(query_row_set, key_row_set)
    row_max = jnp.max(scores, axis=3)
    total = row_max + jnp.log(jnp.sum(jnp.exp(scores - row_max[..., None]), axis=3))
    return jnp.transpose(total, (0, 2, 1)).reshape(query_row_set.shape[0], query_row_set.shape[1])


def local_output(query_row_set, key_row_set, value_row_set, log_norm):
    scores = local_scores(query_row_set, key_row_set)
    prob_bf = jnp.exp(scores - lse_view(log_norm)[..., None]).astype(jnp.bfloat16)
    output = jnp.einsum(
        "bhqk,bkhd->bqhd", prob_bf, block_view(value_row_set), preferred_element_type=jnp.float32
    )
    return output.astype(jnp.bfloat16).reshape(query_row_set.shape)


def local_backward(query_row_set, key_row_set, value_row_set, grad_rows, log_norm, delta_row):
    scaling = 1.0 / math.sqrt(query_row_set.shape[-1])
    scores = local_scores(query_row_set, key_row_set)
    prob_full = jnp.exp(scores - lse_view(log_norm)[..., None])
    prob_bf = prob_full.astype(jnp.bfloat16)
    grad_prob = jnp.einsum(
        "bqhd,bkhd->bhqk",
        block_view(grad_rows),
        block_view(value_row_set),
        preferred_element_type=jnp.float32,
    )
    grad_score = (prob_full * (grad_prob - lse_view(delta_row)[..., None])).astype(jnp.bfloat16)
    grad_q = jnp.einsum(
        "bhqk,bkhd->bqhd", grad_score, block_view(key_row_set), preferred_element_type=jnp.float32
    )
    grad_k = jnp.einsum(
        "bhqk,bqhd->bkhd", grad_score, block_view(query_row_set), preferred_element_type=jnp.float32
    )
    grad_v = jnp.einsum(
        "bhqk,bqhd->bkhd", prob_bf, block_view(grad_rows), preferred_element_type=jnp.float32
    )
    shape = query_row_set.shape
    return (
        (grad_q * scaling).astype(jnp.bfloat16).reshape(shape),
        (grad_k * scaling).astype(jnp.bfloat16).reshape(shape),
        grad_v.astype(jnp.bfloat16).reshape(shape),
    )


def packed_positions(start, count, head_indices):
    rows = start + jnp.arange(count, dtype=jnp.int32)
    return 2 * rows[None, :] + (head_indices % 2)[:, None]


def dilation_multiplier(
    query_positions, key_positions, head_indices, segment_blocks, dilation_rates
):
    counted = jnp.zeros(
        (head_indices.shape[0], query_positions.shape[1], key_positions.shape[1]), jnp.float32
    )
    for dilation_branch in range(1, G):
        seg_width = segment_blocks[dilation_branch] * BLK
        dilation_rate = dilation_rates[dilation_branch]
        same_seg = (
            query_positions[:, :, None] // seg_width == key_positions[:, None, :] // seg_width
        )
        selected_queries = query_positions % dilation_rate == head_indices[:, None] % dilation_rate
        selected_keys = key_positions % dilation_rate == head_indices[:, None] % dilation_rate
        counted = counted + (
            same_seg & selected_queries[:, :, None] & selected_keys[:, None, :]
        ).astype(jnp.float32)
    return counted


def sparse_attention_forward(
    query_row_set,
    key_row_set,
    value_row_set,
    baseline_logsumexp,
    head_indices,
    segment_blocks,
    dilation_rates,
):
    length_all, heads_here, head_size = query_row_set.shape
    rows_per_block = min(512, length_all)
    blocks = length_all // rows_per_block
    scaling = 1.0 / math.sqrt(head_size)
    key_positions = packed_positions(0, length_all, head_indices)

    def one_block(block_id):
        starting_row = block_id * rows_per_block
        q_block = lax.dynamic_slice_in_dim(query_row_set, starting_row, rows_per_block, 0)
        own_lse = lax.dynamic_slice_in_dim(baseline_logsumexp, starting_row, rows_per_block, 0).T
        counted = dilation_multiplier(
            packed_positions(starting_row, rows_per_block, head_indices),
            key_positions,
            head_indices,
            segment_blocks,
            dilation_rates,
        )
        scores = (
            jnp.einsum("qhd,khd->hqk", q_block, key_row_set, preferred_element_type=jnp.float32)
            * scaling
        )
        masked = jnp.where(counted > 0, scores, -1e30)
        row_max = jnp.max(masked, axis=2)
        part_lse = row_max + jnp.log(
            jnp.sum(counted * jnp.exp(masked - row_max[:, :, None]), axis=2)
        )
        top = jnp.maximum(part_lse, own_lse)
        log_norm = top + jnp.log(jnp.exp(part_lse - top) + jnp.exp(own_lse - top))
        prob_bf = (counted * jnp.exp(masked - log_norm[:, :, None])).astype(jnp.bfloat16)
        output = jnp.einsum(
            "hqk,khd->qhd", prob_bf, value_row_set, preferred_element_type=jnp.float32
        ).astype(jnp.bfloat16)
        return (output, log_norm)

    outputs, lse_blocks = lax.map(one_block, jnp.arange(blocks, dtype=jnp.int32))
    return (
        outputs.reshape(length_all, heads_here, head_size),
        jnp.transpose(lse_blocks, (0, 2, 1)).reshape(length_all, heads_here),
    )


def dilated_backward(
    query_row_set,
    key_row_set,
    value_row_set,
    grad_rows,
    log_norm,
    delta_row,
    head_indices,
    segment_blocks,
    dilation_rates,
):
    length_all, heads_here, head_size = query_row_set.shape
    rows_per_block = min(512, length_all)
    blocks = length_all // rows_per_block
    scaling = 1.0 / math.sqrt(head_size)
    key_positions = packed_positions(0, length_all, head_indices)

    def step(carry, block_id):
        acc_k, acc_v = carry
        starting_row = block_id * rows_per_block
        q_block = lax.dynamic_slice_in_dim(query_row_set, starting_row, rows_per_block, 0)
        g_block = lax.dynamic_slice_in_dim(grad_rows, starting_row, rows_per_block, 0)
        lse_block = lax.dynamic_slice_in_dim(log_norm, starting_row, rows_per_block, 0).T
        delta_block = lax.dynamic_slice_in_dim(delta_row, starting_row, rows_per_block, 0).T
        counted = dilation_multiplier(
            packed_positions(starting_row, rows_per_block, head_indices),
            key_positions,
            head_indices,
            segment_blocks,
            dilation_rates,
        )
        scores = (
            jnp.einsum("qhd,khd->hqk", q_block, key_row_set, preferred_element_type=jnp.float32)
            * scaling
        )
        masked = jnp.where(counted > 0, scores, -1e30)
        prob_full = counted * jnp.exp(masked - lse_block[:, :, None])
        prob_bf = prob_full.astype(jnp.bfloat16)
        grad_prob = jnp.einsum(
            "qhd,khd->hqk", g_block, value_row_set, preferred_element_type=jnp.float32
        )
        grad_score = (prob_full * (grad_prob - delta_block[:, :, None])).astype(jnp.bfloat16)
        grad_q = (
            jnp.einsum("hqk,khd->qhd", grad_score, key_row_set, preferred_element_type=jnp.float32)
            * scaling
        ).astype(jnp.bfloat16)
        acc_k = acc_k + jnp.einsum(
            "hqk,qhd->khd", grad_score, q_block, preferred_element_type=jnp.float32
        )
        acc_v = acc_v + jnp.einsum(
            "hqk,qhd->khd", prob_bf, g_block, preferred_element_type=jnp.float32
        )
        return ((acc_k, acc_v), grad_q)

    zeros_all = jnp.zeros((length_all, heads_here, head_size), jnp.float32)
    (acc_k, acc_v), grad_q = lax.scan(
        step, (zeros_all, zeros_all), jnp.arange(blocks, dtype=jnp.int32)
    )
    return (
        grad_q.reshape(length_all, heads_here, head_size),
        (acc_k * scaling).astype(jnp.bfloat16),
        acc_v.astype(jnp.bfloat16),
    )


def dense_attention_forward(
    query_row_set, key_row_set, value_row_set, head_indices, segment_blocks, dilation_rates
):
    parity = head_indices % 2
    own_lse = local_lse(query_row_set, key_row_set)
    packed_out, packed_lse = sparse_attention_forward(
        pick_rows(query_row_set, parity),
        pick_rows(key_row_set, parity),
        pick_rows(value_row_set, parity),
        pick_rows(own_lse, parity),
        head_indices,
        segment_blocks,
        dilation_rates,
    )
    log_norm = spread_rows(packed_lse, parity, own_lse)
    attended = add_parts(
        local_output(query_row_set, key_row_set, value_row_set, log_norm), packed_out, parity
    )
    return (attended, log_norm)


def full_backward(
    query_row_set,
    key_row_set,
    value_row_set,
    attended,
    grad_attended,
    log_norm,
    head_indices,
    segment_blocks,
    dilation_rates,
):
    parity = head_indices % 2
    delta_row = jnp.sum(grad_attended.astype(jnp.float32) * attended.astype(jnp.float32), axis=2)
    local_parts = local_backward(
        query_row_set, key_row_set, value_row_set, grad_attended, log_norm, delta_row
    )
    packed_parts = dilated_backward(
        pick_rows(query_row_set, parity),
        pick_rows(key_row_set, parity),
        pick_rows(value_row_set, parity),
        pick_rows(grad_attended, parity),
        pick_rows(log_norm, parity),
        pick_rows(delta_row, parity),
        head_indices,
        segment_blocks,
        dilation_rates,
    )
    return tuple(
        (
            add_parts(first_branch, second, parity)
            for first_branch, second in zip(local_parts, packed_parts)
        )
    )


def head_major(array, groups):
    tokens, width = array.shape
    return jnp.swapaxes(array.reshape(tokens, groups, width // groups), 0, 1)


def token_major(array):
    groups, tokens, width = array.shape
    return jnp.swapaxes(array, 0, 1).reshape(1, tokens, groups * width)


def head_norm(values, cot_rows, gain, bias):
    feature_axes = (0, 2)
    mean_row = jnp.mean(values, axis=feature_axes, keepdims=True)
    var_row = jnp.mean(values * values, axis=feature_axes, keepdims=True) - mean_row * mean_row
    inv_std = lax.rsqrt(var_row + epsilon)
    centered = (values - mean_row) * inv_std
    normed = (centered * gain + bias).astype(jnp.bfloat16)
    grad_y = cot_rows.astype(jnp.float32)
    scaled = grad_y * gain
    grad_tokens = (
        inv_std
        * (
            scaled
            - jnp.mean(scaled, axis=feature_axes, keepdims=True)
            - centered * jnp.mean(scaled * centered, axis=feature_axes, keepdims=True)
        )
    ).astype(jnp.bfloat16)
    return (normed, grad_tokens, jnp.sum(grad_y * centered, axis=1), jnp.sum(grad_y, axis=1))


def shards(
    queries,
    key_state_matrix,
    value_state_matrix,
    cotangent,
    sublayer_norm_gain,
    sublayer_norm_bias,
    segment_blocks,
    dilation_rates,
):
    tokens_here = queries.shape[1]
    width_all = queries.shape[2]
    head_size = width_all // H
    ctx_count = lax.axis_size("ctx")
    heads_here = H // ctx_count
    width_here = width_all // ctx_count
    head_first = lax.axis_index("ctx") * heads_here
    head_indices = head_first + jnp.arange(heads_here, dtype=jnp.int32)
    loss_scale = 1.0 / math.sqrt(lax.axis_size("dp") * tokens_here * ctx_count)
    tokens_all = tokens_here * ctx_count

    def to_rows(array):
        return array.reshape(tokens_all, heads_here, head_size)

    stacked_in = jnp.stack(
        [
            head_major(queries[0], ctx_count),
            head_major(key_state_matrix[0], ctx_count),
            head_major(value_state_matrix[0], ctx_count),
        ]
    )
    stacked_in = lax.all_to_all(stacked_in, "ctx", split_axis=1, concat_axis=1, tiled=True)
    query_head_tensor, key_head_tensor, value_head_tensor = (
        to_rows(stacked_in[0]),
        to_rows(stacked_in[1]),
        to_rows(stacked_in[2]),
    )
    attended, log_norm = dense_attention_forward(
        query_head_tensor,
        key_head_tensor,
        value_head_tensor,
        head_indices,
        segment_blocks,
        dilation_rates,
    )
    attended_hm = lax.all_to_all(
        attended.reshape(ctx_count, tokens_here, width_here), "ctx", 0, 0, tiled=True
    )
    gain_hm = sublayer_norm_gain.reshape(ctx_count, 1, width_here)
    bias_hm = sublayer_norm_bias.reshape(ctx_count, 1, width_here)
    normed_hm, grad_hm, gain_part, bias_part = head_norm(
        attended_hm.astype(jnp.float32),
        head_major(cotangent[0], ctx_count),
        gain_hm,
        bias_hm,
    )
    normed = token_major(normed_hm)
    grad_attended = to_rows(lax.all_to_all(grad_hm, "ctx", 0, 0, tiled=True))
    both = jnp.stack([gain_part, bias_part], axis=1)
    both = jnp.sum(lax.all_to_all(both, "ctx", 0, 0, tiled=True), axis=0)
    dp_count = lax.axis_size("dp")
    both = jnp.broadcast_to(both[None], (dp_count,) + both.shape)
    both = jnp.sum(lax.all_to_all(both, "dp", 0, 0, tiled=True), axis=0)
    grad_gain, grad_bias = both[0], both[1]
    grad_q, grad_k, grad_v = full_backward(
        query_head_tensor,
        key_head_tensor,
        value_head_tensor,
        attended,
        grad_attended,
        log_norm,
        head_indices,
        segment_blocks,
        dilation_rates,
    )
    stacked_out = lax.all_to_all(
        jnp.stack([part.reshape(ctx_count, tokens_here, width_here) for part in (grad_q, grad_k, grad_v)]),
        "ctx",
        split_axis=1,
        concat_axis=1,
        tiled=True,
    )
    return (
        normed,
        token_major(stacked_out[0]),
        token_major(stacked_out[1]),
        token_major(stacked_out[2]),
        grad_gain * loss_scale,
        grad_bias * loss_scale,
    )


def solution(mesh):
    return jax.shard_map(
        shards,
        mesh=mesh,
        in_specs=(
            P("dp", "ctx", None),
            P("dp", "ctx", None),
            P("dp", "ctx", None),
            P("dp", "ctx", None),
            P(),
            P(),
            P(),
            P(),
        ),
        out_specs=(
            P("dp", "ctx", None),
            P("dp", "ctx", None),
            P("dp", "ctx", None),
            P("dp", "ctx", None),
            P("ctx"),
            P("ctx"),
        ),
        check_vma=False,
    )
```

```python
import math

import jax
import jax.numpy as jnp
from jax import lax
from jax.sharding import PartitionSpec as P

H = 16
BLK = 128
G = 4


epsilon = 1e-05


def pick_rows(array, parity):
    pairs = array.reshape((array.shape[0] // 2, 2) + array.shape[1:])
    cond = (parity == 0).reshape((-1,) + (1,) * (array.ndim - 2))
    return jnp.where(cond, pairs[:, 0], pairs[:, 1])


def spread_rows(packed, parity, base):
    pairs = base.reshape((base.shape[0] // 2, 2) + base.shape[1:])
    cond = (parity == 0).reshape((-1,) + (1,) * (base.ndim - 2))
    first_branch = jnp.where(cond, packed, pairs[:, 0])
    second = jnp.where(cond, pairs[:, 1], packed)
    return jnp.stack([first_branch, second], axis=1).reshape(base.shape)


def add_parts(full_part, packed_part, parity):
    spread = spread_rows(packed_part, parity, jnp.zeros_like(full_part))
    full_part = lax.optimization_barrier(full_part)
    spread = lax.optimization_barrier(spread)
    return (full_part.astype(jnp.float32) + spread.astype(jnp.float32)).astype(jnp.bfloat16)


def block_view(array):
    return array.reshape((array.shape[0] // BLK, BLK) + array.shape[1:])


def lse_view(log_norm):
    return jnp.transpose(block_view(log_norm), (0, 2, 1))


def local_scores(query_row_set, key_row_set):
    scaling = 1.0 / math.sqrt(query_row_set.shape[-1])
    return (
        jnp.einsum(
            "bqhd,bkhd->bhqk",
            block_view(query_row_set),
            block_view(key_row_set),
            preferred_element_type=jnp.float32,
        )
        * scaling
    )


def local_lse(query_row_set, key_row_set):
    scores = local_scores(query_row_set, key_row_set)
    row_max = jnp.max(scores, axis=3)
    total = row_max + jnp.log(jnp.sum(jnp.exp(scores - row_max[..., None]), axis=3))
    return jnp.transpose(total, (0, 2, 1)).reshape(query_row_set.shape[0], query_row_set.shape[1])


def local_output(query_row_set, key_row_set, value_row_set, log_norm):
    scores = local_scores(query_row_set, key_row_set)
    prob_bf = jnp.exp(scores - lse_view(log_norm)[..., None]).astype(jnp.bfloat16)
    output = jnp.einsum(
        "bhqk,bkhd->bqhd", prob_bf, block_view(value_row_set), preferred_element_type=jnp.float32
    )
    return output.astype(jnp.bfloat16).reshape(query_row_set.shape)


def local_backward(query_row_set, key_row_set, value_row_set, grad_rows, log_norm, delta_row):
    scaling = 1.0 / math.sqrt(query_row_set.shape[-1])
    scores = local_scores(query_row_set, key_row_set)
    prob_full = jnp.exp(scores - lse_view(log_norm)[..., None])
    prob_bf = prob_full.astype(jnp.bfloat16)
    grad_prob = jnp.einsum(
        "bqhd,bkhd->bhqk",
        block_view(grad_rows),
        block_view(value_row_set),
        preferred_element_type=jnp.float32,
    )
    grad_score = (prob_full * (grad_prob - lse_view(delta_row)[..., None])).astype(jnp.bfloat16)
    grad_q = jnp.einsum(
        "bhqk,bkhd->bqhd", grad_score, block_view(key_row_set), preferred_element_type=jnp.float32
    )
    grad_k = jnp.einsum(
        "bhqk,bqhd->bkhd", grad_score, block_view(query_row_set), preferred_element_type=jnp.float32
    )
    grad_v = jnp.einsum(
        "bhqk,bqhd->bkhd", prob_bf, block_view(grad_rows), preferred_element_type=jnp.float32
    )
    shape = query_row_set.shape
    return (
        (grad_q * scaling).astype(jnp.bfloat16).reshape(shape),
        (grad_k * scaling).astype(jnp.bfloat16).reshape(shape),
        grad_v.astype(jnp.bfloat16).reshape(shape),
    )


def packed_positions(start, count, head_indices):
    rows = start + jnp.arange(count, dtype=jnp.int32)
    return 2 * rows[None, :] + (head_indices % 2)[:, None]


def dilation_multiplier(
    query_positions, key_positions, head_indices, segment_blocks, dilation_rates
):
    counted = jnp.zeros(
        (head_indices.shape[0], query_positions.shape[1], key_positions.shape[1]), jnp.float32
    )
    for dilation_branch in range(1, G):
        seg_width = segment_blocks[dilation_branch] * BLK
        dilation_rate = dilation_rates[dilation_branch]
        same_seg = (
            query_positions[:, :, None] // seg_width == key_positions[:, None, :] // seg_width
        )
        selected_queries = query_positions % dilation_rate == head_indices[:, None] % dilation_rate
        selected_keys = key_positions % dilation_rate == head_indices[:, None] % dilation_rate
        counted = counted + (
            same_seg & selected_queries[:, :, None] & selected_keys[:, None, :]
        ).astype(jnp.float32)
    return counted


def sparse_attention_forward(
    query_row_set,
    key_row_set,
    value_row_set,
    baseline_logsumexp,
    head_indices,
    segment_blocks,
    dilation_rates,
):
    length_all, heads_here, head_size = query_row_set.shape
    rows_per_block = length_all
    blocks = length_all // rows_per_block
    scaling = 1.0 / math.sqrt(head_size)
    key_positions = packed_positions(0, length_all, head_indices)

    def one_block(block_id):
        starting_row = block_id * rows_per_block
        q_block = lax.dynamic_slice_in_dim(query_row_set, starting_row, rows_per_block, 0)
        own_lse = lax.dynamic_slice_in_dim(baseline_logsumexp, starting_row, rows_per_block, 0).T
        counted = dilation_multiplier(
            packed_positions(starting_row, rows_per_block, head_indices),
            key_positions,
            head_indices,
            segment_blocks,
            dilation_rates,
        )
        scores = (
            jnp.einsum("qhd,khd->hqk", q_block, key_row_set, preferred_element_type=jnp.float32)
            * scaling
        )
        masked = jnp.where(counted > 0, scores, -1e30)
        row_max = jnp.max(masked, axis=2)
        part_lse = row_max + jnp.log(
            jnp.sum(counted * jnp.exp(masked - row_max[:, :, None]), axis=2)
        )
        top = jnp.maximum(part_lse, own_lse)
        log_norm = top + jnp.log(jnp.exp(part_lse - top) + jnp.exp(own_lse - top))
        prob_bf = (counted * jnp.exp(masked - log_norm[:, :, None])).astype(jnp.bfloat16)
        output = jnp.einsum(
            "hqk,khd->qhd", prob_bf, value_row_set, preferred_element_type=jnp.float32
        ).astype(jnp.bfloat16)
        return (output, log_norm)

    outputs, lse_blocks = lax.map(one_block, jnp.arange(blocks, dtype=jnp.int32))
    return (
        outputs.reshape(length_all, heads_here, head_size),
        jnp.transpose(lse_blocks, (0, 2, 1)).reshape(length_all, heads_here),
    )


def dilated_backward(
    query_row_set,
    key_row_set,
    value_row_set,
    grad_rows,
    log_norm,
    delta_row,
    head_indices,
    segment_blocks,
    dilation_rates,
):
    length_all, heads_here, head_size = query_row_set.shape
    rows_per_block = length_all
    blocks = length_all // rows_per_block
    scaling = 1.0 / math.sqrt(head_size)
    key_positions = packed_positions(0, length_all, head_indices)

    def step(carry, block_id):
        acc_k, acc_v = carry
        starting_row = block_id * rows_per_block
        q_block = lax.dynamic_slice_in_dim(query_row_set, starting_row, rows_per_block, 0)
        g_block = lax.dynamic_slice_in_dim(grad_rows, starting_row, rows_per_block, 0)
        lse_block = lax.dynamic_slice_in_dim(log_norm, starting_row, rows_per_block, 0).T
        delta_block = lax.dynamic_slice_in_dim(delta_row, starting_row, rows_per_block, 0).T
        counted = dilation_multiplier(
            packed_positions(starting_row, rows_per_block, head_indices),
            key_positions,
            head_indices,
            segment_blocks,
            dilation_rates,
        )
        scores = (
            jnp.einsum("qhd,khd->hqk", q_block, key_row_set, preferred_element_type=jnp.float32)
            * scaling
        )
        masked = jnp.where(counted > 0, scores, -1e30)
        prob_full = counted * jnp.exp(masked - lse_block[:, :, None])
        prob_bf = prob_full.astype(jnp.bfloat16)
        grad_prob = jnp.einsum(
            "qhd,khd->hqk", g_block, value_row_set, preferred_element_type=jnp.float32
        )
        grad_score = (prob_full * (grad_prob - delta_block[:, :, None])).astype(jnp.bfloat16)
        grad_q = (
            jnp.einsum("hqk,khd->qhd", grad_score, key_row_set, preferred_element_type=jnp.float32)
            * scaling
        ).astype(jnp.bfloat16)
        acc_k = acc_k + jnp.einsum(
            "hqk,qhd->khd", grad_score, q_block, preferred_element_type=jnp.float32
        )
        acc_v = acc_v + jnp.einsum(
            "hqk,qhd->khd", prob_bf, g_block, preferred_element_type=jnp.float32
        )
        return ((acc_k, acc_v), grad_q)

    zeros_all = jnp.zeros((length_all, heads_here, head_size), jnp.float32)
    (acc_k, acc_v), grad_q = lax.scan(
        step, (zeros_all, zeros_all), jnp.arange(blocks, dtype=jnp.int32)
    )
    return (
        grad_q.reshape(length_all, heads_here, head_size),
        (acc_k * scaling).astype(jnp.bfloat16),
        acc_v.astype(jnp.bfloat16),
    )


def dense_attention_forward(
    query_row_set, key_row_set, value_row_set, head_indices, segment_blocks, dilation_rates
):
    parity = head_indices % 2
    own_lse = local_lse(query_row_set, key_row_set)
    packed_out, packed_lse = sparse_attention_forward(
        pick_rows(query_row_set, parity),
        pick_rows(key_row_set, parity),
        pick_rows(value_row_set, parity),
        pick_rows(own_lse, parity),
        head_indices,
        segment_blocks,
        dilation_rates,
    )
    log_norm = spread_rows(packed_lse, parity, own_lse)
    attended = add_parts(
        local_output(query_row_set, key_row_set, value_row_set, log_norm), packed_out, parity
    )
    return (attended, log_norm)


def full_backward(
    query_row_set,
    key_row_set,
    value_row_set,
    attended,
    grad_attended,
    log_norm,
    head_indices,
    segment_blocks,
    dilation_rates,
):
    parity = head_indices % 2
    delta_row = jnp.sum(grad_attended.astype(jnp.float32) * attended.astype(jnp.float32), axis=2)
    local_parts = local_backward(
        query_row_set, key_row_set, value_row_set, grad_attended, log_norm, delta_row
    )
    packed_parts = dilated_backward(
        pick_rows(query_row_set, parity),
        pick_rows(key_row_set, parity),
        pick_rows(value_row_set, parity),
        pick_rows(grad_attended, parity),
        pick_rows(log_norm, parity),
        pick_rows(delta_row, parity),
        head_indices,
        segment_blocks,
        dilation_rates,
    )
    return tuple(
        (
            add_parts(first_branch, second, parity)
            for first_branch, second in zip(local_parts, packed_parts)
        )
    )


def head_major(array, groups):
    tokens, width = array.shape
    return jnp.swapaxes(array.reshape(tokens, groups, width // groups), 0, 1)


def token_major(array):
    groups, tokens, width = array.shape
    return jnp.swapaxes(array, 0, 1).reshape(1, tokens, groups * width)


def head_norm(values, cot_rows, gain, bias):
    feature_axes = (0, 2)
    mean_row = jnp.mean(values, axis=feature_axes, keepdims=True)
    var_row = jnp.mean(values * values, axis=feature_axes, keepdims=True) - mean_row * mean_row
    inv_std = lax.rsqrt(var_row + epsilon)
    centered = (values - mean_row) * inv_std
    normed = (centered * gain + bias).astype(jnp.bfloat16)
    grad_y = cot_rows.astype(jnp.float32)
    scaled = grad_y * gain
    grad_tokens = (
        inv_std
        * (
            scaled
            - jnp.mean(scaled, axis=feature_axes, keepdims=True)
            - centered * jnp.mean(scaled * centered, axis=feature_axes, keepdims=True)
        )
    ).astype(jnp.bfloat16)
    return (normed, grad_tokens, jnp.sum(grad_y * centered, axis=1), jnp.sum(grad_y, axis=1))


def shards(
    queries,
    key_state_matrix,
    value_state_matrix,
    cotangent,
    sublayer_norm_gain,
    sublayer_norm_bias,
    segment_blocks,
    dilation_rates,
):
    tokens_here = queries.shape[1]
    width_all = queries.shape[2]
    head_size = width_all // H
    ctx_count = lax.axis_size("ctx")
    heads_here = H // ctx_count
    width_here = width_all // ctx_count
    head_first = lax.axis_index("ctx") * heads_here
    head_indices = head_first + jnp.arange(heads_here, dtype=jnp.int32)
    loss_scale = 1.0 / math.sqrt(lax.axis_size("dp") * tokens_here * ctx_count)
    tokens_all = tokens_here * ctx_count

    def to_rows(array):
        return array.reshape(tokens_all, heads_here, head_size)

    stacked_in = jnp.stack(
        [
            head_major(queries[0], ctx_count),
            head_major(key_state_matrix[0], ctx_count),
            head_major(value_state_matrix[0], ctx_count),
        ]
    )
    stacked_in = lax.all_to_all(stacked_in, "ctx", split_axis=1, concat_axis=1, tiled=True)
    query_head_tensor, key_head_tensor, value_head_tensor = (
        to_rows(stacked_in[0]),
        to_rows(stacked_in[1]),
        to_rows(stacked_in[2]),
    )
    attended, log_norm = dense_attention_forward(
        query_head_tensor,
        key_head_tensor,
        value_head_tensor,
        head_indices,
        segment_blocks,
        dilation_rates,
    )
    attended_hm = lax.all_to_all(
        attended.reshape(ctx_count, tokens_here, width_here), "ctx", 0, 0, tiled=True
    )
    gain_hm = sublayer_norm_gain.reshape(ctx_count, 1, width_here)
    bias_hm = sublayer_norm_bias.reshape(ctx_count, 1, width_here)
    normed_hm, grad_hm, gain_part, bias_part = head_norm(
        attended_hm.astype(jnp.float32),
        head_major(cotangent[0], ctx_count),
        gain_hm,
        bias_hm,
    )
    normed = token_major(normed_hm)
    grad_attended = to_rows(lax.all_to_all(grad_hm, "ctx", 0, 0, tiled=True))
    both = jnp.stack([gain_part, bias_part], axis=1)
    both = jnp.sum(lax.all_to_all(both, "ctx", 0, 0, tiled=True), axis=0)
    dp_count = lax.axis_size("dp")
    both = jnp.broadcast_to(both[None], (dp_count,) + both.shape)
    both = jnp.sum(lax.all_to_all(both, "dp", 0, 0, tiled=True), axis=0)
    grad_gain, grad_bias = both[0], both[1]
    grad_q, grad_k, grad_v = full_backward(
        query_head_tensor,
        key_head_tensor,
        value_head_tensor,
        attended,
        grad_attended,
        log_norm,
        head_indices,
        segment_blocks,
        dilation_rates,
    )
    stacked_out = lax.all_to_all(
        jnp.stack([part.reshape(ctx_count, tokens_here, width_here) for part in (grad_q, grad_k, grad_v)]),
        "ctx",
        split_axis=1,
        concat_axis=1,
        tiled=True,
    )
    return (
        normed,
        token_major(stacked_out[0]),
        token_major(stacked_out[1]),
        token_major(stacked_out[2]),
        grad_gain * loss_scale,
        grad_bias * loss_scale,
    )


def solution(mesh):
    return jax.shard_map(
        shards,
        mesh=mesh,
        in_specs=(
            P("dp", "ctx", None),
            P("dp", "ctx", None),
            P("dp", "ctx", None),
            P("dp", "ctx", None),
            P(),
            P(),
            P(),
            P(),
        ),
        out_specs=(
            P("dp", "ctx", None),
            P("dp", "ctx", None),
            P("dp", "ctx", None),
            P("dp", "ctx", None),
            P("ctx"),
            P("ctx"),
        ),
        check_vma=False,
    )
```

```python
import math

import jax
import jax.numpy as jnp
from jax import lax
from jax.sharding import PartitionSpec as P

H = 16
BLK = 128
G = 4


epsilon = 1e-05


def pick_rows(array, parity):
    pairs = array.reshape((array.shape[0] // 2, 2) + array.shape[1:])
    cond = (parity == 0).reshape((-1,) + (1,) * (array.ndim - 2))
    return jnp.where(cond, pairs[:, 0], pairs[:, 1])


def spread_rows(packed, parity, base):
    pairs = base.reshape((base.shape[0] // 2, 2) + base.shape[1:])
    cond = (parity == 0).reshape((-1,) + (1,) * (base.ndim - 2))
    first_branch = jnp.where(cond, packed, pairs[:, 0])
    second = jnp.where(cond, pairs[:, 1], packed)
    return jnp.stack([first_branch, second], axis=1).reshape(base.shape)


def add_parts(full_part, packed_part, parity):
    spread = spread_rows(packed_part, parity, jnp.zeros_like(full_part))
    full_part = lax.optimization_barrier(full_part)
    spread = lax.optimization_barrier(spread)
    return (full_part.astype(jnp.float32) + spread.astype(jnp.float32)).astype(jnp.bfloat16)


def block_view(array):
    return array.reshape((array.shape[0] // BLK, BLK) + array.shape[1:])


def lse_view(log_norm):
    return jnp.transpose(block_view(log_norm), (0, 2, 1))


def local_scores(query_row_set, key_row_set):
    scaling = 1.0 / math.sqrt(query_row_set.shape[-1])
    return (
        jnp.einsum(
            "bqhd,bkhd->bhqk",
            block_view(query_row_set),
            block_view(key_row_set),
            preferred_element_type=jnp.float32,
        )
        * scaling
    )


def local_lse(query_row_set, key_row_set):
    scores = local_scores(query_row_set, key_row_set)
    row_max = jnp.max(scores, axis=3)
    total = row_max + jnp.log(jnp.sum(jnp.exp(scores - row_max[..., None]), axis=3))
    return jnp.transpose(total, (0, 2, 1)).reshape(query_row_set.shape[0], query_row_set.shape[1])


def local_output(query_row_set, key_row_set, value_row_set, log_norm):
    scores = local_scores(query_row_set, key_row_set)
    prob_bf = jnp.exp(scores - lse_view(log_norm)[..., None]).astype(jnp.bfloat16)
    output = jnp.einsum(
        "bhqk,bkhd->bqhd", prob_bf, block_view(value_row_set), preferred_element_type=jnp.float32
    )
    return output.astype(jnp.bfloat16).reshape(query_row_set.shape)


def local_backward(query_row_set, key_row_set, value_row_set, grad_rows, log_norm, delta_row):
    scaling = 1.0 / math.sqrt(query_row_set.shape[-1])
    scores = local_scores(query_row_set, key_row_set)
    prob_full = jnp.exp(scores - lse_view(log_norm)[..., None])
    prob_bf = prob_full.astype(jnp.bfloat16)
    grad_prob = jnp.einsum(
        "bqhd,bkhd->bhqk",
        block_view(grad_rows),
        block_view(value_row_set),
        preferred_element_type=jnp.float32,
    )
    grad_score = (prob_full * (grad_prob - lse_view(delta_row)[..., None])).astype(jnp.bfloat16)
    grad_q = jnp.einsum(
        "bhqk,bkhd->bqhd", grad_score, block_view(key_row_set), preferred_element_type=jnp.float32
    )
    grad_k = jnp.einsum(
        "bhqk,bqhd->bkhd", grad_score, block_view(query_row_set), preferred_element_type=jnp.float32
    )
    grad_v = jnp.einsum(
        "bhqk,bqhd->bkhd", prob_bf, block_view(grad_rows), preferred_element_type=jnp.float32
    )
    shape = query_row_set.shape
    return (
        (grad_q * scaling).astype(jnp.bfloat16).reshape(shape),
        (grad_k * scaling).astype(jnp.bfloat16).reshape(shape),
        grad_v.astype(jnp.bfloat16).reshape(shape),
    )


def packed_positions(start, count, head_indices):
    rows = start + jnp.arange(count, dtype=jnp.int32)
    return 2 * rows[None, :] + (head_indices % 2)[:, None]


def dilation_multiplier(
    query_positions, key_positions, head_indices, segment_blocks, dilation_rates
):
    counted = jnp.zeros(
        (head_indices.shape[0], query_positions.shape[1], key_positions.shape[1]), jnp.float32
    )
    for dilation_branch in range(1, G):
        seg_width = segment_blocks[dilation_branch] * BLK
        dilation_rate = dilation_rates[dilation_branch]
        same_seg = (
            query_positions[:, :, None] // seg_width == key_positions[:, None, :] // seg_width
        )
        selected_queries = query_positions % dilation_rate == head_indices[:, None] % dilation_rate
        selected_keys = key_positions % dilation_rate == head_indices[:, None] % dilation_rate
        counted = counted + (
            same_seg & selected_queries[:, :, None] & selected_keys[:, None, :]
        ).astype(jnp.float32)
    return counted


def sparse_attention_forward(
    query_row_set,
    key_row_set,
    value_row_set,
    baseline_logsumexp,
    head_indices,
    segment_blocks,
    dilation_rates,
):
    length_all, heads_here, head_size = query_row_set.shape
    scaling = 1.0 / math.sqrt(head_size)
    positions = packed_positions(0, length_all, head_indices)
    counted = dilation_multiplier(
        positions, positions, head_indices, segment_blocks, dilation_rates
    )
    own_lse = baseline_logsumexp.T
    scores = (
        jnp.einsum("qhd,khd->hqk", query_row_set, key_row_set, preferred_element_type=jnp.float32)
        * scaling
    )
    masked = jnp.where(counted > 0, scores, -1e30)
    row_max = jnp.max(masked, axis=2)
    part_lse = row_max + jnp.log(jnp.sum(counted * jnp.exp(masked - row_max[:, :, None]), axis=2))
    top = jnp.maximum(part_lse, own_lse)
    log_norm = top + jnp.log(jnp.exp(part_lse - top) + jnp.exp(own_lse - top))
    prob_full = counted * jnp.exp(masked - log_norm[:, :, None])
    output = jnp.einsum(
        "hqk,khd->qhd",
        prob_full.astype(jnp.bfloat16),
        value_row_set,
        preferred_element_type=jnp.float32,
    ).astype(jnp.bfloat16)
    return (output, log_norm.T, prob_full)


def dilated_backward(
    query_row_set,
    key_row_set,
    value_row_set,
    grad_rows,
    prob_full,
    delta_row,
):
    head_size = query_row_set.shape[-1]
    scaling = 1.0 / math.sqrt(head_size)
    prob_bf = prob_full.astype(jnp.bfloat16)
    grad_prob = jnp.einsum(
        "qhd,khd->hqk", grad_rows, value_row_set, preferred_element_type=jnp.float32
    )
    grad_score = (prob_full * (grad_prob - delta_row.T[:, :, None])).astype(jnp.bfloat16)
    grad_q = (
        jnp.einsum("hqk,khd->qhd", grad_score, key_row_set, preferred_element_type=jnp.float32)
        * scaling
    ).astype(jnp.bfloat16)
    grad_k = (
        jnp.einsum("hqk,qhd->khd", grad_score, query_row_set, preferred_element_type=jnp.float32)
        * scaling
    ).astype(jnp.bfloat16)
    grad_v = jnp.einsum(
        "hqk,qhd->khd", prob_bf, grad_rows, preferred_element_type=jnp.float32
    ).astype(jnp.bfloat16)
    return (grad_q, grad_k, grad_v)


def dense_attention_forward(
    query_row_set, key_row_set, value_row_set, head_indices, segment_blocks, dilation_rates
):
    parity = head_indices % 2
    own_lse = local_lse(query_row_set, key_row_set)
    packed_out, packed_lse, prob_full = sparse_attention_forward(
        pick_rows(query_row_set, parity),
        pick_rows(key_row_set, parity),
        pick_rows(value_row_set, parity),
        pick_rows(own_lse, parity),
        head_indices,
        segment_blocks,
        dilation_rates,
    )
    log_norm = spread_rows(packed_lse, parity, own_lse)
    attended = add_parts(
        local_output(query_row_set, key_row_set, value_row_set, log_norm), packed_out, parity
    )
    return (attended, log_norm, prob_full)


def full_backward(
    query_row_set,
    key_row_set,
    value_row_set,
    attended,
    grad_attended,
    log_norm,
    prob_full,
    head_indices,
):
    parity = head_indices % 2
    delta_row = jnp.sum(grad_attended.astype(jnp.float32) * attended.astype(jnp.float32), axis=2)
    local_parts = local_backward(
        query_row_set, key_row_set, value_row_set, grad_attended, log_norm, delta_row
    )
    packed_parts = dilated_backward(
        pick_rows(query_row_set, parity),
        pick_rows(key_row_set, parity),
        pick_rows(value_row_set, parity),
        pick_rows(grad_attended, parity),
        prob_full,
        pick_rows(delta_row, parity),
    )
    return tuple(
        (
            add_parts(first_branch, second, parity)
            for first_branch, second in zip(local_parts, packed_parts)
        )
    )


def head_major(array, groups):
    tokens, width = array.shape
    return jnp.swapaxes(array.reshape(tokens, groups, width // groups), 0, 1)


def token_major(array):
    groups, tokens, width = array.shape
    return jnp.swapaxes(array, 0, 1).reshape(1, tokens, groups * width)


def head_norm(values, cot_rows, gain, bias):
    feature_axes = (0, 2)
    mean_row = jnp.mean(values, axis=feature_axes, keepdims=True)
    var_row = jnp.mean(values * values, axis=feature_axes, keepdims=True) - mean_row * mean_row
    inv_std = lax.rsqrt(var_row + epsilon)
    centered = (values - mean_row) * inv_std
    normed = (centered * gain + bias).astype(jnp.bfloat16)
    grad_y = cot_rows.astype(jnp.float32)
    scaled = grad_y * gain
    grad_tokens = (
        inv_std
        * (
            scaled
            - jnp.mean(scaled, axis=feature_axes, keepdims=True)
            - centered * jnp.mean(scaled * centered, axis=feature_axes, keepdims=True)
        )
    ).astype(jnp.bfloat16)
    return (normed, grad_tokens, jnp.sum(grad_y * centered, axis=1), jnp.sum(grad_y, axis=1))


def shards(
    queries,
    key_state_matrix,
    value_state_matrix,
    cotangent,
    sublayer_norm_gain,
    sublayer_norm_bias,
    segment_blocks,
    dilation_rates,
):
    tokens_here = queries.shape[1]
    width_all = queries.shape[2]
    head_size = width_all // H
    ctx_count = lax.axis_size("ctx")
    heads_here = H // ctx_count
    width_here = width_all // ctx_count
    head_first = lax.axis_index("ctx") * heads_here
    head_indices = head_first + jnp.arange(heads_here, dtype=jnp.int32)
    loss_scale = 1.0 / math.sqrt(lax.axis_size("dp") * tokens_here * ctx_count)
    tokens_all = tokens_here * ctx_count

    def to_rows(array):
        return array.reshape(tokens_all, heads_here, head_size)

    stacked_in = jnp.stack(
        [
            head_major(queries[0], ctx_count),
            head_major(key_state_matrix[0], ctx_count),
            head_major(value_state_matrix[0], ctx_count),
        ]
    )
    stacked_in = lax.all_to_all(stacked_in, "ctx", split_axis=1, concat_axis=1, tiled=True)
    query_head_tensor, key_head_tensor, value_head_tensor = (
        to_rows(stacked_in[0]),
        to_rows(stacked_in[1]),
        to_rows(stacked_in[2]),
    )
    attended, log_norm, prob_full = dense_attention_forward(
        query_head_tensor,
        key_head_tensor,
        value_head_tensor,
        head_indices,
        segment_blocks,
        dilation_rates,
    )
    attended_hm = lax.all_to_all(
        attended.reshape(ctx_count, tokens_here, width_here), "ctx", 0, 0, tiled=True
    )
    gain_hm = sublayer_norm_gain.reshape(ctx_count, 1, width_here)
    bias_hm = sublayer_norm_bias.reshape(ctx_count, 1, width_here)
    normed_hm, grad_hm, gain_part, bias_part = head_norm(
        attended_hm.astype(jnp.float32),
        head_major(cotangent[0], ctx_count),
        gain_hm,
        bias_hm,
    )
    normed = token_major(normed_hm)
    grad_attended = to_rows(lax.all_to_all(grad_hm, "ctx", 0, 0, tiled=True))
    both = jnp.stack([gain_part, bias_part], axis=1)
    both = jnp.sum(lax.all_to_all(both, "ctx", 0, 0, tiled=True), axis=0)
    dp_count = lax.axis_size("dp")
    both = jnp.broadcast_to(both[None], (dp_count,) + both.shape)
    both = jnp.sum(lax.all_to_all(both, "dp", 0, 0, tiled=True), axis=0)
    grad_gain, grad_bias = both[0], both[1]
    grad_q, grad_k, grad_v = full_backward(
        query_head_tensor,
        key_head_tensor,
        value_head_tensor,
        attended,
        grad_attended,
        log_norm,
        prob_full,
        head_indices,
    )
    stacked_out = lax.all_to_all(
        jnp.stack([part.reshape(ctx_count, tokens_here, width_here) for part in (grad_q, grad_k, grad_v)]),
        "ctx",
        split_axis=1,
        concat_axis=1,
        tiled=True,
    )
    return (
        normed,
        token_major(stacked_out[0]),
        token_major(stacked_out[1]),
        token_major(stacked_out[2]),
        grad_gain * loss_scale,
        grad_bias * loss_scale,
    )


def solution(mesh):
    return jax.shard_map(
        shards,
        mesh=mesh,
        in_specs=(
            P("dp", "ctx", None),
            P("dp", "ctx", None),
            P("dp", "ctx", None),
            P("dp", "ctx", None),
            P(),
            P(),
            P(),
            P(),
        ),
        out_specs=(
            P("dp", "ctx", None),
            P("dp", "ctx", None),
            P("dp", "ctx", None),
            P("dp", "ctx", None),
            P("ctx"),
            P("ctx"),
        ),
        check_vma=False,
    )
```

```python
import math

import jax
import jax.numpy as jnp
from jax import lax
from jax.sharding import PartitionSpec as P

H = 16
BLK = 128
G = 4


epsilon = 1e-05


def pick_rows(array, parity):
    pairs = array.reshape((array.shape[0] // 2, 2) + array.shape[1:])
    cond = (parity == 0).reshape((-1,) + (1,) * (array.ndim - 2))
    return jnp.where(cond, pairs[:, 0], pairs[:, 1])


def spread_rows(packed, parity, base):
    pairs = base.reshape((base.shape[0] // 2, 2) + base.shape[1:])
    cond = (parity == 0).reshape((-1,) + (1,) * (base.ndim - 2))
    first_branch = jnp.where(cond, packed, pairs[:, 0])
    second = jnp.where(cond, pairs[:, 1], packed)
    return jnp.stack([first_branch, second], axis=1).reshape(base.shape)


def add_parts(full_part, packed_part, parity):
    spread = spread_rows(packed_part, parity, jnp.zeros_like(full_part))
    full_part = lax.optimization_barrier(full_part)
    spread = lax.optimization_barrier(spread)
    return (full_part.astype(jnp.float32) + spread.astype(jnp.float32)).astype(jnp.bfloat16)


def block_view(array):
    return array.reshape((array.shape[0] // BLK, BLK) + array.shape[1:])


def lse_view(log_norm):
    return jnp.transpose(block_view(log_norm), (0, 2, 1))


def local_scores(query_row_set, key_row_set):
    scaling = 1.0 / math.sqrt(query_row_set.shape[-1])
    return (
        jnp.einsum(
            "bqhd,bkhd->bhqk",
            block_view(query_row_set),
            block_view(key_row_set),
            preferred_element_type=jnp.float32,
        )
        * scaling
    )


def local_lse(query_row_set, key_row_set):
    scores = local_scores(query_row_set, key_row_set)
    row_max = jnp.max(scores, axis=3)
    total = row_max + jnp.log(jnp.sum(jnp.exp(scores - row_max[..., None]), axis=3))
    return jnp.transpose(total, (0, 2, 1)).reshape(query_row_set.shape[0], query_row_set.shape[1])


def local_output(query_row_set, key_row_set, value_row_set, log_norm):
    scores = local_scores(query_row_set, key_row_set)
    prob_bf = jnp.exp(scores - lse_view(log_norm)[..., None]).astype(jnp.bfloat16)
    output = jnp.einsum(
        "bhqk,bkhd->bqhd", prob_bf, block_view(value_row_set), preferred_element_type=jnp.float32
    )
    return output.astype(jnp.bfloat16).reshape(query_row_set.shape)


def local_backward(query_row_set, key_row_set, value_row_set, grad_rows, log_norm, delta_row):
    scaling = 1.0 / math.sqrt(query_row_set.shape[-1])
    scores = local_scores(query_row_set, key_row_set)
    prob_full = jnp.exp(scores - lse_view(log_norm)[..., None])
    prob_bf = prob_full.astype(jnp.bfloat16)
    grad_prob = jnp.einsum(
        "bqhd,bkhd->bhqk",
        block_view(grad_rows),
        block_view(value_row_set),
        preferred_element_type=jnp.float32,
    )
    grad_score = (prob_full * (grad_prob - lse_view(delta_row)[..., None])).astype(jnp.bfloat16)
    grad_q = jnp.einsum(
        "bhqk,bkhd->bqhd", grad_score, block_view(key_row_set), preferred_element_type=jnp.float32
    )
    grad_k = jnp.einsum(
        "bhqk,bqhd->bkhd", grad_score, block_view(query_row_set), preferred_element_type=jnp.float32
    )
    grad_v = jnp.einsum(
        "bhqk,bqhd->bkhd", prob_bf, block_view(grad_rows), preferred_element_type=jnp.float32
    )
    shape = query_row_set.shape
    return (
        (grad_q * scaling).astype(jnp.bfloat16).reshape(shape),
        (grad_k * scaling).astype(jnp.bfloat16).reshape(shape),
        grad_v.astype(jnp.bfloat16).reshape(shape),
    )


def packed_positions(start, count, head_indices):
    rows = start + jnp.arange(count, dtype=jnp.int32)
    return 2 * rows[None, :] + (head_indices % 2)[:, None]


def dilation_multiplier(
    query_positions, key_positions, head_indices, segment_blocks, dilation_rates
):
    counted = jnp.zeros(
        (head_indices.shape[0], query_positions.shape[1], key_positions.shape[1]), jnp.float32
    )
    for dilation_branch in range(1, G):
        seg_width = segment_blocks[dilation_branch] * BLK
        low_bits = dilation_rates[dilation_branch] - 1
        same_seg = (query_positions[:, :, None] ^ key_positions[:, None, :]) < seg_width
        selected_queries = ((query_positions ^ head_indices[:, None]) & low_bits) == 0
        selected_keys = ((key_positions ^ head_indices[:, None]) & low_bits) == 0
        counted = counted + (
            same_seg & selected_queries[:, :, None] & selected_keys[:, None, :]
        ).astype(jnp.float32)
    return counted


def sparse_attention_forward(
    query_row_set,
    key_row_set,
    value_row_set,
    baseline_logsumexp,
    head_indices,
    segment_blocks,
    dilation_rates,
):
    length_all, heads_here, head_size = query_row_set.shape
    rows_per_block = length_all
    blocks = length_all // rows_per_block
    scaling = 1.0 / math.sqrt(head_size)
    key_positions = packed_positions(0, length_all, head_indices)

    def one_block(block_id):
        starting_row = block_id * rows_per_block
        q_block = lax.dynamic_slice_in_dim(query_row_set, starting_row, rows_per_block, 0)
        own_lse = lax.dynamic_slice_in_dim(baseline_logsumexp, starting_row, rows_per_block, 0).T
        counted = dilation_multiplier(
            packed_positions(starting_row, rows_per_block, head_indices),
            key_positions,
            head_indices,
            segment_blocks,
            dilation_rates,
        )
        scores = (
            jnp.einsum("qhd,khd->hqk", q_block, key_row_set, preferred_element_type=jnp.float32)
            * scaling
        )
        masked = jnp.where(counted > 0, scores, -1e30)
        row_max = jnp.max(masked, axis=2)
        part_lse = row_max + jnp.log(
            jnp.sum(counted * jnp.exp(masked - row_max[:, :, None]), axis=2)
        )
        top = jnp.maximum(part_lse, own_lse)
        log_norm = top + jnp.log(jnp.exp(part_lse - top) + jnp.exp(own_lse - top))
        prob_bf = (counted * jnp.exp(masked - log_norm[:, :, None])).astype(jnp.bfloat16)
        output = jnp.einsum(
            "hqk,khd->qhd", prob_bf, value_row_set, preferred_element_type=jnp.float32
        ).astype(jnp.bfloat16)
        return (output, log_norm)

    outputs, lse_blocks = lax.map(one_block, jnp.arange(blocks, dtype=jnp.int32))
    return (
        outputs.reshape(length_all, heads_here, head_size),
        jnp.transpose(lse_blocks, (0, 2, 1)).reshape(length_all, heads_here),
    )


def dilated_backward(
    query_row_set,
    key_row_set,
    value_row_set,
    grad_rows,
    log_norm,
    delta_row,
    head_indices,
    segment_blocks,
    dilation_rates,
):
    length_all, heads_here, head_size = query_row_set.shape
    rows_per_block = length_all
    blocks = length_all // rows_per_block
    scaling = 1.0 / math.sqrt(head_size)
    key_positions = packed_positions(0, length_all, head_indices)

    def step(carry, block_id):
        acc_k, acc_v = carry
        starting_row = block_id * rows_per_block
        q_block = lax.dynamic_slice_in_dim(query_row_set, starting_row, rows_per_block, 0)
        g_block = lax.dynamic_slice_in_dim(grad_rows, starting_row, rows_per_block, 0)
        lse_block = lax.dynamic_slice_in_dim(log_norm, starting_row, rows_per_block, 0).T
        delta_block = lax.dynamic_slice_in_dim(delta_row, starting_row, rows_per_block, 0).T
        counted = dilation_multiplier(
            packed_positions(starting_row, rows_per_block, head_indices),
            key_positions,
            head_indices,
            segment_blocks,
            dilation_rates,
        )
        scores = (
            jnp.einsum("qhd,khd->hqk", q_block, key_row_set, preferred_element_type=jnp.float32)
            * scaling
        )
        masked = jnp.where(counted > 0, scores, -1e30)
        prob_full = counted * jnp.exp(masked - lse_block[:, :, None])
        prob_bf = prob_full.astype(jnp.bfloat16)
        grad_prob = jnp.einsum(
            "qhd,khd->hqk", g_block, value_row_set, preferred_element_type=jnp.float32
        )
        grad_score = (prob_full * (grad_prob - delta_block[:, :, None])).astype(jnp.bfloat16)
        grad_q = (
            jnp.einsum("hqk,khd->qhd", grad_score, key_row_set, preferred_element_type=jnp.float32)
            * scaling
        ).astype(jnp.bfloat16)
        acc_k = acc_k + jnp.einsum(
            "hqk,qhd->khd", grad_score, q_block, preferred_element_type=jnp.float32
        )
        acc_v = acc_v + jnp.einsum(
            "hqk,qhd->khd", prob_bf, g_block, preferred_element_type=jnp.float32
        )
        return ((acc_k, acc_v), grad_q)

    zeros_all = jnp.zeros((length_all, heads_here, head_size), jnp.float32)
    (acc_k, acc_v), grad_q = lax.scan(
        step, (zeros_all, zeros_all), jnp.arange(blocks, dtype=jnp.int32)
    )
    return (
        grad_q.reshape(length_all, heads_here, head_size),
        (acc_k * scaling).astype(jnp.bfloat16),
        acc_v.astype(jnp.bfloat16),
    )


def dense_attention_forward(
    query_row_set, key_row_set, value_row_set, head_indices, segment_blocks, dilation_rates
):
    parity = head_indices % 2
    own_lse = local_lse(query_row_set, key_row_set)
    packed_out, packed_lse = sparse_attention_forward(
        pick_rows(query_row_set, parity),
        pick_rows(key_row_set, parity),
        pick_rows(value_row_set, parity),
        pick_rows(own_lse, parity),
        head_indices,
        segment_blocks,
        dilation_rates,
    )
    log_norm = spread_rows(packed_lse, parity, own_lse)
    attended = add_parts(
        local_output(query_row_set, key_row_set, value_row_set, log_norm), packed_out, parity
    )
    return (attended, log_norm)


def full_backward(
    query_row_set,
    key_row_set,
    value_row_set,
    attended,
    grad_attended,
    log_norm,
    head_indices,
    segment_blocks,
    dilation_rates,
):
    parity = head_indices % 2
    delta_row = jnp.sum(grad_attended.astype(jnp.float32) * attended.astype(jnp.float32), axis=2)
    local_parts = local_backward(
        query_row_set, key_row_set, value_row_set, grad_attended, log_norm, delta_row
    )
    packed_parts = dilated_backward(
        pick_rows(query_row_set, parity),
        pick_rows(key_row_set, parity),
        pick_rows(value_row_set, parity),
        pick_rows(grad_attended, parity),
        pick_rows(log_norm, parity),
        pick_rows(delta_row, parity),
        head_indices,
        segment_blocks,
        dilation_rates,
    )
    return tuple(
        (
            add_parts(first_branch, second, parity)
            for first_branch, second in zip(local_parts, packed_parts)
        )
    )


def head_major(array, groups):
    tokens, width = array.shape
    return jnp.swapaxes(array.reshape(tokens, groups, width // groups), 0, 1)


def token_major(array):
    groups, tokens, width = array.shape
    return jnp.swapaxes(array, 0, 1).reshape(1, tokens, groups * width)


def head_norm(values, cot_rows, gain, bias):
    feature_axes = (0, 2)
    mean_row = jnp.mean(values, axis=feature_axes, keepdims=True)
    var_row = jnp.mean(values * values, axis=feature_axes, keepdims=True) - mean_row * mean_row
    inv_std = lax.rsqrt(var_row + epsilon)
    centered = (values - mean_row) * inv_std
    normed = (centered * gain + bias).astype(jnp.bfloat16)
    grad_y = cot_rows.astype(jnp.float32)
    scaled = grad_y * gain
    grad_tokens = (
        inv_std
        * (
            scaled
            - jnp.mean(scaled, axis=feature_axes, keepdims=True)
            - centered * jnp.mean(scaled * centered, axis=feature_axes, keepdims=True)
        )
    ).astype(jnp.bfloat16)
    return (normed, grad_tokens, jnp.sum(grad_y * centered, axis=1), jnp.sum(grad_y, axis=1))


def shards(
    queries,
    key_state_matrix,
    value_state_matrix,
    cotangent,
    sublayer_norm_gain,
    sublayer_norm_bias,
    segment_blocks,
    dilation_rates,
):
    tokens_here = queries.shape[1]
    width_all = queries.shape[2]
    head_size = width_all // H
    ctx_count = lax.axis_size("ctx")
    heads_here = H // ctx_count
    width_here = width_all // ctx_count
    head_first = lax.axis_index("ctx") * heads_here
    head_indices = head_first + jnp.arange(heads_here, dtype=jnp.int32)
    loss_scale = 1.0 / math.sqrt(lax.axis_size("dp") * tokens_here * ctx_count)
    tokens_all = tokens_here * ctx_count

    def to_rows(array):
        return array.reshape(tokens_all, heads_here, head_size)

    stacked_in = jnp.stack(
        [
            head_major(queries[0], ctx_count),
            head_major(key_state_matrix[0], ctx_count),
            head_major(value_state_matrix[0], ctx_count),
        ]
    )
    stacked_in = lax.all_to_all(stacked_in, "ctx", split_axis=1, concat_axis=1, tiled=True)
    query_head_tensor, key_head_tensor, value_head_tensor = (
        to_rows(stacked_in[0]),
        to_rows(stacked_in[1]),
        to_rows(stacked_in[2]),
    )
    attended, log_norm = dense_attention_forward(
        query_head_tensor,
        key_head_tensor,
        value_head_tensor,
        head_indices,
        segment_blocks,
        dilation_rates,
    )
    attended_hm = lax.all_to_all(
        attended.reshape(ctx_count, tokens_here, width_here), "ctx", 0, 0, tiled=True
    )
    gain_hm = sublayer_norm_gain.reshape(ctx_count, 1, width_here)
    bias_hm = sublayer_norm_bias.reshape(ctx_count, 1, width_here)
    normed_hm, grad_hm, gain_part, bias_part = head_norm(
        attended_hm.astype(jnp.float32),
        head_major(cotangent[0], ctx_count),
        gain_hm,
        bias_hm,
    )
    normed = token_major(normed_hm)
    grad_attended = to_rows(lax.all_to_all(grad_hm, "ctx", 0, 0, tiled=True))
    both = jnp.stack([gain_part, bias_part], axis=1)
    both = jnp.sum(lax.all_to_all(both, "ctx", 0, 0, tiled=True), axis=0)
    dp_count = lax.axis_size("dp")
    both = jnp.broadcast_to(both[None], (dp_count,) + both.shape)
    both = jnp.sum(lax.all_to_all(both, "dp", 0, 0, tiled=True), axis=0)
    grad_gain, grad_bias = both[0], both[1]
    grad_q, grad_k, grad_v = full_backward(
        query_head_tensor,
        key_head_tensor,
        value_head_tensor,
        attended,
        grad_attended,
        log_norm,
        head_indices,
        segment_blocks,
        dilation_rates,
    )
    stacked_out = lax.all_to_all(
        jnp.stack([part.reshape(ctx_count, tokens_here, width_here) for part in (grad_q, grad_k, grad_v)]),
        "ctx",
        split_axis=1,
        concat_axis=1,
        tiled=True,
    )
    return (
        normed,
        token_major(stacked_out[0]),
        token_major(stacked_out[1]),
        token_major(stacked_out[2]),
        grad_gain * loss_scale,
        grad_bias * loss_scale,
    )


def solution(mesh):
    return jax.shard_map(
        shards,
        mesh=mesh,
        in_specs=(
            P("dp", "ctx", None),
            P("dp", "ctx", None),
            P("dp", "ctx", None),
            P("dp", "ctx", None),
            P(),
            P(),
            P(),
            P(),
        ),
        out_specs=(
            P("dp", "ctx", None),
            P("dp", "ctx", None),
            P("dp", "ctx", None),
            P("dp", "ctx", None),
            P("ctx"),
            P("ctx"),
        ),
        check_vma=False,
    )
```

```python
import math

import jax
import jax.numpy as jnp
from jax import lax
from jax.experimental import pallas as pl
from jax.experimental.pallas import tpu as pltpu
from jax.sharding import PartitionSpec as P

H = 16
BLK = 128
G = 4


epsilon = 1e-05


def pick_rows(array, parity):
    pairs = array.reshape((array.shape[0] // 2, 2) + array.shape[1:])
    cond = (parity == 0).reshape((-1,) + (1,) * (array.ndim - 2))
    return jnp.where(cond, pairs[:, 0], pairs[:, 1])


def spread_rows(packed, parity, base):
    pairs = base.reshape((base.shape[0] // 2, 2) + base.shape[1:])
    cond = (parity == 0).reshape((-1,) + (1,) * (base.ndim - 2))
    first_branch = jnp.where(cond, packed, pairs[:, 0])
    second = jnp.where(cond, pairs[:, 1], packed)
    return jnp.stack([first_branch, second], axis=1).reshape(base.shape)


def add_parts(full_part, packed_part, parity):
    spread = spread_rows(packed_part, parity, jnp.zeros_like(full_part))
    full_part = lax.optimization_barrier(full_part)
    spread = lax.optimization_barrier(spread)
    return (full_part.astype(jnp.float32) + spread.astype(jnp.float32)).astype(jnp.bfloat16)


def block_view(array):
    return array.reshape((array.shape[0] // BLK, BLK) + array.shape[1:])


def lse_view(log_norm):
    return jnp.transpose(block_view(log_norm), (0, 2, 1))


def local_scores(query_row_set, key_row_set):
    scaling = 1.0 / math.sqrt(query_row_set.shape[-1])
    return (
        jnp.einsum(
            "bqhd,bkhd->bhqk",
            block_view(query_row_set),
            block_view(key_row_set),
            preferred_element_type=jnp.float32,
        )
        * scaling
    )


def local_lse(query_row_set, key_row_set):
    scores = local_scores(query_row_set, key_row_set)
    row_max = jnp.max(scores, axis=3)
    total = row_max + jnp.log(jnp.sum(jnp.exp(scores - row_max[..., None]), axis=3))
    return jnp.transpose(total, (0, 2, 1)).reshape(query_row_set.shape[0], query_row_set.shape[1])


def local_output(query_row_set, key_row_set, value_row_set, log_norm):
    scores = local_scores(query_row_set, key_row_set)
    prob_bf = jnp.exp(scores - lse_view(log_norm)[..., None]).astype(jnp.bfloat16)
    output = jnp.einsum(
        "bhqk,bkhd->bqhd", prob_bf, block_view(value_row_set), preferred_element_type=jnp.float32
    )
    return output.astype(jnp.bfloat16).reshape(query_row_set.shape)


def local_backward(query_row_set, key_row_set, value_row_set, grad_rows, log_norm, delta_row):
    scaling = 1.0 / math.sqrt(query_row_set.shape[-1])
    scores = local_scores(query_row_set, key_row_set)
    prob_full = jnp.exp(scores - lse_view(log_norm)[..., None])
    prob_bf = prob_full.astype(jnp.bfloat16)
    grad_prob = jnp.einsum(
        "bqhd,bkhd->bhqk",
        block_view(grad_rows),
        block_view(value_row_set),
        preferred_element_type=jnp.float32,
    )
    grad_score = (prob_full * (grad_prob - lse_view(delta_row)[..., None])).astype(jnp.bfloat16)
    grad_q = jnp.einsum(
        "bhqk,bkhd->bqhd", grad_score, block_view(key_row_set), preferred_element_type=jnp.float32
    )
    grad_k = jnp.einsum(
        "bhqk,bqhd->bkhd", grad_score, block_view(query_row_set), preferred_element_type=jnp.float32
    )
    grad_v = jnp.einsum(
        "bhqk,bqhd->bkhd", prob_bf, block_view(grad_rows), preferred_element_type=jnp.float32
    )
    shape = query_row_set.shape
    return (
        (grad_q * scaling).astype(jnp.bfloat16).reshape(shape),
        (grad_k * scaling).astype(jnp.bfloat16).reshape(shape),
        grad_v.astype(jnp.bfloat16).reshape(shape),
    )


def packed_positions(start, count, head_indices):
    rows = start + jnp.arange(count, dtype=jnp.int32)
    return 2 * rows[None, :] + (head_indices % 2)[:, None]


def dilation_multiplier(
    query_positions, key_positions, head_indices, segment_blocks, dilation_rates
):
    counted = jnp.zeros(
        (head_indices.shape[0], query_positions.shape[1], key_positions.shape[1]), jnp.float32
    )
    for dilation_branch in range(1, G):
        seg_width = segment_blocks[dilation_branch] * BLK
        low_bits = dilation_rates[dilation_branch] - 1
        same_seg = (query_positions[:, :, None] ^ key_positions[:, None, :]) < seg_width
        selected_queries = ((query_positions ^ head_indices[:, None]) & low_bits) == 0
        selected_keys = ((key_positions ^ head_indices[:, None]) & low_bits) == 0
        counted = counted + (
            same_seg & selected_queries[:, :, None] & selected_keys[:, None, :]
        ).astype(jnp.float32)
    return counted


def dilated_mask(params_ref, rows, keys, row_first):
    head = params_ref[2 * G]
    parity = params_ref[2 * G + 1]
    query_positions = 2 * (row_first + lax.broadcasted_iota(jnp.int32, (rows, keys), 0)) + parity
    key_positions = 2 * lax.broadcasted_iota(jnp.int32, (rows, keys), 1) + parity
    apart = query_positions ^ key_positions
    query_phase = query_positions ^ head
    key_phase = key_positions ^ head
    counted = jnp.zeros((rows, keys), jnp.float32)
    for branch in range(1, G):
        low_bits = params_ref[G + branch]
        kept = (
            (apart < params_ref[branch])
            & ((query_phase & low_bits) == 0)
            & ((key_phase & low_bits) == 0)
        )
        counted = counted + jnp.where(kept, 1.0, 0.0)
    return counted


def dilated_forward_kernel(params_ref, q_ref, k_ref, v_ref, own_ref, out_ref, lse_ref):
    rows, head_size = q_ref.shape
    keys = k_ref.shape[0]
    scaling = 1.0 / math.sqrt(head_size)
    counted = dilated_mask(params_ref, rows, keys, pl.program_id(0) * rows)
    scores = (
        lax.dot_general(
            q_ref[...], k_ref[...], (((1,), (1,)), ((), ())), preferred_element_type=jnp.float32
        )
        * scaling
    )
    masked = jnp.where(counted > 0, scores, -1e30)
    row_max = jnp.max(masked, axis=1, keepdims=True)
    part_lse = row_max + jnp.log(
        jnp.sum(counted * jnp.exp(masked - row_max), axis=1, keepdims=True)
    )
    own_lse = own_ref[...]
    top = jnp.maximum(part_lse, own_lse)
    log_norm = top + jnp.log(jnp.exp(part_lse - top) + jnp.exp(own_lse - top))
    prob_bf = (counted * jnp.exp(masked - log_norm)).astype(jnp.bfloat16)
    out_ref[...] = jnp.dot(prob_bf, v_ref[...], preferred_element_type=jnp.float32).astype(
        out_ref.dtype
    )
    lse_ref[...] = log_norm


def mask_params(head, segment_blocks, dilation_rates):
    return jnp.concatenate(
        [
            segment_blocks.astype(jnp.int32) * BLK,
            dilation_rates.astype(jnp.int32) - 1,
            jnp.stack([head, head % 2]).astype(jnp.int32),
        ]
    )


def dilated_forward_call(params, q, k, v, own, row_block=256):
    rows, head_size = q.shape
    keys = k.shape[0]
    grid = (rows // row_block,)
    return pl.pallas_call(
        dilated_forward_kernel,
        grid=grid,
        in_specs=[
            pl.BlockSpec(memory_space=pltpu.SMEM),
            pl.BlockSpec((row_block, head_size), lambda i: (i, 0)),
            pl.BlockSpec((keys, head_size), lambda i: (0, 0)),
            pl.BlockSpec((keys, head_size), lambda i: (0, 0)),
            pl.BlockSpec((row_block, 1), lambda i: (i, 0)),
        ],
        out_specs=[
            pl.BlockSpec((row_block, head_size), lambda i: (i, 0)),
            pl.BlockSpec((row_block, 1), lambda i: (i, 0)),
        ],
        out_shape=[
            jax.ShapeDtypeStruct((rows, head_size), jnp.bfloat16),
            jax.ShapeDtypeStruct((rows, 1), jnp.float32),
        ],
        cost_estimate=pl.CostEstimate(
            flops=4 * rows * keys * head_size,
            transcendentals=rows * keys,
            bytes_accessed=2 * (3 * rows * head_size + rows * head_size) + 8 * rows,
        ),
    )(params, q, k, v, own)


def sparse_attention_forward(
    query_row_set,
    key_row_set,
    value_row_set,
    baseline_logsumexp,
    head_indices,
    segment_blocks,
    dilation_rates,
):
    length_all, heads_here, head_size = query_row_set.shape
    rows_per_block = length_all
    blocks = length_all // rows_per_block
    scaling = 1.0 / math.sqrt(head_size)
    key_positions = packed_positions(0, length_all, head_indices)

    def one_block(block_id):
        starting_row = block_id * rows_per_block
        q_block = lax.dynamic_slice_in_dim(query_row_set, starting_row, rows_per_block, 0)
        own_lse = lax.dynamic_slice_in_dim(baseline_logsumexp, starting_row, rows_per_block, 0).T
        counted = dilation_multiplier(
            packed_positions(starting_row, rows_per_block, head_indices),
            key_positions,
            head_indices,
            segment_blocks,
            dilation_rates,
        )
        scores = (
            jnp.einsum("qhd,khd->hqk", q_block, key_row_set, preferred_element_type=jnp.float32)
            * scaling
        )
        masked = jnp.where(counted > 0, scores, -1e30)
        row_max = jnp.max(masked, axis=2)
        part_lse = row_max + jnp.log(
            jnp.sum(counted * jnp.exp(masked - row_max[:, :, None]), axis=2)
        )
        top = jnp.maximum(part_lse, own_lse)
        log_norm = top + jnp.log(jnp.exp(part_lse - top) + jnp.exp(own_lse - top))
        prob_bf = (counted * jnp.exp(masked - log_norm[:, :, None])).astype(jnp.bfloat16)
        output = jnp.einsum(
            "hqk,khd->qhd", prob_bf, value_row_set, preferred_element_type=jnp.float32
        ).astype(jnp.bfloat16)
        return (output, log_norm)

    outputs, lse_blocks = lax.map(one_block, jnp.arange(blocks, dtype=jnp.int32))
    return (
        outputs.reshape(length_all, heads_here, head_size),
        jnp.transpose(lse_blocks, (0, 2, 1)).reshape(length_all, heads_here),
    )


def dilated_backward(
    query_row_set,
    key_row_set,
    value_row_set,
    grad_rows,
    log_norm,
    delta_row,
    head_indices,
    segment_blocks,
    dilation_rates,
):
    length_all, heads_here, head_size = query_row_set.shape
    rows_per_block = length_all
    blocks = length_all // rows_per_block
    scaling = 1.0 / math.sqrt(head_size)
    key_positions = packed_positions(0, length_all, head_indices)

    def step(carry, block_id):
        acc_k, acc_v = carry
        starting_row = block_id * rows_per_block
        q_block = lax.dynamic_slice_in_dim(query_row_set, starting_row, rows_per_block, 0)
        g_block = lax.dynamic_slice_in_dim(grad_rows, starting_row, rows_per_block, 0)
        lse_block = lax.dynamic_slice_in_dim(log_norm, starting_row, rows_per_block, 0).T
        delta_block = lax.dynamic_slice_in_dim(delta_row, starting_row, rows_per_block, 0).T
        counted = dilation_multiplier(
            packed_positions(starting_row, rows_per_block, head_indices),
            key_positions,
            head_indices,
            segment_blocks,
            dilation_rates,
        )
        scores = (
            jnp.einsum("qhd,khd->hqk", q_block, key_row_set, preferred_element_type=jnp.float32)
            * scaling
        )
        masked = jnp.where(counted > 0, scores, -1e30)
        prob_full = counted * jnp.exp(masked - lse_block[:, :, None])
        prob_bf = prob_full.astype(jnp.bfloat16)
        grad_prob = jnp.einsum(
            "qhd,khd->hqk", g_block, value_row_set, preferred_element_type=jnp.float32
        )
        grad_score = (prob_full * (grad_prob - delta_block[:, :, None])).astype(jnp.bfloat16)
        grad_q = (
            jnp.einsum("hqk,khd->qhd", grad_score, key_row_set, preferred_element_type=jnp.float32)
            * scaling
        ).astype(jnp.bfloat16)
        acc_k = acc_k + jnp.einsum(
            "hqk,qhd->khd", grad_score, q_block, preferred_element_type=jnp.float32
        )
        acc_v = acc_v + jnp.einsum(
            "hqk,qhd->khd", prob_bf, g_block, preferred_element_type=jnp.float32
        )
        return ((acc_k, acc_v), grad_q)

    zeros_all = jnp.zeros((length_all, heads_here, head_size), jnp.float32)
    (acc_k, acc_v), grad_q = lax.scan(
        step, (zeros_all, zeros_all), jnp.arange(blocks, dtype=jnp.int32)
    )
    return (
        grad_q.reshape(length_all, heads_here, head_size),
        (acc_k * scaling).astype(jnp.bfloat16),
        acc_v.astype(jnp.bfloat16),
    )


def dense_attention_forward(
    query_row_set, key_row_set, value_row_set, head_indices, segment_blocks, dilation_rates
):
    parity = head_indices % 2
    own_lse = local_lse(query_row_set, key_row_set)
    if query_row_set.shape[1] == 1:
        params = mask_params(head_indices[0], segment_blocks, dilation_rates)
        packed_out, packed_lse = dilated_forward_call(
            params,
            pick_rows(query_row_set, parity)[:, 0],
            pick_rows(key_row_set, parity)[:, 0],
            pick_rows(value_row_set, parity)[:, 0],
            pick_rows(own_lse, parity),
        )
        packed_out = packed_out[:, None]
    else:
        packed_out, packed_lse = sparse_attention_forward(
            pick_rows(query_row_set, parity),
            pick_rows(key_row_set, parity),
            pick_rows(value_row_set, parity),
            pick_rows(own_lse, parity),
            head_indices,
            segment_blocks,
            dilation_rates,
        )
    log_norm = spread_rows(packed_lse, parity, own_lse)
    attended = add_parts(
        local_output(query_row_set, key_row_set, value_row_set, log_norm), packed_out, parity
    )
    return (attended, log_norm)


def full_backward(
    query_row_set,
    key_row_set,
    value_row_set,
    attended,
    grad_attended,
    log_norm,
    head_indices,
    segment_blocks,
    dilation_rates,
):
    parity = head_indices % 2
    delta_row = jnp.sum(grad_attended.astype(jnp.float32) * attended.astype(jnp.float32), axis=2)
    local_parts = local_backward(
        query_row_set, key_row_set, value_row_set, grad_attended, log_norm, delta_row
    )
    packed_parts = dilated_backward(
        pick_rows(query_row_set, parity),
        pick_rows(key_row_set, parity),
        pick_rows(value_row_set, parity),
        pick_rows(grad_attended, parity),
        pick_rows(log_norm, parity),
        pick_rows(delta_row, parity),
        head_indices,
        segment_blocks,
        dilation_rates,
    )
    return tuple(
        (
            add_parts(first_branch, second, parity)
            for first_branch, second in zip(local_parts, packed_parts)
        )
    )


def head_major(array, groups):
    tokens, width = array.shape
    return jnp.swapaxes(array.reshape(tokens, groups, width // groups), 0, 1)


def token_major(array):
    groups, tokens, width = array.shape
    return jnp.swapaxes(array, 0, 1).reshape(1, tokens, groups * width)


def head_norm(values, cot_rows, gain, bias):
    feature_axes = (0, 2)
    mean_row = jnp.mean(values, axis=feature_axes, keepdims=True)
    var_row = jnp.mean(values * values, axis=feature_axes, keepdims=True) - mean_row * mean_row
    inv_std = lax.rsqrt(var_row + epsilon)
    centered = (values - mean_row) * inv_std
    normed = (centered * gain + bias).astype(jnp.bfloat16)
    grad_y = cot_rows.astype(jnp.float32)
    scaled = grad_y * gain
    grad_tokens = (
        inv_std
        * (
            scaled
            - jnp.mean(scaled, axis=feature_axes, keepdims=True)
            - centered * jnp.mean(scaled * centered, axis=feature_axes, keepdims=True)
        )
    ).astype(jnp.bfloat16)
    return (normed, grad_tokens, jnp.sum(grad_y * centered, axis=1), jnp.sum(grad_y, axis=1))


def shards(
    queries,
    key_state_matrix,
    value_state_matrix,
    cotangent,
    sublayer_norm_gain,
    sublayer_norm_bias,
    segment_blocks,
    dilation_rates,
):
    tokens_here = queries.shape[1]
    width_all = queries.shape[2]
    head_size = width_all // H
    ctx_count = lax.axis_size("ctx")
    heads_here = H // ctx_count
    width_here = width_all // ctx_count
    head_first = lax.axis_index("ctx") * heads_here
    head_indices = head_first + jnp.arange(heads_here, dtype=jnp.int32)
    loss_scale = 1.0 / math.sqrt(lax.axis_size("dp") * tokens_here * ctx_count)
    tokens_all = tokens_here * ctx_count

    def to_rows(array):
        return array.reshape(tokens_all, heads_here, head_size)

    stacked_in = jnp.stack(
        [
            head_major(queries[0], ctx_count),
            head_major(key_state_matrix[0], ctx_count),
            head_major(value_state_matrix[0], ctx_count),
        ]
    )
    stacked_in = lax.all_to_all(stacked_in, "ctx", split_axis=1, concat_axis=1, tiled=True)
    query_head_tensor, key_head_tensor, value_head_tensor = (
        to_rows(stacked_in[0]),
        to_rows(stacked_in[1]),
        to_rows(stacked_in[2]),
    )
    attended, log_norm = dense_attention_forward(
        query_head_tensor,
        key_head_tensor,
        value_head_tensor,
        head_indices,
        segment_blocks,
        dilation_rates,
    )
    attended_hm = lax.all_to_all(
        attended.reshape(ctx_count, tokens_here, width_here), "ctx", 0, 0, tiled=True
    )
    gain_hm = sublayer_norm_gain.reshape(ctx_count, 1, width_here)
    bias_hm = sublayer_norm_bias.reshape(ctx_count, 1, width_here)
    normed_hm, grad_hm, gain_part, bias_part = head_norm(
        attended_hm.astype(jnp.float32),
        head_major(cotangent[0], ctx_count),
        gain_hm,
        bias_hm,
    )
    normed = token_major(normed_hm)
    grad_attended = to_rows(lax.all_to_all(grad_hm, "ctx", 0, 0, tiled=True))
    both = jnp.stack([gain_part, bias_part], axis=1)
    both = jnp.sum(lax.all_to_all(both, "ctx", 0, 0, tiled=True), axis=0)
    dp_count = lax.axis_size("dp")
    both = jnp.broadcast_to(both[None], (dp_count,) + both.shape)
    both = jnp.sum(lax.all_to_all(both, "dp", 0, 0, tiled=True), axis=0)
    grad_gain, grad_bias = both[0], both[1]
    grad_q, grad_k, grad_v = full_backward(
        query_head_tensor,
        key_head_tensor,
        value_head_tensor,
        attended,
        grad_attended,
        log_norm,
        head_indices,
        segment_blocks,
        dilation_rates,
    )
    stacked_out = lax.all_to_all(
        jnp.stack([part.reshape(ctx_count, tokens_here, width_here) for part in (grad_q, grad_k, grad_v)]),
        "ctx",
        split_axis=1,
        concat_axis=1,
        tiled=True,
    )
    return (
        normed,
        token_major(stacked_out[0]),
        token_major(stacked_out[1]),
        token_major(stacked_out[2]),
        grad_gain * loss_scale,
        grad_bias * loss_scale,
    )


def solution(mesh):
    return jax.shard_map(
        shards,
        mesh=mesh,
        in_specs=(
            P("dp", "ctx", None),
            P("dp", "ctx", None),
            P("dp", "ctx", None),
            P("dp", "ctx", None),
            P(),
            P(),
            P(),
            P(),
        ),
        out_specs=(
            P("dp", "ctx", None),
            P("dp", "ctx", None),
            P("dp", "ctx", None),
            P("dp", "ctx", None),
            P("ctx"),
            P("ctx"),
        ),
        check_vma=False,
    )
```

```python
import math

import jax
import jax.numpy as jnp
from jax import lax
from jax.experimental import pallas as pl
from jax.experimental.pallas import tpu as pltpu
from jax.sharding import PartitionSpec as P

H = 16
BLK = 128
G = 4


epsilon = 1e-05


def pick_rows(array, parity):
    pairs = array.reshape((array.shape[0] // 2, 2) + array.shape[1:])
    cond = (parity == 0).reshape((-1,) + (1,) * (array.ndim - 2))
    return jnp.where(cond, pairs[:, 0], pairs[:, 1])


def spread_rows(packed, parity, base):
    pairs = base.reshape((base.shape[0] // 2, 2) + base.shape[1:])
    cond = (parity == 0).reshape((-1,) + (1,) * (base.ndim - 2))
    first_branch = jnp.where(cond, packed, pairs[:, 0])
    second = jnp.where(cond, pairs[:, 1], packed)
    return jnp.stack([first_branch, second], axis=1).reshape(base.shape)


def add_parts(full_part, packed_part, parity):
    spread = spread_rows(packed_part, parity, jnp.zeros_like(full_part))
    full_part = lax.optimization_barrier(full_part)
    spread = lax.optimization_barrier(spread)
    return (full_part.astype(jnp.float32) + spread.astype(jnp.float32)).astype(jnp.bfloat16)


def block_view(array):
    return array.reshape((array.shape[0] // BLK, BLK) + array.shape[1:])


def lse_view(log_norm):
    return jnp.transpose(block_view(log_norm), (0, 2, 1))


def local_scores(query_row_set, key_row_set):
    scaling = 1.0 / math.sqrt(query_row_set.shape[-1])
    return (
        jnp.einsum(
            "bqhd,bkhd->bhqk",
            block_view(query_row_set),
            block_view(key_row_set),
            preferred_element_type=jnp.float32,
        )
        * scaling
    )


def local_lse(query_row_set, key_row_set):
    scores = local_scores(query_row_set, key_row_set)
    row_max = jnp.max(scores, axis=3)
    total = row_max + jnp.log(jnp.sum(jnp.exp(scores - row_max[..., None]), axis=3))
    return jnp.transpose(total, (0, 2, 1)).reshape(query_row_set.shape[0], query_row_set.shape[1])


def local_output(query_row_set, key_row_set, value_row_set, log_norm):
    scores = local_scores(query_row_set, key_row_set)
    prob_bf = jnp.exp(scores - lse_view(log_norm)[..., None]).astype(jnp.bfloat16)
    output = jnp.einsum(
        "bhqk,bkhd->bqhd", prob_bf, block_view(value_row_set), preferred_element_type=jnp.float32
    )
    return output.astype(jnp.bfloat16).reshape(query_row_set.shape)


def local_backward(query_row_set, key_row_set, value_row_set, grad_rows, log_norm, delta_row):
    scaling = 1.0 / math.sqrt(query_row_set.shape[-1])
    scores = local_scores(query_row_set, key_row_set)
    prob_full = jnp.exp(scores - lse_view(log_norm)[..., None])
    prob_bf = prob_full.astype(jnp.bfloat16)
    grad_prob = jnp.einsum(
        "bqhd,bkhd->bhqk",
        block_view(grad_rows),
        block_view(value_row_set),
        preferred_element_type=jnp.float32,
    )
    grad_score = (prob_full * (grad_prob - lse_view(delta_row)[..., None])).astype(jnp.bfloat16)
    grad_q = jnp.einsum(
        "bhqk,bkhd->bqhd", grad_score, block_view(key_row_set), preferred_element_type=jnp.float32
    )
    grad_k = jnp.einsum(
        "bhqk,bqhd->bkhd", grad_score, block_view(query_row_set), preferred_element_type=jnp.float32
    )
    grad_v = jnp.einsum(
        "bhqk,bqhd->bkhd", prob_bf, block_view(grad_rows), preferred_element_type=jnp.float32
    )
    shape = query_row_set.shape
    return (
        (grad_q * scaling).astype(jnp.bfloat16).reshape(shape),
        (grad_k * scaling).astype(jnp.bfloat16).reshape(shape),
        grad_v.astype(jnp.bfloat16).reshape(shape),
    )


def packed_positions(start, count, head_indices):
    rows = start + jnp.arange(count, dtype=jnp.int32)
    return 2 * rows[None, :] + (head_indices % 2)[:, None]


def dilation_multiplier(
    query_positions, key_positions, head_indices, segment_blocks, dilation_rates
):
    counted = jnp.zeros(
        (head_indices.shape[0], query_positions.shape[1], key_positions.shape[1]), jnp.float32
    )
    for dilation_branch in range(1, G):
        seg_width = segment_blocks[dilation_branch] * BLK
        low_bits = dilation_rates[dilation_branch] - 1
        same_seg = (query_positions[:, :, None] ^ key_positions[:, None, :]) < seg_width
        selected_queries = ((query_positions ^ head_indices[:, None]) & low_bits) == 0
        selected_keys = ((key_positions ^ head_indices[:, None]) & low_bits) == 0
        counted = counted + (
            same_seg & selected_queries[:, :, None] & selected_keys[:, None, :]
        ).astype(jnp.float32)
    return counted


def dilated_mask(params_ref, rows, keys, row_first):
    head = params_ref[2 * G]
    parity = params_ref[2 * G + 1]
    query_positions = 2 * (row_first + lax.broadcasted_iota(jnp.int32, (rows, keys), 0)) + parity
    key_positions = 2 * lax.broadcasted_iota(jnp.int32, (rows, keys), 1) + parity
    apart = query_positions ^ key_positions
    query_phase = query_positions ^ head
    key_phase = key_positions ^ head
    counted = jnp.zeros((rows, keys), jnp.float32)
    for branch in range(1, G):
        low_bits = params_ref[G + branch]
        kept = (
            (apart < params_ref[branch])
            & ((query_phase & low_bits) == 0)
            & ((key_phase & low_bits) == 0)
        )
        counted = counted + jnp.where(kept, 1.0, 0.0)
    return counted


def dilated_forward_kernel(params_ref, q_ref, k_ref, v_ref, own_ref, out_ref, lse_ref):
    rows, head_size = q_ref.shape
    keys = k_ref.shape[0]
    scaling = 1.0 / math.sqrt(head_size)
    counted = dilated_mask(params_ref, rows, keys, pl.program_id(0) * rows)
    scores = (
        lax.dot_general(
            q_ref[...], k_ref[...], (((1,), (1,)), ((), ())), preferred_element_type=jnp.float32
        )
        * scaling
    )
    masked = jnp.where(counted > 0, scores, -1e30)
    row_max = jnp.max(masked, axis=1, keepdims=True)
    part_lse = row_max + jnp.log(
        jnp.sum(counted * jnp.exp(masked - row_max), axis=1, keepdims=True)
    )
    own_lse = own_ref[...]
    top = jnp.maximum(part_lse, own_lse)
    log_norm = top + jnp.log(jnp.exp(part_lse - top) + jnp.exp(own_lse - top))
    prob_bf = (counted * jnp.exp(masked - log_norm)).astype(jnp.bfloat16)
    out_ref[...] = jnp.dot(prob_bf, v_ref[...], preferred_element_type=jnp.float32).astype(
        out_ref.dtype
    )
    lse_ref[...] = log_norm


def mask_params(head, segment_blocks, dilation_rates):
    return jnp.concatenate(
        [
            segment_blocks.astype(jnp.int32) * BLK,
            dilation_rates.astype(jnp.int32) - 1,
            jnp.stack([head, head % 2]).astype(jnp.int32),
        ]
    )


def dilated_forward_call(params, q, k, v, own, row_block=256):
    rows, head_size = q.shape
    keys = k.shape[0]
    grid = (rows // row_block,)
    return pl.pallas_call(
        dilated_forward_kernel,
        grid=grid,
        in_specs=[
            pl.BlockSpec(memory_space=pltpu.SMEM),
            pl.BlockSpec((row_block, head_size), lambda i: (i, 0)),
            pl.BlockSpec((keys, head_size), lambda i: (0, 0)),
            pl.BlockSpec((keys, head_size), lambda i: (0, 0)),
            pl.BlockSpec((row_block, 1), lambda i: (i, 0)),
        ],
        out_specs=[
            pl.BlockSpec((row_block, head_size), lambda i: (i, 0)),
            pl.BlockSpec((row_block, 1), lambda i: (i, 0)),
        ],
        out_shape=[
            jax.ShapeDtypeStruct((rows, head_size), jnp.bfloat16),
            jax.ShapeDtypeStruct((rows, 1), jnp.float32),
        ],
        cost_estimate=pl.CostEstimate(
            flops=4 * rows * keys * head_size,
            transcendentals=rows * keys,
            bytes_accessed=2 * (3 * rows * head_size + rows * head_size) + 8 * rows,
        ),
    )(params, q, k, v, own)


def dilated_backward_kernel(
    params_ref, q_ref, k_ref, v_ref, g_ref, lse_ref, delta_ref, dq_ref, dk_ref, dv_ref, dk_acc, dv_acc
):
    rows, head_size = q_ref.shape
    keys = k_ref.shape[0]
    step = pl.program_id(0)
    scaling = 1.0 / math.sqrt(head_size)

    @pl.when(step == 0)
    def _():
        dk_acc[...] = jnp.zeros_like(dk_acc)
        dv_acc[...] = jnp.zeros_like(dv_acc)

    counted = dilated_mask(params_ref, rows, keys, step * rows)
    q_block = q_ref[...]
    g_block = g_ref[...]
    scores = (
        lax.dot_general(
            q_block, k_ref[...], (((1,), (1,)), ((), ())), preferred_element_type=jnp.float32
        )
        * scaling
    )
    masked = jnp.where(counted > 0, scores, -1e30)
    prob_full = counted * jnp.exp(masked - lse_ref[...])
    grad_prob = lax.dot_general(
        g_block, v_ref[...], (((1,), (1,)), ((), ())), preferred_element_type=jnp.float32
    )
    grad_score = (prob_full * (grad_prob - delta_ref[...])).astype(jnp.bfloat16)
    dq_ref[...] = (
        jnp.dot(grad_score, k_ref[...], preferred_element_type=jnp.float32) * scaling
    ).astype(dq_ref.dtype)
    dk_acc[...] += lax.dot_general(
        grad_score, q_block, (((0,), (0,)), ((), ())), preferred_element_type=jnp.float32
    )
    dv_acc[...] += lax.dot_general(
        prob_full.astype(jnp.bfloat16),
        g_block,
        (((0,), (0,)), ((), ())),
        preferred_element_type=jnp.float32,
    )

    @pl.when(step == pl.num_programs(0) - 1)
    def _():
        dk_ref[...] = (dk_acc[...] * scaling).astype(dk_ref.dtype)
        dv_ref[...] = dv_acc[...].astype(dv_ref.dtype)


def dilated_backward_call(params, q, k, v, g, lse, delta, row_block=256):
    rows, head_size = q.shape
    keys = k.shape[0]
    row_spec = pl.BlockSpec((row_block, head_size), lambda i: (i, 0))
    full_spec = pl.BlockSpec((keys, head_size), lambda i: (0, 0))
    column_spec = pl.BlockSpec((row_block, 1), lambda i: (i, 0))
    return pl.pallas_call(
        dilated_backward_kernel,
        grid=(rows // row_block,),
        in_specs=[
            pl.BlockSpec(memory_space=pltpu.SMEM),
            row_spec,
            full_spec,
            full_spec,
            row_spec,
            column_spec,
            column_spec,
        ],
        out_specs=[row_spec, full_spec, full_spec],
        out_shape=[jax.ShapeDtypeStruct((rows, head_size), jnp.bfloat16)] * 3,
        scratch_shapes=[
            pltpu.VMEM((keys, head_size), jnp.float32),
            pltpu.VMEM((keys, head_size), jnp.float32),
        ],
        compiler_params=pltpu.CompilerParams(dimension_semantics=("arbitrary",)),
        cost_estimate=pl.CostEstimate(
            flops=10 * rows * keys * head_size,
            transcendentals=rows * keys,
            bytes_accessed=2 * 8 * rows * head_size + 8 * rows,
        ),
    )(params, q, k, v, g, lse, delta)


def sparse_attention_forward(
    query_row_set,
    key_row_set,
    value_row_set,
    baseline_logsumexp,
    head_indices,
    segment_blocks,
    dilation_rates,
):
    length_all, heads_here, head_size = query_row_set.shape
    rows_per_block = length_all
    blocks = length_all // rows_per_block
    scaling = 1.0 / math.sqrt(head_size)
    key_positions = packed_positions(0, length_all, head_indices)

    def one_block(block_id):
        starting_row = block_id * rows_per_block
        q_block = lax.dynamic_slice_in_dim(query_row_set, starting_row, rows_per_block, 0)
        own_lse = lax.dynamic_slice_in_dim(baseline_logsumexp, starting_row, rows_per_block, 0).T
        counted = dilation_multiplier(
            packed_positions(starting_row, rows_per_block, head_indices),
            key_positions,
            head_indices,
            segment_blocks,
            dilation_rates,
        )
        scores = (
            jnp.einsum("qhd,khd->hqk", q_block, key_row_set, preferred_element_type=jnp.float32)
            * scaling
        )
        masked = jnp.where(counted > 0, scores, -1e30)
        row_max = jnp.max(masked, axis=2)
        part_lse = row_max + jnp.log(
            jnp.sum(counted * jnp.exp(masked - row_max[:, :, None]), axis=2)
        )
        top = jnp.maximum(part_lse, own_lse)
        log_norm = top + jnp.log(jnp.exp(part_lse - top) + jnp.exp(own_lse - top))
        prob_bf = (counted * jnp.exp(masked - log_norm[:, :, None])).astype(jnp.bfloat16)
        output = jnp.einsum(
            "hqk,khd->qhd", prob_bf, value_row_set, preferred_element_type=jnp.float32
        ).astype(jnp.bfloat16)
        return (output, log_norm)

    outputs, lse_blocks = lax.map(one_block, jnp.arange(blocks, dtype=jnp.int32))
    return (
        outputs.reshape(length_all, heads_here, head_size),
        jnp.transpose(lse_blocks, (0, 2, 1)).reshape(length_all, heads_here),
    )


def dilated_backward(
    query_row_set,
    key_row_set,
    value_row_set,
    grad_rows,
    log_norm,
    delta_row,
    head_indices,
    segment_blocks,
    dilation_rates,
):
    length_all, heads_here, head_size = query_row_set.shape
    rows_per_block = length_all
    blocks = length_all // rows_per_block
    scaling = 1.0 / math.sqrt(head_size)
    key_positions = packed_positions(0, length_all, head_indices)

    def step(carry, block_id):
        acc_k, acc_v = carry
        starting_row = block_id * rows_per_block
        q_block = lax.dynamic_slice_in_dim(query_row_set, starting_row, rows_per_block, 0)
        g_block = lax.dynamic_slice_in_dim(grad_rows, starting_row, rows_per_block, 0)
        lse_block = lax.dynamic_slice_in_dim(log_norm, starting_row, rows_per_block, 0).T
        delta_block = lax.dynamic_slice_in_dim(delta_row, starting_row, rows_per_block, 0).T
        counted = dilation_multiplier(
            packed_positions(starting_row, rows_per_block, head_indices),
            key_positions,
            head_indices,
            segment_blocks,
            dilation_rates,
        )
        scores = (
            jnp.einsum("qhd,khd->hqk", q_block, key_row_set, preferred_element_type=jnp.float32)
            * scaling
        )
        masked = jnp.where(counted > 0, scores, -1e30)
        prob_full = counted * jnp.exp(masked - lse_block[:, :, None])
        prob_bf = prob_full.astype(jnp.bfloat16)
        grad_prob = jnp.einsum(
            "qhd,khd->hqk", g_block, value_row_set, preferred_element_type=jnp.float32
        )
        grad_score = (prob_full * (grad_prob - delta_block[:, :, None])).astype(jnp.bfloat16)
        grad_q = (
            jnp.einsum("hqk,khd->qhd", grad_score, key_row_set, preferred_element_type=jnp.float32)
            * scaling
        ).astype(jnp.bfloat16)
        acc_k = acc_k + jnp.einsum(
            "hqk,qhd->khd", grad_score, q_block, preferred_element_type=jnp.float32
        )
        acc_v = acc_v + jnp.einsum(
            "hqk,qhd->khd", prob_bf, g_block, preferred_element_type=jnp.float32
        )
        return ((acc_k, acc_v), grad_q)

    zeros_all = jnp.zeros((length_all, heads_here, head_size), jnp.float32)
    (acc_k, acc_v), grad_q = lax.scan(
        step, (zeros_all, zeros_all), jnp.arange(blocks, dtype=jnp.int32)
    )
    return (
        grad_q.reshape(length_all, heads_here, head_size),
        (acc_k * scaling).astype(jnp.bfloat16),
        acc_v.astype(jnp.bfloat16),
    )


def dense_attention_forward(
    query_row_set, key_row_set, value_row_set, head_indices, segment_blocks, dilation_rates
):
    parity = head_indices % 2
    own_lse = local_lse(query_row_set, key_row_set)
    if query_row_set.shape[1] == 1:
        params = mask_params(head_indices[0], segment_blocks, dilation_rates)
        packed_out, packed_lse = dilated_forward_call(
            params,
            pick_rows(query_row_set, parity)[:, 0],
            pick_rows(key_row_set, parity)[:, 0],
            pick_rows(value_row_set, parity)[:, 0],
            pick_rows(own_lse, parity),
        )
        packed_out = packed_out[:, None]
    else:
        packed_out, packed_lse = sparse_attention_forward(
            pick_rows(query_row_set, parity),
            pick_rows(key_row_set, parity),
            pick_rows(value_row_set, parity),
            pick_rows(own_lse, parity),
            head_indices,
            segment_blocks,
            dilation_rates,
        )
    log_norm = spread_rows(packed_lse, parity, own_lse)
    attended = add_parts(
        local_output(query_row_set, key_row_set, value_row_set, log_norm), packed_out, parity
    )
    return (attended, log_norm)


def full_backward(
    query_row_set,
    key_row_set,
    value_row_set,
    attended,
    grad_attended,
    log_norm,
    head_indices,
    segment_blocks,
    dilation_rates,
):
    parity = head_indices % 2
    delta_row = jnp.sum(grad_attended.astype(jnp.float32) * attended.astype(jnp.float32), axis=2)
    local_parts = local_backward(
        query_row_set, key_row_set, value_row_set, grad_attended, log_norm, delta_row
    )
    if query_row_set.shape[1] == 1:
        params = mask_params(head_indices[0], segment_blocks, dilation_rates)
        packed_parts = dilated_backward_call(
            params,
            pick_rows(query_row_set, parity)[:, 0],
            pick_rows(key_row_set, parity)[:, 0],
            pick_rows(value_row_set, parity)[:, 0],
            pick_rows(grad_attended, parity)[:, 0],
            pick_rows(log_norm, parity),
            pick_rows(delta_row, parity),
        )
        packed_parts = tuple(part[:, None] for part in packed_parts)
    else:
        packed_parts = dilated_backward(
            pick_rows(query_row_set, parity),
            pick_rows(key_row_set, parity),
            pick_rows(value_row_set, parity),
            pick_rows(grad_attended, parity),
            pick_rows(log_norm, parity),
            pick_rows(delta_row, parity),
            head_indices,
            segment_blocks,
            dilation_rates,
        )
    return tuple(
        (
            add_parts(first_branch, second, parity)
            for first_branch, second in zip(local_parts, packed_parts)
        )
    )


def head_major(array, groups):
    tokens, width = array.shape
    return jnp.swapaxes(array.reshape(tokens, groups, width // groups), 0, 1)


def token_major(array):
    groups, tokens, width = array.shape
    return jnp.swapaxes(array, 0, 1).reshape(1, tokens, groups * width)


def head_norm(values, cot_rows, gain, bias):
    feature_axes = (0, 2)
    mean_row = jnp.mean(values, axis=feature_axes, keepdims=True)
    var_row = jnp.mean(values * values, axis=feature_axes, keepdims=True) - mean_row * mean_row
    inv_std = lax.rsqrt(var_row + epsilon)
    centered = (values - mean_row) * inv_std
    normed = (centered * gain + bias).astype(jnp.bfloat16)
    grad_y = cot_rows.astype(jnp.float32)
    scaled = grad_y * gain
    grad_tokens = (
        inv_std
        * (
            scaled
            - jnp.mean(scaled, axis=feature_axes, keepdims=True)
            - centered * jnp.mean(scaled * centered, axis=feature_axes, keepdims=True)
        )
    ).astype(jnp.bfloat16)
    return (normed, grad_tokens, jnp.sum(grad_y * centered, axis=1), jnp.sum(grad_y, axis=1))


def shards(
    queries,
    key_state_matrix,
    value_state_matrix,
    cotangent,
    sublayer_norm_gain,
    sublayer_norm_bias,
    segment_blocks,
    dilation_rates,
):
    tokens_here = queries.shape[1]
    width_all = queries.shape[2]
    head_size = width_all // H
    ctx_count = lax.axis_size("ctx")
    heads_here = H // ctx_count
    width_here = width_all // ctx_count
    head_first = lax.axis_index("ctx") * heads_here
    head_indices = head_first + jnp.arange(heads_here, dtype=jnp.int32)
    loss_scale = 1.0 / math.sqrt(lax.axis_size("dp") * tokens_here * ctx_count)
    tokens_all = tokens_here * ctx_count

    def to_rows(array):
        return array.reshape(tokens_all, heads_here, head_size)

    stacked_in = jnp.stack(
        [
            head_major(queries[0], ctx_count),
            head_major(key_state_matrix[0], ctx_count),
            head_major(value_state_matrix[0], ctx_count),
        ]
    )
    stacked_in = lax.all_to_all(stacked_in, "ctx", split_axis=1, concat_axis=1, tiled=True)
    query_head_tensor, key_head_tensor, value_head_tensor = (
        to_rows(stacked_in[0]),
        to_rows(stacked_in[1]),
        to_rows(stacked_in[2]),
    )
    attended, log_norm = dense_attention_forward(
        query_head_tensor,
        key_head_tensor,
        value_head_tensor,
        head_indices,
        segment_blocks,
        dilation_rates,
    )
    attended_hm = lax.all_to_all(
        attended.reshape(ctx_count, tokens_here, width_here), "ctx", 0, 0, tiled=True
    )
    gain_hm = sublayer_norm_gain.reshape(ctx_count, 1, width_here)
    bias_hm = sublayer_norm_bias.reshape(ctx_count, 1, width_here)
    normed_hm, grad_hm, gain_part, bias_part = head_norm(
        attended_hm.astype(jnp.float32),
        head_major(cotangent[0], ctx_count),
        gain_hm,
        bias_hm,
    )
    normed = token_major(normed_hm)
    grad_attended = to_rows(lax.all_to_all(grad_hm, "ctx", 0, 0, tiled=True))
    both = jnp.stack([gain_part, bias_part], axis=1)
    both = jnp.sum(lax.all_to_all(both, "ctx", 0, 0, tiled=True), axis=0)
    dp_count = lax.axis_size("dp")
    both = jnp.broadcast_to(both[None], (dp_count,) + both.shape)
    both = jnp.sum(lax.all_to_all(both, "dp", 0, 0, tiled=True), axis=0)
    grad_gain, grad_bias = both[0], both[1]
    grad_q, grad_k, grad_v = full_backward(
        query_head_tensor,
        key_head_tensor,
        value_head_tensor,
        attended,
        grad_attended,
        log_norm,
        head_indices,
        segment_blocks,
        dilation_rates,
    )
    stacked_out = lax.all_to_all(
        jnp.stack([part.reshape(ctx_count, tokens_here, width_here) for part in (grad_q, grad_k, grad_v)]),
        "ctx",
        split_axis=1,
        concat_axis=1,
        tiled=True,
    )
    return (
        normed,
        token_major(stacked_out[0]),
        token_major(stacked_out[1]),
        token_major(stacked_out[2]),
        grad_gain * loss_scale,
        grad_bias * loss_scale,
    )


def solution(mesh):
    return jax.shard_map(
        shards,
        mesh=mesh,
        in_specs=(
            P("dp", "ctx", None),
            P("dp", "ctx", None),
            P("dp", "ctx", None),
            P("dp", "ctx", None),
            P(),
            P(),
            P(),
            P(),
        ),
        out_specs=(
            P("dp", "ctx", None),
            P("dp", "ctx", None),
            P("dp", "ctx", None),
            P("dp", "ctx", None),
            P("ctx"),
            P("ctx"),
        ),
        check_vma=False,
    )
```

```python
import math

import jax
import jax.numpy as jnp
from jax import lax
from jax.experimental import pallas as pl
from jax.experimental.pallas import tpu as pltpu
from jax.sharding import PartitionSpec as P

H = 16
BLK = 128
G = 4


epsilon = 1e-05


def pick_rows(array, parity):
    pairs = array.reshape((array.shape[0] // 2, 2) + array.shape[1:])
    cond = (parity == 0).reshape((-1,) + (1,) * (array.ndim - 2))
    return jnp.where(cond, pairs[:, 0], pairs[:, 1])


def spread_rows(packed, parity, base):
    pairs = base.reshape((base.shape[0] // 2, 2) + base.shape[1:])
    cond = (parity == 0).reshape((-1,) + (1,) * (base.ndim - 2))
    first_branch = jnp.where(cond, packed, pairs[:, 0])
    second = jnp.where(cond, pairs[:, 1], packed)
    return jnp.stack([first_branch, second], axis=1).reshape(base.shape)


def add_parts(full_part, packed_part, parity):
    spread = spread_rows(packed_part, parity, jnp.zeros_like(full_part))
    full_part = lax.optimization_barrier(full_part)
    spread = lax.optimization_barrier(spread)
    return (full_part.astype(jnp.float32) + spread.astype(jnp.float32)).astype(jnp.bfloat16)


def block_view(array):
    return array.reshape((array.shape[0] // BLK, BLK) + array.shape[1:])


def lse_view(log_norm):
    return jnp.transpose(block_view(log_norm), (0, 2, 1))


def local_scores(query_row_set, key_row_set):
    scaling = 1.0 / math.sqrt(query_row_set.shape[-1])
    return (
        jnp.einsum(
            "bqhd,bkhd->bhqk",
            block_view(query_row_set),
            block_view(key_row_set),
            preferred_element_type=jnp.float32,
        )
        * scaling
    )


def local_lse(query_row_set, key_row_set):
    scores = local_scores(query_row_set, key_row_set)
    row_max = jnp.max(scores, axis=3)
    total = row_max + jnp.log(jnp.sum(jnp.exp(scores - row_max[..., None]), axis=3))
    return jnp.transpose(total, (0, 2, 1)).reshape(query_row_set.shape[0], query_row_set.shape[1])


def local_output(query_row_set, key_row_set, value_row_set, log_norm):
    scores = local_scores(query_row_set, key_row_set)
    prob_bf = jnp.exp(scores - lse_view(log_norm)[..., None]).astype(jnp.bfloat16)
    output = jnp.einsum(
        "bhqk,bkhd->bqhd", prob_bf, block_view(value_row_set), preferred_element_type=jnp.float32
    )
    return output.astype(jnp.bfloat16).reshape(query_row_set.shape)


def local_backward(query_row_set, key_row_set, value_row_set, grad_rows, log_norm, delta_row):
    scaling = 1.0 / math.sqrt(query_row_set.shape[-1])
    scores = local_scores(query_row_set, key_row_set)
    prob_full = jnp.exp(scores - lse_view(log_norm)[..., None])
    prob_bf = prob_full.astype(jnp.bfloat16)
    grad_prob = jnp.einsum(
        "bqhd,bkhd->bhqk",
        block_view(grad_rows),
        block_view(value_row_set),
        preferred_element_type=jnp.float32,
    )
    grad_score = (prob_full * (grad_prob - lse_view(delta_row)[..., None])).astype(jnp.bfloat16)
    grad_q = jnp.einsum(
        "bhqk,bkhd->bqhd", grad_score, block_view(key_row_set), preferred_element_type=jnp.float32
    )
    grad_k = jnp.einsum(
        "bhqk,bqhd->bkhd", grad_score, block_view(query_row_set), preferred_element_type=jnp.float32
    )
    grad_v = jnp.einsum(
        "bhqk,bqhd->bkhd", prob_bf, block_view(grad_rows), preferred_element_type=jnp.float32
    )
    shape = query_row_set.shape
    return (
        (grad_q * scaling).astype(jnp.bfloat16).reshape(shape),
        (grad_k * scaling).astype(jnp.bfloat16).reshape(shape),
        grad_v.astype(jnp.bfloat16).reshape(shape),
    )


def packed_positions(start, count, head_indices):
    rows = start + jnp.arange(count, dtype=jnp.int32)
    return 2 * rows[None, :] + (head_indices % 2)[:, None]


def dilation_multiplier(
    query_positions, key_positions, head_indices, segment_blocks, dilation_rates
):
    counted = jnp.zeros(
        (head_indices.shape[0], query_positions.shape[1], key_positions.shape[1]), jnp.float32
    )
    for dilation_branch in range(1, G):
        seg_width = segment_blocks[dilation_branch] * BLK
        low_bits = dilation_rates[dilation_branch] - 1
        same_seg = (query_positions[:, :, None] ^ key_positions[:, None, :]) < seg_width
        selected_queries = ((query_positions ^ head_indices[:, None]) & low_bits) == 0
        selected_keys = ((key_positions ^ head_indices[:, None]) & low_bits) == 0
        counted = counted + (
            same_seg & selected_queries[:, :, None] & selected_keys[:, None, :]
        ).astype(jnp.float32)
    return counted


def dilated_mask(params_ref, rows, keys, row_first):
    head = params_ref[2 * G]
    parity = params_ref[2 * G + 1]
    query_positions = 2 * (row_first + lax.broadcasted_iota(jnp.int32, (rows, keys), 0)) + parity
    key_positions = 2 * lax.broadcasted_iota(jnp.int32, (rows, keys), 1) + parity
    apart = query_positions ^ key_positions
    query_phase = query_positions ^ head
    key_phase = key_positions ^ head
    counted = jnp.zeros((rows, keys), jnp.float32)
    for branch in range(1, G):
        low_bits = params_ref[G + branch]
        kept = (
            (apart < params_ref[branch])
            & ((query_phase & low_bits) == 0)
            & ((key_phase & low_bits) == 0)
        )
        counted = counted + jnp.where(kept, 1.0, 0.0)
    return counted


def dilated_forward_kernel(params_ref, q_ref, k_ref, v_ref, own_ref, out_ref, lse_ref):
    rows, head_size = q_ref.shape
    keys = k_ref.shape[0]
    scaling = 1.0 / math.sqrt(head_size)
    counted = dilated_mask(params_ref, rows, keys, pl.program_id(0) * rows)
    scores = (
        lax.dot_general(
            q_ref[...], k_ref[...], (((1,), (1,)), ((), ())), preferred_element_type=jnp.float32
        )
        * scaling
    )
    masked = jnp.where(counted > 0, scores, -1e30)
    row_max = jnp.max(masked, axis=1, keepdims=True)
    part_lse = row_max + jnp.log(
        jnp.sum(counted * jnp.exp(masked - row_max), axis=1, keepdims=True)
    )
    own_lse = own_ref[...]
    top = jnp.maximum(part_lse, own_lse)
    log_norm = top + jnp.log(jnp.exp(part_lse - top) + jnp.exp(own_lse - top))
    prob_bf = (counted * jnp.exp(masked - log_norm)).astype(jnp.bfloat16)
    out_ref[...] = jnp.dot(prob_bf, v_ref[...], preferred_element_type=jnp.float32).astype(
        out_ref.dtype
    )
    lse_ref[...] = log_norm


def mask_params(head, segment_blocks, dilation_rates):
    return jnp.concatenate(
        [
            segment_blocks.astype(jnp.int32) * BLK,
            dilation_rates.astype(jnp.int32) - 1,
            jnp.stack([head, head % 2]).astype(jnp.int32),
        ]
    )


def dilated_forward_call(params, q, k, v, own, row_block=256):
    rows, head_size = q.shape
    keys = k.shape[0]
    grid = (rows // row_block,)
    return pl.pallas_call(
        dilated_forward_kernel,
        grid=grid,
        in_specs=[
            pl.BlockSpec(memory_space=pltpu.SMEM),
            pl.BlockSpec((row_block, head_size), lambda i: (i, 0)),
            pl.BlockSpec((keys, head_size), lambda i: (0, 0)),
            pl.BlockSpec((keys, head_size), lambda i: (0, 0)),
            pl.BlockSpec((row_block, 1), lambda i: (i, 0)),
        ],
        out_specs=[
            pl.BlockSpec((row_block, head_size), lambda i: (i, 0)),
            pl.BlockSpec((row_block, 1), lambda i: (i, 0)),
        ],
        out_shape=[
            jax.ShapeDtypeStruct((rows, head_size), jnp.bfloat16),
            jax.ShapeDtypeStruct((rows, 1), jnp.float32),
        ],
        cost_estimate=pl.CostEstimate(
            flops=4 * rows * keys * head_size,
            transcendentals=rows * keys,
            bytes_accessed=2 * (3 * rows * head_size + rows * head_size) + 8 * rows,
        ),
    )(params, q, k, v, own)


def sparse_attention_forward(
    query_row_set,
    key_row_set,
    value_row_set,
    baseline_logsumexp,
    head_indices,
    segment_blocks,
    dilation_rates,
):
    length_all, heads_here, head_size = query_row_set.shape
    rows_per_block = length_all
    blocks = length_all // rows_per_block
    scaling = 1.0 / math.sqrt(head_size)
    key_positions = packed_positions(0, length_all, head_indices)

    def one_block(block_id):
        starting_row = block_id * rows_per_block
        q_block = lax.dynamic_slice_in_dim(query_row_set, starting_row, rows_per_block, 0)
        own_lse = lax.dynamic_slice_in_dim(baseline_logsumexp, starting_row, rows_per_block, 0).T
        counted = dilation_multiplier(
            packed_positions(starting_row, rows_per_block, head_indices),
            key_positions,
            head_indices,
            segment_blocks,
            dilation_rates,
        )
        scores = (
            jnp.einsum("qhd,khd->hqk", q_block, key_row_set, preferred_element_type=jnp.float32)
            * scaling
        )
        masked = jnp.where(counted > 0, scores, -1e30)
        row_max = jnp.max(masked, axis=2)
        part_lse = row_max + jnp.log(
            jnp.sum(counted * jnp.exp(masked - row_max[:, :, None]), axis=2)
        )
        top = jnp.maximum(part_lse, own_lse)
        log_norm = top + jnp.log(jnp.exp(part_lse - top) + jnp.exp(own_lse - top))
        prob_bf = (counted * jnp.exp(masked - log_norm[:, :, None])).astype(jnp.bfloat16)
        output = jnp.einsum(
            "hqk,khd->qhd", prob_bf, value_row_set, preferred_element_type=jnp.float32
        ).astype(jnp.bfloat16)
        return (output, log_norm)

    outputs, lse_blocks = lax.map(one_block, jnp.arange(blocks, dtype=jnp.int32))
    return (
        outputs.reshape(length_all, heads_here, head_size),
        jnp.transpose(lse_blocks, (0, 2, 1)).reshape(length_all, heads_here),
    )


def dilated_backward(
    query_row_set,
    key_row_set,
    value_row_set,
    grad_rows,
    log_norm,
    delta_row,
    head_indices,
    segment_blocks,
    dilation_rates,
):
    length_all, heads_here, head_size = query_row_set.shape
    rows_per_block = length_all
    blocks = length_all // rows_per_block
    scaling = 1.0 / math.sqrt(head_size)
    key_positions = packed_positions(0, length_all, head_indices)

    def step(carry, block_id):
        acc_k, acc_v = carry
        starting_row = block_id * rows_per_block
        q_block = lax.dynamic_slice_in_dim(query_row_set, starting_row, rows_per_block, 0)
        g_block = lax.dynamic_slice_in_dim(grad_rows, starting_row, rows_per_block, 0)
        lse_block = lax.dynamic_slice_in_dim(log_norm, starting_row, rows_per_block, 0).T
        delta_block = lax.dynamic_slice_in_dim(delta_row, starting_row, rows_per_block, 0).T
        counted = dilation_multiplier(
            packed_positions(starting_row, rows_per_block, head_indices),
            key_positions,
            head_indices,
            segment_blocks,
            dilation_rates,
        )
        scores = (
            jnp.einsum("qhd,khd->hqk", q_block, key_row_set, preferred_element_type=jnp.float32)
            * scaling
        )
        masked = jnp.where(counted > 0, scores, -1e30)
        prob_full = counted * jnp.exp(masked - lse_block[:, :, None])
        prob_bf = prob_full.astype(jnp.bfloat16)
        grad_prob = jnp.einsum(
            "qhd,khd->hqk", g_block, value_row_set, preferred_element_type=jnp.float32
        )
        grad_score = (prob_full * (grad_prob - delta_block[:, :, None])).astype(jnp.bfloat16)
        grad_q = (
            jnp.einsum("hqk,khd->qhd", grad_score, key_row_set, preferred_element_type=jnp.float32)
            * scaling
        ).astype(jnp.bfloat16)
        acc_k = acc_k + jnp.einsum(
            "hqk,qhd->khd", grad_score, q_block, preferred_element_type=jnp.float32
        )
        acc_v = acc_v + jnp.einsum(
            "hqk,qhd->khd", prob_bf, g_block, preferred_element_type=jnp.float32
        )
        return ((acc_k, acc_v), grad_q)

    zeros_all = jnp.zeros((length_all, heads_here, head_size), jnp.float32)
    (acc_k, acc_v), grad_q = lax.scan(
        step, (zeros_all, zeros_all), jnp.arange(blocks, dtype=jnp.int32)
    )
    return (
        grad_q.reshape(length_all, heads_here, head_size),
        (acc_k * scaling).astype(jnp.bfloat16),
        acc_v.astype(jnp.bfloat16),
    )


def dense_attention_forward(
    query_row_set, key_row_set, value_row_set, head_indices, segment_blocks, dilation_rates
):
    parity = head_indices % 2
    own_lse = local_lse(query_row_set, key_row_set)
    if query_row_set.shape[1] == 1:
        params = mask_params(head_indices[0], segment_blocks, dilation_rates)
        packed_out, packed_lse = dilated_forward_call(
            params,
            pick_rows(query_row_set, parity)[:, 0],
            pick_rows(key_row_set, parity)[:, 0],
            pick_rows(value_row_set, parity)[:, 0],
            pick_rows(own_lse, parity),
        )
        packed_out = packed_out[:, None]
    else:
        packed_out, packed_lse = sparse_attention_forward(
            pick_rows(query_row_set, parity),
            pick_rows(key_row_set, parity),
            pick_rows(value_row_set, parity),
            pick_rows(own_lse, parity),
            head_indices,
            segment_blocks,
            dilation_rates,
        )
    log_norm = spread_rows(packed_lse, parity, own_lse)
    attended = add_parts(
        local_output(query_row_set, key_row_set, value_row_set, log_norm), packed_out, parity
    )
    return (attended, log_norm)


def full_backward(
    query_row_set,
    key_row_set,
    value_row_set,
    attended,
    grad_attended,
    log_norm,
    head_indices,
    segment_blocks,
    dilation_rates,
):
    parity = head_indices % 2
    delta_row = jnp.sum(grad_attended.astype(jnp.float32) * attended.astype(jnp.float32), axis=2)
    local_parts = local_backward(
        query_row_set, key_row_set, value_row_set, grad_attended, log_norm, delta_row
    )
    packed_parts = dilated_backward(
        pick_rows(query_row_set, parity),
        pick_rows(key_row_set, parity),
        pick_rows(value_row_set, parity),
        pick_rows(grad_attended, parity),
        pick_rows(log_norm, parity),
        pick_rows(delta_row, parity),
        head_indices,
        segment_blocks,
        dilation_rates,
    )
    return tuple(
        (
            add_parts(first_branch, second, parity)
            for first_branch, second in zip(local_parts, packed_parts)
        )
    )


def head_major(array, groups):
    tokens, width = array.shape
    return jnp.swapaxes(array.reshape(tokens, groups, width // groups), 0, 1)


def token_major(array):
    groups, tokens, width = array.shape
    return jnp.swapaxes(array, 0, 1).reshape(1, tokens, groups * width)


def head_norm(values, cot_rows, gain, bias):
    feature_axes = (0, 2)
    mean_row = jnp.mean(values, axis=feature_axes, keepdims=True)
    var_row = jnp.mean(values * values, axis=feature_axes, keepdims=True) - mean_row * mean_row
    inv_std = lax.rsqrt(var_row + epsilon)
    centered = (values - mean_row) * inv_std
    normed = (centered * gain + bias).astype(jnp.bfloat16)
    grad_y = cot_rows.astype(jnp.float32)
    scaled = grad_y * gain
    grad_tokens = (
        inv_std
        * (
            scaled
            - jnp.mean(scaled, axis=feature_axes, keepdims=True)
            - centered * jnp.mean(scaled * centered, axis=feature_axes, keepdims=True)
        )
    ).astype(jnp.bfloat16)
    return (normed, grad_tokens, jnp.sum(grad_y * centered, axis=1), jnp.sum(grad_y, axis=1))


def shards(
    queries,
    key_state_matrix,
    value_state_matrix,
    cotangent,
    sublayer_norm_gain,
    sublayer_norm_bias,
    segment_blocks,
    dilation_rates,
):
    tokens_here = queries.shape[1]
    width_all = queries.shape[2]
    head_size = width_all // H
    ctx_count = lax.axis_size("ctx")
    heads_here = H // ctx_count
    width_here = width_all // ctx_count
    head_first = lax.axis_index("ctx") * heads_here
    head_indices = head_first + jnp.arange(heads_here, dtype=jnp.int32)
    loss_scale = 1.0 / math.sqrt(lax.axis_size("dp") * tokens_here * ctx_count)
    tokens_all = tokens_here * ctx_count

    def to_rows(array):
        return array.reshape(tokens_all, heads_here, head_size)

    stacked_in = jnp.stack(
        [
            head_major(queries[0], ctx_count),
            head_major(key_state_matrix[0], ctx_count),
            head_major(value_state_matrix[0], ctx_count),
        ]
    )
    stacked_in = lax.all_to_all(stacked_in, "ctx", split_axis=1, concat_axis=1, tiled=True)
    query_head_tensor, key_head_tensor, value_head_tensor = (
        to_rows(stacked_in[0]),
        to_rows(stacked_in[1]),
        to_rows(stacked_in[2]),
    )
    attended, log_norm = dense_attention_forward(
        query_head_tensor,
        key_head_tensor,
        value_head_tensor,
        head_indices,
        segment_blocks,
        dilation_rates,
    )
    attended_hm = lax.all_to_all(
        attended.reshape(ctx_count, tokens_here, width_here), "ctx", 0, 0, tiled=True
    )
    gain_hm = sublayer_norm_gain.reshape(ctx_count, 1, width_here)
    bias_hm = sublayer_norm_bias.reshape(ctx_count, 1, width_here)
    normed_hm, grad_hm, gain_part, bias_part = head_norm(
        attended_hm.astype(jnp.float32),
        head_major(cotangent[0], ctx_count),
        gain_hm,
        bias_hm,
    )
    normed = token_major(normed_hm)
    both = jnp.stack([gain_part, bias_part], axis=1)
    carried = jnp.concatenate([grad_hm.astype(jnp.float32), both], axis=1)
    carried = lax.all_to_all(carried, "ctx", 0, 0, tiled=True)
    grad_attended = to_rows(carried[:, :tokens_here].astype(jnp.bfloat16))
    both = jnp.sum(carried[:, tokens_here:], axis=0)
    dp_count = lax.axis_size("dp")
    both = jnp.broadcast_to(both[None], (dp_count,) + both.shape)
    both = jnp.sum(lax.all_to_all(both, "dp", 0, 0, tiled=True), axis=0)
    grad_gain, grad_bias = both[0], both[1]
    grad_q, grad_k, grad_v = full_backward(
        query_head_tensor,
        key_head_tensor,
        value_head_tensor,
        attended,
        grad_attended,
        log_norm,
        head_indices,
        segment_blocks,
        dilation_rates,
    )
    stacked_out = lax.all_to_all(
        jnp.stack([part.reshape(ctx_count, tokens_here, width_here) for part in (grad_q, grad_k, grad_v)]),
        "ctx",
        split_axis=1,
        concat_axis=1,
        tiled=True,
    )
    return (
        normed,
        token_major(stacked_out[0]),
        token_major(stacked_out[1]),
        token_major(stacked_out[2]),
        grad_gain * loss_scale,
        grad_bias * loss_scale,
    )


def solution(mesh):
    return jax.shard_map(
        shards,
        mesh=mesh,
        in_specs=(
            P("dp", "ctx", None),
            P("dp", "ctx", None),
            P("dp", "ctx", None),
            P("dp", "ctx", None),
            P(),
            P(),
            P(),
            P(),
        ),
        out_specs=(
            P("dp", "ctx", None),
            P("dp", "ctx", None),
            P("dp", "ctx", None),
            P("dp", "ctx", None),
            P("ctx"),
            P("ctx"),
        ),
        check_vma=False,
    )
```

```python
import math

import jax
import jax.numpy as jnp
from jax import lax
from jax.experimental import pallas as pl
from jax.experimental.pallas import tpu as pltpu
from jax.sharding import PartitionSpec as P

H = 16
BLK = 128
G = 4


epsilon = 1e-05


def pick_rows(array, parity):
    pairs = array.reshape((array.shape[0] // 2, 2) + array.shape[1:])
    cond = (parity == 0).reshape((-1,) + (1,) * (array.ndim - 2))
    return jnp.where(cond, pairs[:, 0], pairs[:, 1])


def spread_rows(packed, parity, base):
    pairs = base.reshape((base.shape[0] // 2, 2) + base.shape[1:])
    cond = (parity == 0).reshape((-1,) + (1,) * (base.ndim - 2))
    first_branch = jnp.where(cond, packed, pairs[:, 0])
    second = jnp.where(cond, pairs[:, 1], packed)
    return jnp.stack([first_branch, second], axis=1).reshape(base.shape)


def add_parts(full_part, packed_part, parity):
    spread = spread_rows(packed_part, parity, jnp.zeros_like(full_part))
    full_part = lax.optimization_barrier(full_part)
    spread = lax.optimization_barrier(spread)
    return (full_part.astype(jnp.float32) + spread.astype(jnp.float32)).astype(jnp.bfloat16)


def block_view(array):
    return array.reshape((array.shape[0] // BLK, BLK) + array.shape[1:])


def lse_view(log_norm):
    return jnp.transpose(block_view(log_norm), (0, 2, 1))


def local_scores(query_row_set, key_row_set):
    scaling = 1.0 / math.sqrt(query_row_set.shape[-1])
    return (
        jnp.einsum(
            "bqhd,bkhd->bhqk",
            block_view(query_row_set),
            block_view(key_row_set),
            preferred_element_type=jnp.float32,
        )
        * scaling
    )


def local_lse(query_row_set, key_row_set):
    scores = local_scores(query_row_set, key_row_set)
    row_max = jnp.max(scores, axis=3)
    total = row_max + jnp.log(jnp.sum(jnp.exp(scores - row_max[..., None]), axis=3))
    return jnp.transpose(total, (0, 2, 1)).reshape(query_row_set.shape[0], query_row_set.shape[1])


def local_output(query_row_set, key_row_set, value_row_set, log_norm):
    scores = local_scores(query_row_set, key_row_set)
    prob_bf = jnp.exp(scores - lse_view(log_norm)[..., None]).astype(jnp.bfloat16)
    output = jnp.einsum(
        "bhqk,bkhd->bqhd", prob_bf, block_view(value_row_set), preferred_element_type=jnp.float32
    )
    return output.astype(jnp.bfloat16).reshape(query_row_set.shape)


def local_backward(query_row_set, key_row_set, value_row_set, grad_rows, log_norm, delta_row):
    scaling = 1.0 / math.sqrt(query_row_set.shape[-1])
    scores = local_scores(query_row_set, key_row_set)
    prob_full = jnp.exp(scores - lse_view(log_norm)[..., None])
    prob_bf = prob_full.astype(jnp.bfloat16)
    grad_prob = jnp.einsum(
        "bqhd,bkhd->bhqk",
        block_view(grad_rows),
        block_view(value_row_set),
        preferred_element_type=jnp.float32,
    )
    grad_score = (prob_full * (grad_prob - lse_view(delta_row)[..., None])).astype(jnp.bfloat16)
    grad_q = jnp.einsum(
        "bhqk,bkhd->bqhd", grad_score, block_view(key_row_set), preferred_element_type=jnp.float32
    )
    grad_k = jnp.einsum(
        "bhqk,bqhd->bkhd", grad_score, block_view(query_row_set), preferred_element_type=jnp.float32
    )
    grad_v = jnp.einsum(
        "bhqk,bqhd->bkhd", prob_bf, block_view(grad_rows), preferred_element_type=jnp.float32
    )
    shape = query_row_set.shape
    return (
        (grad_q * scaling).astype(jnp.bfloat16).reshape(shape),
        (grad_k * scaling).astype(jnp.bfloat16).reshape(shape),
        grad_v.astype(jnp.bfloat16).reshape(shape),
    )


def packed_positions(start, count, head_indices):
    rows = start + jnp.arange(count, dtype=jnp.int32)
    return 2 * rows[None, :] + (head_indices % 2)[:, None]


def dilation_multiplier(
    query_positions, key_positions, head_indices, segment_blocks, dilation_rates
):
    counted = jnp.zeros(
        (head_indices.shape[0], query_positions.shape[1], key_positions.shape[1]), jnp.float32
    )
    for dilation_branch in range(1, G):
        seg_width = segment_blocks[dilation_branch] * BLK
        low_bits = dilation_rates[dilation_branch] - 1
        same_seg = (query_positions[:, :, None] ^ key_positions[:, None, :]) < seg_width
        selected_queries = ((query_positions ^ head_indices[:, None]) & low_bits) == 0
        selected_keys = ((key_positions ^ head_indices[:, None]) & low_bits) == 0
        counted = counted + (
            same_seg & selected_queries[:, :, None] & selected_keys[:, None, :]
        ).astype(jnp.float32)
    return counted


def dilated_mask(params_ref, rows, keys, row_first):
    head = params_ref[2 * G]
    parity = params_ref[2 * G + 1]
    query_positions = 2 * (row_first + lax.broadcasted_iota(jnp.int32, (rows, keys), 0)) + parity
    key_positions = 2 * lax.broadcasted_iota(jnp.int32, (rows, keys), 1) + parity
    apart = query_positions ^ key_positions
    query_phase = query_positions ^ head
    key_phase = key_positions ^ head
    counted = jnp.zeros((rows, keys), jnp.float32)
    for branch in range(1, G):
        low_bits = params_ref[G + branch]
        kept = (
            (apart < params_ref[branch])
            & ((query_phase & low_bits) == 0)
            & ((key_phase & low_bits) == 0)
        )
        counted = counted + jnp.where(kept, 1.0, 0.0)
    return counted


def dilated_forward_kernel(params_ref, q_ref, k_ref, v_ref, own_ref, out_ref, lse_ref):
    rows, head_size = q_ref.shape
    keys = k_ref.shape[0]
    scaling = 1.0 / math.sqrt(head_size)
    counted = dilated_mask(params_ref, rows, keys, pl.program_id(0) * rows)
    scores = (
        lax.dot_general(
            q_ref[...], k_ref[...], (((1,), (1,)), ((), ())), preferred_element_type=jnp.float32
        )
        * scaling
    )
    masked = jnp.where(counted > 0, scores, -1e30)
    row_max = jnp.max(masked, axis=1, keepdims=True)
    shifted = counted * jnp.exp(masked - row_max)
    part_lse = row_max + jnp.log(jnp.sum(shifted, axis=1, keepdims=True))
    own_lse = own_ref[...]
    top = jnp.maximum(part_lse, own_lse)
    log_norm = top + jnp.log(jnp.exp(part_lse - top) + jnp.exp(own_lse - top))
    prob_bf = (shifted * jnp.exp(row_max - log_norm)).astype(jnp.bfloat16)
    out_ref[...] = jnp.dot(prob_bf, v_ref[...], preferred_element_type=jnp.float32).astype(
        out_ref.dtype
    )
    lse_ref[...] = log_norm


def mask_params(head, segment_blocks, dilation_rates):
    return jnp.concatenate(
        [
            segment_blocks.astype(jnp.int32) * BLK,
            dilation_rates.astype(jnp.int32) - 1,
            jnp.stack([head, head % 2]).astype(jnp.int32),
        ]
    )


def dilated_forward_call(params, q, k, v, own, row_block=256):
    rows, head_size = q.shape
    keys = k.shape[0]
    grid = (rows // row_block,)
    return pl.pallas_call(
        dilated_forward_kernel,
        grid=grid,
        in_specs=[
            pl.BlockSpec(memory_space=pltpu.SMEM),
            pl.BlockSpec((row_block, head_size), lambda i: (i, 0)),
            pl.BlockSpec((keys, head_size), lambda i: (0, 0)),
            pl.BlockSpec((keys, head_size), lambda i: (0, 0)),
            pl.BlockSpec((row_block, 1), lambda i: (i, 0)),
        ],
        out_specs=[
            pl.BlockSpec((row_block, head_size), lambda i: (i, 0)),
            pl.BlockSpec((row_block, 1), lambda i: (i, 0)),
        ],
        out_shape=[
            jax.ShapeDtypeStruct((rows, head_size), jnp.bfloat16),
            jax.ShapeDtypeStruct((rows, 1), jnp.float32),
        ],
        cost_estimate=pl.CostEstimate(
            flops=4 * rows * keys * head_size,
            transcendentals=rows * keys,
            bytes_accessed=2 * (3 * rows * head_size + rows * head_size) + 8 * rows,
        ),
    )(params, q, k, v, own)


def sparse_attention_forward(
    query_row_set,
    key_row_set,
    value_row_set,
    baseline_logsumexp,
    head_indices,
    segment_blocks,
    dilation_rates,
):
    length_all, heads_here, head_size = query_row_set.shape
    rows_per_block = length_all
    blocks = length_all // rows_per_block
    scaling = 1.0 / math.sqrt(head_size)
    key_positions = packed_positions(0, length_all, head_indices)

    def one_block(block_id):
        starting_row = block_id * rows_per_block
        q_block = lax.dynamic_slice_in_dim(query_row_set, starting_row, rows_per_block, 0)
        own_lse = lax.dynamic_slice_in_dim(baseline_logsumexp, starting_row, rows_per_block, 0).T
        counted = dilation_multiplier(
            packed_positions(starting_row, rows_per_block, head_indices),
            key_positions,
            head_indices,
            segment_blocks,
            dilation_rates,
        )
        scores = (
            jnp.einsum("qhd,khd->hqk", q_block, key_row_set, preferred_element_type=jnp.float32)
            * scaling
        )
        masked = jnp.where(counted > 0, scores, -1e30)
        row_max = jnp.max(masked, axis=2)
        part_lse = row_max + jnp.log(
            jnp.sum(counted * jnp.exp(masked - row_max[:, :, None]), axis=2)
        )
        top = jnp.maximum(part_lse, own_lse)
        log_norm = top + jnp.log(jnp.exp(part_lse - top) + jnp.exp(own_lse - top))
        prob_bf = (counted * jnp.exp(masked - log_norm[:, :, None])).astype(jnp.bfloat16)
        output = jnp.einsum(
            "hqk,khd->qhd", prob_bf, value_row_set, preferred_element_type=jnp.float32
        ).astype(jnp.bfloat16)
        return (output, log_norm)

    outputs, lse_blocks = lax.map(one_block, jnp.arange(blocks, dtype=jnp.int32))
    return (
        outputs.reshape(length_all, heads_here, head_size),
        jnp.transpose(lse_blocks, (0, 2, 1)).reshape(length_all, heads_here),
    )


def dilated_backward(
    query_row_set,
    key_row_set,
    value_row_set,
    grad_rows,
    log_norm,
    delta_row,
    head_indices,
    segment_blocks,
    dilation_rates,
):
    length_all, heads_here, head_size = query_row_set.shape
    rows_per_block = length_all
    blocks = length_all // rows_per_block
    scaling = 1.0 / math.sqrt(head_size)
    key_positions = packed_positions(0, length_all, head_indices)

    def step(carry, block_id):
        acc_k, acc_v = carry
        starting_row = block_id * rows_per_block
        q_block = lax.dynamic_slice_in_dim(query_row_set, starting_row, rows_per_block, 0)
        g_block = lax.dynamic_slice_in_dim(grad_rows, starting_row, rows_per_block, 0)
        lse_block = lax.dynamic_slice_in_dim(log_norm, starting_row, rows_per_block, 0).T
        delta_block = lax.dynamic_slice_in_dim(delta_row, starting_row, rows_per_block, 0).T
        counted = dilation_multiplier(
            packed_positions(starting_row, rows_per_block, head_indices),
            key_positions,
            head_indices,
            segment_blocks,
            dilation_rates,
        )
        scores = (
            jnp.einsum("qhd,khd->hqk", q_block, key_row_set, preferred_element_type=jnp.float32)
            * scaling
        )
        masked = jnp.where(counted > 0, scores, -1e30)
        prob_full = counted * jnp.exp(masked - lse_block[:, :, None])
        prob_bf = prob_full.astype(jnp.bfloat16)
        grad_prob = jnp.einsum(
            "qhd,khd->hqk", g_block, value_row_set, preferred_element_type=jnp.float32
        )
        grad_score = (prob_full * (grad_prob - delta_block[:, :, None])).astype(jnp.bfloat16)
        grad_q = (
            jnp.einsum("hqk,khd->qhd", grad_score, key_row_set, preferred_element_type=jnp.float32)
            * scaling
        ).astype(jnp.bfloat16)
        acc_k = acc_k + jnp.einsum(
            "hqk,qhd->khd", grad_score, q_block, preferred_element_type=jnp.float32
        )
        acc_v = acc_v + jnp.einsum(
            "hqk,qhd->khd", prob_bf, g_block, preferred_element_type=jnp.float32
        )
        return ((acc_k, acc_v), grad_q)

    zeros_all = jnp.zeros((length_all, heads_here, head_size), jnp.float32)
    (acc_k, acc_v), grad_q = lax.scan(
        step, (zeros_all, zeros_all), jnp.arange(blocks, dtype=jnp.int32)
    )
    return (
        grad_q.reshape(length_all, heads_here, head_size),
        (acc_k * scaling).astype(jnp.bfloat16),
        acc_v.astype(jnp.bfloat16),
    )


def dense_attention_forward(
    query_row_set, key_row_set, value_row_set, head_indices, segment_blocks, dilation_rates
):
    parity = head_indices % 2
    own_lse = local_lse(query_row_set, key_row_set)
    if query_row_set.shape[1] == 1:
        params = mask_params(head_indices[0], segment_blocks, dilation_rates)
        packed_out, packed_lse = dilated_forward_call(
            params,
            pick_rows(query_row_set, parity)[:, 0],
            pick_rows(key_row_set, parity)[:, 0],
            pick_rows(value_row_set, parity)[:, 0],
            pick_rows(own_lse, parity),
        )
        packed_out = packed_out[:, None]
    else:
        packed_out, packed_lse = sparse_attention_forward(
            pick_rows(query_row_set, parity),
            pick_rows(key_row_set, parity),
            pick_rows(value_row_set, parity),
            pick_rows(own_lse, parity),
            head_indices,
            segment_blocks,
            dilation_rates,
        )
    log_norm = spread_rows(packed_lse, parity, own_lse)
    attended = add_parts(
        local_output(query_row_set, key_row_set, value_row_set, log_norm), packed_out, parity
    )
    return (attended, log_norm)


def full_backward(
    query_row_set,
    key_row_set,
    value_row_set,
    attended,
    grad_attended,
    log_norm,
    head_indices,
    segment_blocks,
    dilation_rates,
):
    parity = head_indices % 2
    delta_row = jnp.sum(grad_attended.astype(jnp.float32) * attended.astype(jnp.float32), axis=2)
    local_parts = local_backward(
        query_row_set, key_row_set, value_row_set, grad_attended, log_norm, delta_row
    )
    packed_parts = dilated_backward(
        pick_rows(query_row_set, parity),
        pick_rows(key_row_set, parity),
        pick_rows(value_row_set, parity),
        pick_rows(grad_attended, parity),
        pick_rows(log_norm, parity),
        pick_rows(delta_row, parity),
        head_indices,
        segment_blocks,
        dilation_rates,
    )
    return tuple(
        (
            add_parts(first_branch, second, parity)
            for first_branch, second in zip(local_parts, packed_parts)
        )
    )


def head_major(array, groups):
    tokens, width = array.shape
    return jnp.swapaxes(array.reshape(tokens, groups, width // groups), 0, 1)


def token_major(array):
    groups, tokens, width = array.shape
    return jnp.swapaxes(array, 0, 1).reshape(1, tokens, groups * width)


def head_norm(values, cot_rows, gain, bias):
    feature_axes = (0, 2)
    mean_row = jnp.mean(values, axis=feature_axes, keepdims=True)
    var_row = jnp.mean(values * values, axis=feature_axes, keepdims=True) - mean_row * mean_row
    inv_std = lax.rsqrt(var_row + epsilon)
    centered = (values - mean_row) * inv_std
    normed = (centered * gain + bias).astype(jnp.bfloat16)
    grad_y = cot_rows.astype(jnp.float32)
    scaled = grad_y * gain
    grad_tokens = (
        inv_std
        * (
            scaled
            - jnp.mean(scaled, axis=feature_axes, keepdims=True)
            - centered * jnp.mean(scaled * centered, axis=feature_axes, keepdims=True)
        )
    ).astype(jnp.bfloat16)
    return (normed, grad_tokens, jnp.sum(grad_y * centered, axis=1), jnp.sum(grad_y, axis=1))


def shards(
    queries,
    key_state_matrix,
    value_state_matrix,
    cotangent,
    sublayer_norm_gain,
    sublayer_norm_bias,
    segment_blocks,
    dilation_rates,
):
    tokens_here = queries.shape[1]
    width_all = queries.shape[2]
    head_size = width_all // H
    ctx_count = lax.axis_size("ctx")
    heads_here = H // ctx_count
    width_here = width_all // ctx_count
    head_first = lax.axis_index("ctx") * heads_here
    head_indices = head_first + jnp.arange(heads_here, dtype=jnp.int32)
    loss_scale = 1.0 / math.sqrt(lax.axis_size("dp") * tokens_here * ctx_count)
    tokens_all = tokens_here * ctx_count

    def to_rows(array):
        return array.reshape(tokens_all, heads_here, head_size)

    stacked_in = jnp.stack(
        [
            head_major(queries[0], ctx_count),
            head_major(key_state_matrix[0], ctx_count),
            head_major(value_state_matrix[0], ctx_count),
        ]
    )
    stacked_in = lax.all_to_all(stacked_in, "ctx", split_axis=1, concat_axis=1, tiled=True)
    query_head_tensor, key_head_tensor, value_head_tensor = (
        to_rows(stacked_in[0]),
        to_rows(stacked_in[1]),
        to_rows(stacked_in[2]),
    )
    attended, log_norm = dense_attention_forward(
        query_head_tensor,
        key_head_tensor,
        value_head_tensor,
        head_indices,
        segment_blocks,
        dilation_rates,
    )
    attended_hm = lax.all_to_all(
        attended.reshape(ctx_count, tokens_here, width_here), "ctx", 0, 0, tiled=True
    )
    gain_hm = sublayer_norm_gain.reshape(ctx_count, 1, width_here)
    bias_hm = sublayer_norm_bias.reshape(ctx_count, 1, width_here)
    normed_hm, grad_hm, gain_part, bias_part = head_norm(
        attended_hm.astype(jnp.float32),
        head_major(cotangent[0], ctx_count),
        gain_hm,
        bias_hm,
    )
    normed = token_major(normed_hm)
    grad_attended = to_rows(lax.all_to_all(grad_hm, "ctx", 0, 0, tiled=True))
    both = jnp.stack([gain_part, bias_part], axis=1)
    both = jnp.sum(lax.all_to_all(both, "ctx", 0, 0, tiled=True), axis=0)
    dp_count = lax.axis_size("dp")
    both = jnp.broadcast_to(both[None], (dp_count,) + both.shape)
    both = jnp.sum(lax.all_to_all(both, "dp", 0, 0, tiled=True), axis=0)
    grad_gain, grad_bias = both[0], both[1]
    grad_q, grad_k, grad_v = full_backward(
        query_head_tensor,
        key_head_tensor,
        value_head_tensor,
        attended,
        grad_attended,
        log_norm,
        head_indices,
        segment_blocks,
        dilation_rates,
    )
    stacked_out = lax.all_to_all(
        jnp.stack([part.reshape(ctx_count, tokens_here, width_here) for part in (grad_q, grad_k, grad_v)]),
        "ctx",
        split_axis=1,
        concat_axis=1,
        tiled=True,
    )
    return (
        normed,
        token_major(stacked_out[0]),
        token_major(stacked_out[1]),
        token_major(stacked_out[2]),
        grad_gain * loss_scale,
        grad_bias * loss_scale,
    )


def solution(mesh):
    return jax.shard_map(
        shards,
        mesh=mesh,
        in_specs=(
            P("dp", "ctx", None),
            P("dp", "ctx", None),
            P("dp", "ctx", None),
            P("dp", "ctx", None),
            P(),
            P(),
            P(),
            P(),
        ),
        out_specs=(
            P("dp", "ctx", None),
            P("dp", "ctx", None),
            P("dp", "ctx", None),
            P("dp", "ctx", None),
            P("ctx"),
            P("ctx"),
        ),
        check_vma=False,
    )
```

```python
import math

import jax
import jax.numpy as jnp
from jax import lax
from jax.experimental import pallas as pl
from jax.experimental.pallas import tpu as pltpu
from jax.sharding import PartitionSpec as P

H = 16
BLK = 128
G = 4


epsilon = 1e-05


def pick_rows(array, parity):
    pairs = array.reshape((array.shape[0] // 2, 2) + array.shape[1:])
    cond = (parity == 0).reshape((-1,) + (1,) * (array.ndim - 2))
    return jnp.where(cond, pairs[:, 0], pairs[:, 1])


def spread_rows(packed, parity, base):
    pairs = base.reshape((base.shape[0] // 2, 2) + base.shape[1:])
    cond = (parity == 0).reshape((-1,) + (1,) * (base.ndim - 2))
    first_branch = jnp.where(cond, packed, pairs[:, 0])
    second = jnp.where(cond, pairs[:, 1], packed)
    return jnp.stack([first_branch, second], axis=1).reshape(base.shape)


def add_parts(full_part, packed_part, parity):
    spread = spread_rows(packed_part, parity, jnp.zeros_like(full_part))
    full_part = lax.optimization_barrier(full_part)
    spread = lax.optimization_barrier(spread)
    return (full_part.astype(jnp.float32) + spread.astype(jnp.float32)).astype(jnp.bfloat16)


def block_view(array):
    return array.reshape((array.shape[0] // BLK, BLK) + array.shape[1:])


def lse_view(log_norm):
    return jnp.transpose(block_view(log_norm), (0, 2, 1))


def local_scores(query_row_set, key_row_set):
    scaling = 1.0 / math.sqrt(query_row_set.shape[-1])
    return (
        jnp.einsum(
            "bqhd,bkhd->bhqk",
            block_view(query_row_set),
            block_view(key_row_set),
            preferred_element_type=jnp.float32,
        )
        * scaling
    )


def local_lse(query_row_set, key_row_set):
    scores = local_scores(query_row_set, key_row_set)
    row_max = jnp.max(scores, axis=3)
    total = row_max + jnp.log(jnp.sum(jnp.exp(scores - row_max[..., None]), axis=3))
    return jnp.transpose(total, (0, 2, 1)).reshape(query_row_set.shape[0], query_row_set.shape[1])


def local_output(query_row_set, key_row_set, value_row_set, log_norm):
    scores = local_scores(query_row_set, key_row_set)
    prob_bf = jnp.exp(scores - lse_view(log_norm)[..., None]).astype(jnp.bfloat16)
    output = jnp.einsum(
        "bhqk,bkhd->bqhd", prob_bf, block_view(value_row_set), preferred_element_type=jnp.float32
    )
    return output.astype(jnp.bfloat16).reshape(query_row_set.shape)


def local_backward(query_row_set, key_row_set, value_row_set, grad_rows, log_norm, delta_row):
    scaling = 1.0 / math.sqrt(query_row_set.shape[-1])
    scores = local_scores(query_row_set, key_row_set)
    prob_full = jnp.exp(scores - lse_view(log_norm)[..., None])
    prob_bf = prob_full.astype(jnp.bfloat16)
    grad_prob = jnp.einsum(
        "bqhd,bkhd->bhqk",
        block_view(grad_rows),
        block_view(value_row_set),
        preferred_element_type=jnp.float32,
    )
    grad_score = (prob_full * (grad_prob - lse_view(delta_row)[..., None])).astype(jnp.bfloat16)
    grad_q = jnp.einsum(
        "bhqk,bkhd->bqhd", grad_score, block_view(key_row_set), preferred_element_type=jnp.float32
    )
    grad_k = jnp.einsum(
        "bhqk,bqhd->bkhd", grad_score, block_view(query_row_set), preferred_element_type=jnp.float32
    )
    grad_v = jnp.einsum(
        "bhqk,bqhd->bkhd", prob_bf, block_view(grad_rows), preferred_element_type=jnp.float32
    )
    shape = query_row_set.shape
    return (
        (grad_q * scaling).astype(jnp.bfloat16).reshape(shape),
        (grad_k * scaling).astype(jnp.bfloat16).reshape(shape),
        grad_v.astype(jnp.bfloat16).reshape(shape),
    )


def packed_positions(start, count, head_indices):
    rows = start + jnp.arange(count, dtype=jnp.int32)
    return 2 * rows[None, :] + (head_indices % 2)[:, None]


def dilation_multiplier(
    query_positions, key_positions, head_indices, segment_blocks, dilation_rates
):
    counted = jnp.zeros(
        (head_indices.shape[0], query_positions.shape[1], key_positions.shape[1]), jnp.float32
    )
    for dilation_branch in range(1, G):
        seg_width = segment_blocks[dilation_branch] * BLK
        low_bits = dilation_rates[dilation_branch] - 1
        same_seg = (query_positions[:, :, None] ^ key_positions[:, None, :]) < seg_width
        selected_queries = ((query_positions ^ head_indices[:, None]) & low_bits) == 0
        selected_keys = ((key_positions ^ head_indices[:, None]) & low_bits) == 0
        counted = counted + (
            same_seg & selected_queries[:, :, None] & selected_keys[:, None, :]
        ).astype(jnp.float32)
    return counted


def dilated_mask(params_ref, rows, keys, row_first):
    head = params_ref[2 * G]
    parity = params_ref[2 * G + 1]
    query_positions = 2 * (row_first + lax.broadcasted_iota(jnp.int32, (rows, keys), 0)) + parity
    key_positions = 2 * lax.broadcasted_iota(jnp.int32, (rows, keys), 1) + parity
    apart = query_positions ^ key_positions
    query_phase = query_positions ^ head
    key_phase = key_positions ^ head
    counted = jnp.zeros((rows, keys), jnp.float32)
    for branch in range(1, G):
        low_bits = params_ref[G + branch]
        kept = (
            (apart < params_ref[branch])
            & ((query_phase & low_bits) == 0)
            & ((key_phase & low_bits) == 0)
        )
        counted = counted + jnp.where(kept, 1.0, 0.0)
    return counted


def dilated_forward_kernel(params_ref, q_ref, k_ref, v_ref, own_ref, out_ref, lse_ref):
    rows, head_size = q_ref.shape
    keys = k_ref.shape[0]
    scaling = 1.0 / math.sqrt(head_size)
    counted = dilated_mask(params_ref, rows, keys, pl.program_id(0) * rows)
    scores = (
        lax.dot_general(
            q_ref[...], k_ref[...], (((1,), (1,)), ((), ())), preferred_element_type=jnp.float32
        )
        * scaling
    )
    masked = jnp.where(counted > 0, scores, -1e30)
    row_max = jnp.max(masked, axis=1, keepdims=True)
    shifted = counted * jnp.exp(masked - row_max)
    part_lse = row_max + jnp.log(jnp.sum(shifted, axis=1, keepdims=True))
    own_lse = own_ref[...]
    top = jnp.maximum(part_lse, own_lse)
    log_norm = top + jnp.log(jnp.exp(part_lse - top) + jnp.exp(own_lse - top))
    prob_bf = (shifted * jnp.exp(row_max - log_norm)).astype(jnp.bfloat16)
    out_ref[...] = jnp.dot(prob_bf, v_ref[...], preferred_element_type=jnp.float32).astype(
        out_ref.dtype
    )
    lse_ref[...] = log_norm


def mask_params(head, segment_blocks, dilation_rates):
    return jnp.concatenate(
        [
            segment_blocks.astype(jnp.int32) * BLK,
            dilation_rates.astype(jnp.int32) - 1,
            jnp.stack([head, head % 2]).astype(jnp.int32),
        ]
    )


def dilated_forward_call(params, q, k, v, own, row_block=512):
    rows, head_size = q.shape
    keys = k.shape[0]
    grid = (rows // row_block,)
    return pl.pallas_call(
        dilated_forward_kernel,
        grid=grid,
        in_specs=[
            pl.BlockSpec(memory_space=pltpu.SMEM),
            pl.BlockSpec((row_block, head_size), lambda i: (i, 0)),
            pl.BlockSpec((keys, head_size), lambda i: (0, 0)),
            pl.BlockSpec((keys, head_size), lambda i: (0, 0)),
            pl.BlockSpec((row_block, 1), lambda i: (i, 0)),
        ],
        out_specs=[
            pl.BlockSpec((row_block, head_size), lambda i: (i, 0)),
            pl.BlockSpec((row_block, 1), lambda i: (i, 0)),
        ],
        out_shape=[
            jax.ShapeDtypeStruct((rows, head_size), jnp.bfloat16),
            jax.ShapeDtypeStruct((rows, 1), jnp.float32),
        ],
        cost_estimate=pl.CostEstimate(
            flops=4 * rows * keys * head_size,
            transcendentals=rows * keys,
            bytes_accessed=2 * (3 * rows * head_size + rows * head_size) + 8 * rows,
        ),
    )(params, q, k, v, own)


def sparse_attention_forward(
    query_row_set,
    key_row_set,
    value_row_set,
    baseline_logsumexp,
    head_indices,
    segment_blocks,
    dilation_rates,
):
    length_all, heads_here, head_size = query_row_set.shape
    rows_per_block = length_all
    blocks = length_all // rows_per_block
    scaling = 1.0 / math.sqrt(head_size)
    key_positions = packed_positions(0, length_all, head_indices)

    def one_block(block_id):
        starting_row = block_id * rows_per_block
        q_block = lax.dynamic_slice_in_dim(query_row_set, starting_row, rows_per_block, 0)
        own_lse = lax.dynamic_slice_in_dim(baseline_logsumexp, starting_row, rows_per_block, 0).T
        counted = dilation_multiplier(
            packed_positions(starting_row, rows_per_block, head_indices),
            key_positions,
            head_indices,
            segment_blocks,
            dilation_rates,
        )
        scores = (
            jnp.einsum("qhd,khd->hqk", q_block, key_row_set, preferred_element_type=jnp.float32)
            * scaling
        )
        masked = jnp.where(counted > 0, scores, -1e30)
        row_max = jnp.max(masked, axis=2)
        part_lse = row_max + jnp.log(
            jnp.sum(counted * jnp.exp(masked - row_max[:, :, None]), axis=2)
        )
        top = jnp.maximum(part_lse, own_lse)
        log_norm = top + jnp.log(jnp.exp(part_lse - top) + jnp.exp(own_lse - top))
        prob_bf = (counted * jnp.exp(masked - log_norm[:, :, None])).astype(jnp.bfloat16)
        output = jnp.einsum(
            "hqk,khd->qhd", prob_bf, value_row_set, preferred_element_type=jnp.float32
        ).astype(jnp.bfloat16)
        return (output, log_norm)

    outputs, lse_blocks = lax.map(one_block, jnp.arange(blocks, dtype=jnp.int32))
    return (
        outputs.reshape(length_all, heads_here, head_size),
        jnp.transpose(lse_blocks, (0, 2, 1)).reshape(length_all, heads_here),
    )


def dilated_backward(
    query_row_set,
    key_row_set,
    value_row_set,
    grad_rows,
    log_norm,
    delta_row,
    head_indices,
    segment_blocks,
    dilation_rates,
):
    length_all, heads_here, head_size = query_row_set.shape
    rows_per_block = length_all
    blocks = length_all // rows_per_block
    scaling = 1.0 / math.sqrt(head_size)
    key_positions = packed_positions(0, length_all, head_indices)

    def step(carry, block_id):
        acc_k, acc_v = carry
        starting_row = block_id * rows_per_block
        q_block = lax.dynamic_slice_in_dim(query_row_set, starting_row, rows_per_block, 0)
        g_block = lax.dynamic_slice_in_dim(grad_rows, starting_row, rows_per_block, 0)
        lse_block = lax.dynamic_slice_in_dim(log_norm, starting_row, rows_per_block, 0).T
        delta_block = lax.dynamic_slice_in_dim(delta_row, starting_row, rows_per_block, 0).T
        counted = dilation_multiplier(
            packed_positions(starting_row, rows_per_block, head_indices),
            key_positions,
            head_indices,
            segment_blocks,
            dilation_rates,
        )
        scores = (
            jnp.einsum("qhd,khd->hqk", q_block, key_row_set, preferred_element_type=jnp.float32)
            * scaling
        )
        masked = jnp.where(counted > 0, scores, -1e30)
        prob_full = counted * jnp.exp(masked - lse_block[:, :, None])
        prob_bf = prob_full.astype(jnp.bfloat16)
        grad_prob = jnp.einsum(
            "qhd,khd->hqk", g_block, value_row_set, preferred_element_type=jnp.float32
        )
        grad_score = (prob_full * (grad_prob - delta_block[:, :, None])).astype(jnp.bfloat16)
        grad_q = (
            jnp.einsum("hqk,khd->qhd", grad_score, key_row_set, preferred_element_type=jnp.float32)
            * scaling
        ).astype(jnp.bfloat16)
        acc_k = acc_k + jnp.einsum(
            "hqk,qhd->khd", grad_score, q_block, preferred_element_type=jnp.float32
        )
        acc_v = acc_v + jnp.einsum(
            "hqk,qhd->khd", prob_bf, g_block, preferred_element_type=jnp.float32
        )
        return ((acc_k, acc_v), grad_q)

    zeros_all = jnp.zeros((length_all, heads_here, head_size), jnp.float32)
    (acc_k, acc_v), grad_q = lax.scan(
        step, (zeros_all, zeros_all), jnp.arange(blocks, dtype=jnp.int32)
    )
    return (
        grad_q.reshape(length_all, heads_here, head_size),
        (acc_k * scaling).astype(jnp.bfloat16),
        acc_v.astype(jnp.bfloat16),
    )


def dense_attention_forward(
    query_row_set, key_row_set, value_row_set, head_indices, segment_blocks, dilation_rates
):
    parity = head_indices % 2
    own_lse = local_lse(query_row_set, key_row_set)
    if query_row_set.shape[1] == 1:
        params = mask_params(head_indices[0], segment_blocks, dilation_rates)
        packed_out, packed_lse = dilated_forward_call(
            params,
            pick_rows(query_row_set, parity)[:, 0],
            pick_rows(key_row_set, parity)[:, 0],
            pick_rows(value_row_set, parity)[:, 0],
            pick_rows(own_lse, parity),
        )
        packed_out = packed_out[:, None]
    else:
        packed_out, packed_lse = sparse_attention_forward(
            pick_rows(query_row_set, parity),
            pick_rows(key_row_set, parity),
            pick_rows(value_row_set, parity),
            pick_rows(own_lse, parity),
            head_indices,
            segment_blocks,
            dilation_rates,
        )
    log_norm = spread_rows(packed_lse, parity, own_lse)
    attended = add_parts(
        local_output(query_row_set, key_row_set, value_row_set, log_norm), packed_out, parity
    )
    return (attended, log_norm)


def full_backward(
    query_row_set,
    key_row_set,
    value_row_set,
    attended,
    grad_attended,
    log_norm,
    head_indices,
    segment_blocks,
    dilation_rates,
):
    parity = head_indices % 2
    delta_row = jnp.sum(grad_attended.astype(jnp.float32) * attended.astype(jnp.float32), axis=2)
    local_parts = local_backward(
        query_row_set, key_row_set, value_row_set, grad_attended, log_norm, delta_row
    )
    packed_parts = dilated_backward(
        pick_rows(query_row_set, parity),
        pick_rows(key_row_set, parity),
        pick_rows(value_row_set, parity),
        pick_rows(grad_attended, parity),
        pick_rows(log_norm, parity),
        pick_rows(delta_row, parity),
        head_indices,
        segment_blocks,
        dilation_rates,
    )
    return tuple(
        (
            add_parts(first_branch, second, parity)
            for first_branch, second in zip(local_parts, packed_parts)
        )
    )


def head_major(array, groups):
    tokens, width = array.shape
    return jnp.swapaxes(array.reshape(tokens, groups, width // groups), 0, 1)


def token_major(array):
    groups, tokens, width = array.shape
    return jnp.swapaxes(array, 0, 1).reshape(1, tokens, groups * width)


def head_norm(values, cot_rows, gain, bias):
    feature_axes = (0, 2)
    mean_row = jnp.mean(values, axis=feature_axes, keepdims=True)
    var_row = jnp.mean(values * values, axis=feature_axes, keepdims=True) - mean_row * mean_row
    inv_std = lax.rsqrt(var_row + epsilon)
    centered = (values - mean_row) * inv_std
    normed = (centered * gain + bias).astype(jnp.bfloat16)
    grad_y = cot_rows.astype(jnp.float32)
    scaled = grad_y * gain
    grad_tokens = (
        inv_std
        * (
            scaled
            - jnp.mean(scaled, axis=feature_axes, keepdims=True)
            - centered * jnp.mean(scaled * centered, axis=feature_axes, keepdims=True)
        )
    ).astype(jnp.bfloat16)
    return (normed, grad_tokens, jnp.sum(grad_y * centered, axis=1), jnp.sum(grad_y, axis=1))


def shards(
    queries,
    key_state_matrix,
    value_state_matrix,
    cotangent,
    sublayer_norm_gain,
    sublayer_norm_bias,
    segment_blocks,
    dilation_rates,
):
    tokens_here = queries.shape[1]
    width_all = queries.shape[2]
    head_size = width_all // H
    ctx_count = lax.axis_size("ctx")
    heads_here = H // ctx_count
    width_here = width_all // ctx_count
    head_first = lax.axis_index("ctx") * heads_here
    head_indices = head_first + jnp.arange(heads_here, dtype=jnp.int32)
    loss_scale = 1.0 / math.sqrt(lax.axis_size("dp") * tokens_here * ctx_count)
    tokens_all = tokens_here * ctx_count

    def to_rows(array):
        return array.reshape(tokens_all, heads_here, head_size)

    stacked_in = jnp.stack(
        [
            head_major(queries[0], ctx_count),
            head_major(key_state_matrix[0], ctx_count),
            head_major(value_state_matrix[0], ctx_count),
        ]
    )
    stacked_in = lax.all_to_all(stacked_in, "ctx", split_axis=1, concat_axis=1, tiled=True)
    query_head_tensor, key_head_tensor, value_head_tensor = (
        to_rows(stacked_in[0]),
        to_rows(stacked_in[1]),
        to_rows(stacked_in[2]),
    )
    attended, log_norm = dense_attention_forward(
        query_head_tensor,
        key_head_tensor,
        value_head_tensor,
        head_indices,
        segment_blocks,
        dilation_rates,
    )
    attended_hm = lax.all_to_all(
        attended.reshape(ctx_count, tokens_here, width_here), "ctx", 0, 0, tiled=True
    )
    gain_hm = sublayer_norm_gain.reshape(ctx_count, 1, width_here)
    bias_hm = sublayer_norm_bias.reshape(ctx_count, 1, width_here)
    normed_hm, grad_hm, gain_part, bias_part = head_norm(
        attended_hm.astype(jnp.float32),
        head_major(cotangent[0], ctx_count),
        gain_hm,
        bias_hm,
    )
    normed = token_major(normed_hm)
    grad_attended = to_rows(lax.all_to_all(grad_hm, "ctx", 0, 0, tiled=True))
    both = jnp.stack([gain_part, bias_part], axis=1)
    both = jnp.sum(lax.all_to_all(both, "ctx", 0, 0, tiled=True), axis=0)
    dp_count = lax.axis_size("dp")
    both = jnp.broadcast_to(both[None], (dp_count,) + both.shape)
    both = jnp.sum(lax.all_to_all(both, "dp", 0, 0, tiled=True), axis=0)
    grad_gain, grad_bias = both[0], both[1]
    grad_q, grad_k, grad_v = full_backward(
        query_head_tensor,
        key_head_tensor,
        value_head_tensor,
        attended,
        grad_attended,
        log_norm,
        head_indices,
        segment_blocks,
        dilation_rates,
    )
    stacked_out = lax.all_to_all(
        jnp.stack([part.reshape(ctx_count, tokens_here, width_here) for part in (grad_q, grad_k, grad_v)]),
        "ctx",
        split_axis=1,
        concat_axis=1,
        tiled=True,
    )
    return (
        normed,
        token_major(stacked_out[0]),
        token_major(stacked_out[1]),
        token_major(stacked_out[2]),
        grad_gain * loss_scale,
        grad_bias * loss_scale,
    )


def solution(mesh):
    return jax.shard_map(
        shards,
        mesh=mesh,
        in_specs=(
            P("dp", "ctx", None),
            P("dp", "ctx", None),
            P("dp", "ctx", None),
            P("dp", "ctx", None),
            P(),
            P(),
            P(),
            P(),
        ),
        out_specs=(
            P("dp", "ctx", None),
            P("dp", "ctx", None),
            P("dp", "ctx", None),
            P("dp", "ctx", None),
            P("ctx"),
            P("ctx"),
        ),
        check_vma=False,
    )
```
